32 devices in a mesh: groups: 2 (over y), cols: 4 (over z), slab: 2 (over x), rep: 2 (over core).
Axes of the slice: x: 2, y: 2, z: 4, core: 2. Of those that a mesh axis runs over, the one named last changes fastest.
Arguments:
- fields: bfloat16 [16, 8, 2048, 512], P('cols', 'groups', 'rep', 'slab'), parts along dimension 1, may hold values from -250 to 250
- stresses: bfloat16 [6, 8, 512, 128], P(None, 'groups', 'rep', 'slab'), parts along dimension 1, may hold values from -750 to 750
- planes: int32 [8], P('groups'), parts along dimension 0, may hold values from 0 to 2047, as said below
- active_masks: int32 [3, 6, 256], replicated, may hold values 0 or 1
Outputs:
- coefficients: float32 [3, 12, 256], P(None, 'groups', 'cols'), parts along dimension 1
- misfit: bfloat16 [6, 8, 512, 128], P(None, 'groups', 'rep', 'slab'), parts along dimension 1
The draws below stay inside these ranges and needn't reach their ends.
There are 2 independent parts, one for each index of `groups`. The reference program is written for one: setup_inputs(seed, part) draws one part's arguments, and reference() takes and returns one part's arrays. A program takes and returns all parts, laid end to end along the dimension named above; an argument that names none is the same for every part. Nothing has to cross between parts.
Inputs may be any that keep to these rules, and one draw needn't show every extreme that they name: `planes`: sorted and distinct; either the first is 0 or the last is 2047.
All inputs are finite; a program needn't handle non-finite values.
Results may differ from the reference program's by a relative error of at most 0.0069.
Values may be sent and summed in bfloat16 or wider, within the bound.
No kernel may reach another device: no remote copies, remote signals or barrier semaphores. Data moves between devices by JAX's collectives and lax.ppermute only.
A program may use at most 128 MiB of HBM per device.

```python
import math
import jax
import jax.numpy as jnp
import numpy as np
from jax import lax

CH = 16
STRESS = 6
TERMS = 256
PLANES = 4
NY = 2048
PASSES = 3
ITERS = 3
NX = 2048
NZ = 512
NMX = 512
NMZ = 128
SAMPLES = 262144


def shared_blocks(key):
    base_key = jax.random.fold_in(key, 101)
    own_noise = jnp.clip(jax.random.normal(jax.random.fold_in(base_key, 1), (CH, PLANES, NMX, NMZ), jnp.float32), -4.0, 4.0)
    common = jnp.clip(jax.random.normal(jax.random.fold_in(base_key, 2), (PLANES, NMX, NMZ), jnp.float32), -4.0, 4.0)
    blocks = 0.8 * own_noise + 0.6 * common[None]
    channel_scale = jnp.exp(jax.random.uniform(jax.random.fold_in(base_key, 3), (CH,), jnp.float32, 0.0, math.log(10.0)))
    return (blocks, channel_scale)


def draw_fields(key, part):
    blocks, channel_scale = shared_blocks(key)
    upsampled = jnp.repeat(jnp.repeat(blocks, 4, axis=2), 4, axis=3)
    fine_grain = jnp.clip(jax.random.normal(jax.random.fold_in(key, 7), (CH, PLANES, NX, NZ), jnp.float32), -4.0, 4.0)
    values = (upsampled + 0.5 * fine_grain) * channel_scale[:, None, None, None]
    return values.astype(jnp.bfloat16)


def draw_stresses(key, part):
    blocks, channel_scale = shared_blocks(key)
    channel_ids = np.arange(STRESS)
    values = blocks[channel_ids] * blocks[channel_ids + 6]
    values = values + 0.7 * blocks[channel_ids + 3] * blocks[channel_ids + 9]
    values = values - 0.5 * blocks[channel_ids + 1] * blocks[channel_ids + 10]
    stress_noise = jnp.clip(jax.random.normal(jax.random.fold_in(key, 9), (STRESS, PLANES, NMX, NMZ), jnp.float32), -4.0, 4.0)
    values = values + 0.4 * stress_noise
    return values.astype(jnp.bfloat16)


def draw_planes(key, part):
    plane_key = jax.random.fold_in(key, 211)
    inner = jax.random.permutation(jax.random.fold_in(plane_key, 1), NY - 2)[:PLANES - 1] + 1
    inner = jnp.sort(inner.astype(jnp.int32))
    side_flag = jax.random.randint(jax.random.fold_in(plane_key, 2), (), 0, 2)
    lower_window = jnp.concatenate([jnp.zeros((1,), jnp.int32), inner])
    upper_window = jnp.concatenate([inner, jnp.full((1,), NY - 1, jnp.int32)])
    return jnp.where(side_flag == 0, lower_window, upper_window).astype(jnp.int32)


def touch_ends(entries, own_key, smallest, high):
    spot = [jax.random.randint(jax.random.fold_in(own_key, axis), (), 0, length) for axis, length in enumerate(entries.shape)]
    main_axis = entries.shape.index(max(entries.shape))
    beside = spot[:main_axis] + [(spot[main_axis] + 1) % entries.shape[main_axis]] + spot[main_axis + 1:]
    return entries.at[tuple(spot)].set(smallest).at[tuple(beside)].set(high)


def setup_inputs(seed: int = 0, part: int = 0) -> dict:
    key_list = jax.random.split(jax.random.key(seed), 5)
    own_keys = jax.random.split(jax.random.fold_in(key_list[4], part), 5)
    fields = draw_fields(jax.random.fold_in(jax.random.fold_in(key_list[4], part), 71), part)
    stresses = draw_stresses(jax.random.fold_in(jax.random.fold_in(key_list[4], part), 71), part)
    planes = draw_planes(jax.random.fold_in(jax.random.fold_in(key_list[4], part), 71), part)
    active_masks = touch_ends((jax.random.randint(key_list[3], (PASSES, STRESS, TERMS), 0, 3) < 2).astype(jnp.int32), jax.random.fold_in(key_list[3], 1), 0, 1)
    return {"fields": fields, "stresses": stresses, "planes": planes, "active_masks": active_masks}


ridge_weight = 0.05
epsilon = 1e-06

def kernel(spread):
    offsets = np.arange(13) - 6.0
    values = np.exp(-offsets * offsets / (2.0 * spread * spread))
    return values / values.sum()

def smooth(values, weights, axis_dim, out_count):
    summed = None
    for tap_index in range(13):
        sliced = lax.slice_in_dim(values, 1 + tap_index, 2 + tap_index + 4 * (out_count - 1), 4, axis_dim)
        weighted_tap = sliced * float(weights[tap_index])
        summed = weighted_tap if summed is None else summed + weighted_tap
    return summed

def apply_normal(vector, active, normal_gram):
    product = jnp.einsum('kl,il->ki', active * vector, normal_gram, precision=lax.Precision.HIGHEST)
    return active * product + ridge_weight * vector

def reference(fields, stresses, planes, active_masks):
    height = 2.0 * (planes.astype(jnp.float32) + 0.5) / NY - 1.0
    root_weight = jnp.sqrt(1.2 - height * height)
    narrow_taps = kernel(1.5)
    broad_taps = kernel(3.0)

    def one_channel(channel):
        padded = jnp.pad(channel.astype(jnp.float32), ((0, 0), (5, 5), (5, 5)), mode='wrap')
        narrow = smooth(smooth(padded, narrow_taps, 1, NMX), narrow_taps, 2, NMZ)
        broader = smooth(smooth(padded, broad_taps, 1, NMX), broad_taps, 2, NMZ)
        return (narrow.astype(jnp.bfloat16), (broader * root_weight[:, None, None]).astype(jnp.bfloat16))
    narrow_set, broad_set = lax.map(one_channel, fields)
    narrow_set = narrow_set.reshape(CH, SAMPLES).astype(jnp.float32)
    broad_set = broad_set.reshape(CH, SAMPLES).astype(jnp.float32)
    library_terms = (narrow_set[:, None, :] * broad_set[None, :, :]).astype(jnp.bfloat16)
    library_terms = lax.optimization_barrier(library_terms).astype(jnp.float32).reshape(TERMS, SAMPLES)
    weighted = (stresses.astype(jnp.float32) * root_weight[None, :, None, None]).astype(jnp.bfloat16)
    weighted = lax.optimization_barrier(weighted).astype(jnp.float32).reshape(STRESS, SAMPLES)
    gram_matrix = jnp.dot(library_terms, library_terms.T, precision=lax.Precision.HIGHEST)
    rhs_sums = jnp.dot(library_terms, weighted.T, precision=lax.Precision.HIGHEST)
    column_scale = 1.0 / jnp.sqrt(jnp.diagonal(gram_matrix) / SAMPLES + epsilon)
    normal_gram = column_scale[:, None] * gram_matrix * column_scale[None, :] / SAMPLES
    target_norm = column_scale[None, :] * rhs_sums.T / SAMPLES
    solution = jnp.zeros((STRESS, TERMS), jnp.float32)
    results = []
    for pass_index in range(PASSES):
        active = active_masks[pass_index].astype(jnp.float32)
        solution = active * solution
        remain = active * target_norm - apply_normal(solution, active, normal_gram)
        direction = remain
        norm_now = lax.optimization_barrier(jnp.sum(remain * remain, axis=1))
        for turn_index in range(ITERS):
            applied = apply_normal(direction, active, normal_gram)
            step_size = norm_now / (lax.optimization_barrier(jnp.sum(direction * applied, axis=1)) + epsilon)
            solution = solution + step_size[:, None] * direction
            remain = remain - step_size[:, None] * applied
            norm_next = lax.optimization_barrier(jnp.sum(remain * remain, axis=1))
            direction = remain + (norm_next / (norm_now + epsilon))[:, None] * direction
            norm_now = norm_next
        results.append(solution)
    coefficients = jnp.stack(results)
    final_weights = (column_scale[None, :] * solution).astype(jnp.bfloat16)
    final_weights = lax.optimization_barrier(final_weights).astype(jnp.float32)
    predicted = jnp.dot(final_weights, library_terms, precision=lax.Precision.HIGHEST)
    misfit = (weighted - predicted).astype(jnp.bfloat16).reshape(STRESS, PLANES, NMX, NMZ)
    return (coefficients, misfit)
```

```python
import math

import jax
import jax.numpy as jnp
import numpy as np
from jax import lax
from jax.sharding import PartitionSpec as P

STRESS = 6
TERMS = 256
NY = 2048
PASSES = 3
ITERS = 3


ridge_weight = 0.05
epsilon = 1e-06


def extended(array, sides, width):
    for axis, dim in sides:
        count, length = (lax.axis_size(axis), array.shape[dim])
        up = [(i, (i + 1) % count) for i in range(count)]
        down = [(j, i) for i, j in up]
        last = lax.slice_in_dim(array, length - width, length, axis=dim)
        leading = lax.slice_in_dim(array, 0, width, axis=dim)
        before = lax.ppermute(last, axis, up)
        after = lax.ppermute(leading, axis, down)
        array = jnp.concatenate([before, array, after], axis=dim)
    return array


def kernel(spread):
    offsets = np.arange(13) - 6.0
    values = np.exp(-offsets * offsets / (2.0 * spread * spread))
    return values / values.sum()


def filter_table(cells, first_taps, second_taps):
    out_count = cells // 4
    table = np.zeros((cells + 10, 2, out_count), np.float32)
    for which, taps in ((0, first_taps), (1, second_taps)):
        for out_index in range(out_count):
            for tap_index in range(13):
                table[1 + tap_index + 4 * out_index, which, out_index] = taps[tap_index]
    return table


def library(narrow_part, broad_part):
    product = (
        narrow_part.astype(jnp.float32)[:, None, :] * broad_part.astype(jnp.float32)[None, :, :]
    )
    return product.astype(jnp.bfloat16).reshape(
        narrow_part.shape[0] * broad_part.shape[0], narrow_part.shape[1]
    )


def local(fields, stresses, planes, active_masks):
    chan_dev, plane_count, cells_x, cells_z = fields.shape
    coarse_x = cells_x // 4
    coarse_z = cells_z // 4
    row_count = plane_count * coarse_x * coarse_z
    col_devices = lax.axis_size("cols")
    column_index = lax.axis_index("cols")
    term_dev = TERMS // col_devices
    offset = column_index * term_dev
    samples = float(row_count * lax.axis_size("slab") * lax.axis_size("rep"))
    height = 2.0 * (planes.astype(jnp.float32) + 0.5) / NY - 1.0
    root_weight = jnp.sqrt(1.2 - height * height)
    padded = extended(fields, (("slab", 3), ("rep", 2)), 5)
    widened = padded.astype(jnp.float32)
    narrow_taps = kernel(1.5)
    broad_taps = kernel(3.0)
    span_table = jnp.asarray(filter_table(cells_z, narrow_taps, broad_taps))
    stream_table = jnp.asarray(
        np.transpose(filter_table(cells_x, narrow_taps, broad_taps), (1, 0, 2))
    )
    along_span = jnp.einsum("cpxz,zsn->cpxsn", widened, span_table, precision=lax.Precision.HIGHEST)
    filtered = jnp.einsum(
        "cpxsn,sxm->scpmn", along_span, stream_table, precision=lax.Precision.HIGHEST
    )
    narrow = filtered[0]
    broader = filtered[1]
    narrow_set = narrow.astype(jnp.bfloat16).reshape(chan_dev, row_count)
    broad_set = (
        (broader * root_weight[None, :, None, None])
        .astype(jnp.bfloat16)
        .reshape(chan_dev, row_count)
    )
    weighted = (stresses.astype(jnp.float32) * root_weight[None, :, None, None]).astype(
        jnp.bfloat16
    )
    weighted = weighted.reshape(STRESS, row_count)
    block_rows = math.gcd(row_count, 4096)
    block_count = row_count // block_rows
    both_sets = lax.all_gather(jnp.stack([narrow_set, broad_set]), "cols", axis=1, tiled=True)
    narrow_all, broad_all = both_sets[0], both_sets[1]

    def gram_step(block_index, carry):
        gram_acc, rhs_acc = carry
        start = block_index * block_rows
        narrow_piece = lax.dynamic_slice_in_dim(narrow_all, start, block_rows, 1)
        broad_piece = lax.dynamic_slice_in_dim(broad_all, start, block_rows, 1)
        own_piece = lax.dynamic_slice_in_dim(narrow_set, start, block_rows, 1)
        all_terms = library(narrow_piece, broad_piece)
        own_terms = library(own_piece, broad_piece)
        weighted_piece = lax.dynamic_slice_in_dim(weighted, start, block_rows, 1)
        gram_acc = gram_acc + jnp.einsum(
            "ir,jr->ij", own_terms, all_terms, preferred_element_type=jnp.float32
        )
        rhs_acc = rhs_acc + jnp.einsum(
            "ir,kr->ik", own_terms, weighted_piece, preferred_element_type=jnp.float32
        )
        return (gram_acc, rhs_acc)

    gram_block, rhs_block = lax.fori_loop(
        0,
        block_count,
        gram_step,
        (jnp.zeros((term_dev, TERMS), jnp.float32), jnp.zeros((term_dev, STRESS), jnp.float32)),
    )
    own_rows = jnp.concatenate([gram_block, rhs_block], axis=1)
    placed_rows = lax.dynamic_update_slice_in_dim(
        jnp.zeros((TERMS, TERMS + STRESS), jnp.float32), own_rows, offset, 0
    )
    full_rows = lax.psum(placed_rows, ("cols", "slab", "rep"))
    gram_matrix = full_rows[:, :TERMS]
    rhs_sums = full_rows[:, TERMS:]
    column_scale = 1.0 / jnp.sqrt(jnp.diagonal(gram_matrix) / samples + epsilon)
    normal_gram = column_scale[:, None] * gram_matrix * column_scale[None, :] / samples
    target_norm = column_scale[None, :] * rhs_sums.T / samples
    results = []

    def apply_normal(vector, active):
        product = jnp.einsum(
            "kl,il->ki", active * vector, normal_gram, precision=lax.Precision.HIGHEST
        )
        return active * product + ridge_weight * vector

    solution_all = jnp.zeros((STRESS, TERMS), jnp.float32)
    for pass_index in range(PASSES):
        active = active_masks[pass_index].astype(jnp.float32)
        solution_all = active * solution_all
        remain = active * target_norm - apply_normal(solution_all, active)
        direction = remain
        norm_now = jnp.sum(remain * remain, axis=1)
        for turn_index in range(ITERS):
            applied = apply_normal(direction, active)
            curve_sum = jnp.sum(direction * applied, axis=1)
            step_size = norm_now / (curve_sum + epsilon)
            solution_all = solution_all + step_size[:, None] * direction
            remain = remain - step_size[:, None] * applied
            norm_next = jnp.sum(remain * remain, axis=1)
            direction = remain + (norm_next / (norm_now + epsilon))[:, None] * direction
            norm_now = norm_next
        results.append(lax.dynamic_slice_in_dim(solution_all, offset, term_dev, 1))
    coefficients = jnp.stack(results)
    final_weights = (column_scale[None, :] * solution_all).astype(jnp.bfloat16)

    def misfit_step(block_index, misfit_acc):
        start = block_index * block_rows
        narrow_piece = lax.dynamic_slice_in_dim(narrow_all, start, block_rows, 1)
        broad_piece = lax.dynamic_slice_in_dim(broad_all, start, block_rows, 1)
        all_terms = library(narrow_piece, broad_piece)
        predicted = jnp.dot(final_weights, all_terms, preferred_element_type=jnp.float32)
        weighted_piece = lax.dynamic_slice_in_dim(weighted, start, block_rows, 1)
        piece_misfit = (weighted_piece.astype(jnp.float32) - predicted).astype(jnp.bfloat16)
        return lax.dynamic_update_slice_in_dim(misfit_acc, piece_misfit, start, 1)

    misfit = lax.fori_loop(
        0, block_count, misfit_step, jnp.zeros((STRESS, row_count), jnp.bfloat16)
    )
    misfit = misfit.reshape(STRESS, plane_count, coarse_x, coarse_z)
    return (coefficients, misfit)


def solution(mesh):
    placed = (
        P("cols", "groups", "rep", "slab"),
        P(None, "groups", "rep", "slab"),
        P("groups"),
        P(),
    )
    return jax.shard_map(
        local,
        mesh=mesh,
        in_specs=placed,
        out_specs=(P(None, "groups", "cols"), P(None, "groups", "rep", "slab")),
        check_vma=False,
    )
```

```python
import math

import jax
import jax.numpy as jnp
import numpy as np
from jax import lax
from jax.sharding import PartitionSpec as P

STRESS = 6
TERMS = 256
NY = 2048
PASSES = 3
ITERS = 3


ridge_weight = 0.05
epsilon = 1e-06


def extended(array, sides, width):
    for axis, dim in sides:
        count, length = (lax.axis_size(axis), array.shape[dim])
        up = [(i, (i + 1) % count) for i in range(count)]
        down = [(j, i) for i, j in up]
        last = lax.slice_in_dim(array, length - width, length, axis=dim)
        leading = lax.slice_in_dim(array, 0, width, axis=dim)
        before = lax.ppermute(last, axis, up)
        after = lax.ppermute(leading, axis, down)
        array = jnp.concatenate([before, array, after], axis=dim)
    return array


def tree_sum(value, axes):
    for axis in axes:
        count = lax.axis_size(axis)
        if count & (count - 1):
            value = lax.psum(value, axis)
            continue
        step = 1
        while step < count:
            partner = [(i, i ^ step) for i in range(count)]
            value = value + lax.ppermute(value, axis, partner)
            step *= 2
    return value


def kernel(spread):
    offsets = np.arange(13) - 6.0
    values = np.exp(-offsets * offsets / (2.0 * spread * spread))
    return values / values.sum()


def filter_table(cells, first_taps, second_taps, guard, order):
    out_count = cells // 4
    shape = tuple((cells + 10, 2, out_count)[d] for d in order)
    where = {d: order.index(d) for d in range(3)}
    position = lax.broadcasted_iota(jnp.int32, shape, where[0])
    which = lax.broadcasted_iota(jnp.int32, shape, where[1])
    out_index = lax.broadcasted_iota(jnp.int32, shape, where[2])
    tap_at = position - 1 - 4 * out_index + guard
    table = jnp.zeros(shape, jnp.float32)
    for tap_index in range(13):
        value = jnp.where(
            which == 0, np.float32(first_taps[tap_index]), np.float32(second_taps[tap_index])
        )
        table = jnp.where(tap_at == tap_index, value, table)
    return table


def library(narrow_part, broad_part):
    product = (
        narrow_part.astype(jnp.float32)[:, None, :] * broad_part.astype(jnp.float32)[None, :, :]
    )
    return product.astype(jnp.bfloat16).reshape(
        narrow_part.shape[0] * broad_part.shape[0], narrow_part.shape[1]
    )


def local(fields, stresses, planes, active_masks):
    chan_dev, plane_count, cells_x, cells_z = fields.shape
    coarse_x = cells_x // 4
    coarse_z = cells_z // 4
    row_count = plane_count * coarse_x * coarse_z
    col_devices = lax.axis_size("cols")
    column_index = lax.axis_index("cols")
    term_dev = TERMS // col_devices
    offset = column_index * term_dev
    samples = float(row_count * lax.axis_size("slab") * lax.axis_size("rep"))
    height = 2.0 * (planes.astype(jnp.float32) + 0.5) / NY - 1.0
    root_weight = jnp.sqrt(1.2 - height * height)
    padded = extended(fields, (("slab", 3), ("rep", 2)), 5)
    widened = padded.astype(jnp.float32)
    narrow_taps = kernel(1.5)
    broad_taps = kernel(3.0)
    guard = jnp.minimum(lax.axis_index("rep"), 0)
    span_table = filter_table(cells_z, narrow_taps, broad_taps, guard, (0, 1, 2))
    stream_table = filter_table(cells_x, narrow_taps, broad_taps, guard, (1, 0, 2))
    along_span = jnp.einsum("cpxz,zsn->cpxsn", widened, span_table, precision=lax.Precision.HIGHEST)
    filtered = jnp.einsum(
        "cpxsn,sxm->scpmn", along_span, stream_table, precision=lax.Precision.HIGHEST
    )
    narrow = filtered[0]
    broader = filtered[1]
    narrow_set = narrow.astype(jnp.bfloat16).reshape(chan_dev, row_count)
    broad_set = (
        (broader * root_weight[None, :, None, None])
        .astype(jnp.bfloat16)
        .reshape(chan_dev, row_count)
    )
    weighted = (stresses.astype(jnp.float32) * root_weight[None, :, None, None]).astype(
        jnp.bfloat16
    )
    weighted = weighted.reshape(STRESS, row_count)
    block_rows = math.gcd(row_count, 4096)
    block_count = row_count // block_rows
    both_sets = lax.all_gather(jnp.stack([narrow_set, broad_set]), "cols", axis=1, tiled=True)
    narrow_all, broad_all = both_sets[0], both_sets[1]

    def gram_step(block_index, carry):
        gram_acc, rhs_acc = carry
        start = block_index * block_rows
        narrow_piece = lax.dynamic_slice_in_dim(narrow_all, start, block_rows, 1)
        broad_piece = lax.dynamic_slice_in_dim(broad_all, start, block_rows, 1)
        own_piece = lax.dynamic_slice_in_dim(narrow_set, start, block_rows, 1)
        all_terms = library(narrow_piece, broad_piece)
        own_terms = library(own_piece, broad_piece)
        weighted_piece = lax.dynamic_slice_in_dim(weighted, start, block_rows, 1)
        gram_acc = gram_acc + jnp.einsum(
            "ir,jr->ij", own_terms, all_terms, preferred_element_type=jnp.float32
        )
        rhs_acc = rhs_acc + jnp.einsum(
            "ir,kr->ik", own_terms, weighted_piece, preferred_element_type=jnp.float32
        )
        return (gram_acc, rhs_acc)

    gram_block, rhs_block = lax.fori_loop(
        0,
        block_count,
        gram_step,
        (jnp.zeros((term_dev, TERMS), jnp.float32), jnp.zeros((term_dev, STRESS), jnp.float32)),
    )
    own_rows = tree_sum(jnp.concatenate([gram_block, rhs_block], axis=1), ("rep", "slab"))
    placed_rows = lax.dynamic_update_slice_in_dim(
        jnp.zeros((TERMS, TERMS + STRESS), jnp.float32), own_rows, offset, 0
    )
    full_rows = tree_sum(placed_rows, ("cols",))
    gram_matrix = full_rows[:, :TERMS]
    rhs_sums = full_rows[:, TERMS:]
    column_scale = 1.0 / jnp.sqrt(jnp.diagonal(gram_matrix) / samples + epsilon)
    normal_gram = column_scale[:, None] * gram_matrix * column_scale[None, :] / samples
    target_norm = column_scale[None, :] * rhs_sums.T / samples

    def apply_normal(vector, active):
        product = jnp.einsum(
            "kl,il->ki", active * vector, normal_gram, precision=lax.Precision.HIGHEST
        )
        return active * product + ridge_weight * vector

    def cg_turn(turn_index, state):
        solution_all, remain, direction, norm_now, active = state
        applied = apply_normal(direction, active)
        curve_sum = jnp.sum(direction * applied, axis=1)
        step_size = norm_now / (curve_sum + epsilon)
        solution_all = solution_all + step_size[:, None] * direction
        remain = remain - step_size[:, None] * applied
        norm_next = jnp.sum(remain * remain, axis=1)
        direction = remain + (norm_next / (norm_now + epsilon))[:, None] * direction
        return (solution_all, remain, direction, norm_next, active)

    def cg_pass(pass_index, state):
        solution_all, coefficients = state
        active = lax.dynamic_index_in_dim(active_masks, pass_index, 0, keepdims=False)
        active = active.astype(jnp.float32)
        solution_all = active * solution_all
        remain = active * target_norm - apply_normal(solution_all, active)
        norm_now = jnp.sum(remain * remain, axis=1)
        solution_all = lax.fori_loop(
            0, ITERS, cg_turn, (solution_all, remain, remain, norm_now, active)
        )[0]
        own_part = lax.dynamic_slice_in_dim(solution_all, offset, term_dev, 1)
        coefficients = lax.dynamic_update_index_in_dim(coefficients, own_part, pass_index, 0)
        return (solution_all, coefficients)

    solution_all, coefficients = lax.fori_loop(
        0,
        PASSES,
        cg_pass,
        (
            jnp.zeros((STRESS, TERMS), jnp.float32),
            jnp.zeros((PASSES, STRESS, term_dev), jnp.float32),
        ),
    )
    final_weights = (column_scale[None, :] * solution_all).astype(jnp.bfloat16)

    def misfit_step(block_index, misfit_acc):
        start = block_index * block_rows
        narrow_piece = lax.dynamic_slice_in_dim(narrow_all, start, block_rows, 1)
        broad_piece = lax.dynamic_slice_in_dim(broad_all, start, block_rows, 1)
        all_terms = library(narrow_piece, broad_piece)
        predicted = jnp.dot(final_weights, all_terms, preferred_element_type=jnp.float32)
        weighted_piece = lax.dynamic_slice_in_dim(weighted, start, block_rows, 1)
        piece_misfit = (weighted_piece.astype(jnp.float32) - predicted).astype(jnp.bfloat16)
        return lax.dynamic_update_slice_in_dim(misfit_acc, piece_misfit, start, 1)

    misfit = lax.fori_loop(
        0, block_count, misfit_step, jnp.zeros((STRESS, row_count), jnp.bfloat16)
    )
    misfit = misfit.reshape(STRESS, plane_count, coarse_x, coarse_z)
    return (coefficients, misfit)


def solution(mesh):
    placed = (
        P("cols", "groups", "rep", "slab"),
        P(None, "groups", "rep", "slab"),
        P("groups"),
        P(),
    )
    return jax.shard_map(
        local,
        mesh=mesh,
        in_specs=placed,
        out_specs=(P(None, "groups", "cols"), P(None, "groups", "rep", "slab")),
        check_vma=False,
    )
```

```python
import math

import jax
import jax.numpy as jnp
import numpy as np
from jax import lax
from jax.sharding import PartitionSpec as P

STRESS = 6
TERMS = 256
NY = 2048
PASSES = 3
ITERS = 3


ridge_weight = 0.05
epsilon = 1e-06


def extended(array, sides, width):
    for axis, dim in sides:
        count, length = (lax.axis_size(axis), array.shape[dim])
        up = [(i, (i + 1) % count) for i in range(count)]
        down = [(j, i) for i, j in up]
        last = lax.slice_in_dim(array, length - width, length, axis=dim)
        leading = lax.slice_in_dim(array, 0, width, axis=dim)
        before = lax.ppermute(last, axis, up)
        after = lax.ppermute(leading, axis, down)
        array = jnp.concatenate([before, array, after], axis=dim)
    return array


def tree_sum(value, axes):
    for axis in axes:
        count = lax.axis_size(axis)
        if count & (count - 1):
            value = lax.psum(value, axis)
            continue
        step = 1
        while step < count:
            partner = [(i, i ^ step) for i in range(count)]
            value = value + lax.ppermute(value, axis, partner)
            step *= 2
    return value


def kernel(spread):
    offsets = np.arange(13) - 6.0
    values = np.exp(-offsets * offsets / (2.0 * spread * spread))
    return values / values.sum()


def filter_table(cells, first_taps, second_taps, guard, order):
    out_count = cells // 4
    shape = tuple((cells + 10, 2, out_count)[d] for d in order)
    where = {d: order.index(d) for d in range(3)}
    position = lax.broadcasted_iota(jnp.int32, shape, where[0])
    which = lax.broadcasted_iota(jnp.int32, shape, where[1])
    out_index = lax.broadcasted_iota(jnp.int32, shape, where[2])
    tap_at = position - 1 - 4 * out_index + guard
    table = jnp.zeros(shape, jnp.float32)
    for tap_index in range(13):
        value = jnp.where(
            which == 0, np.float32(first_taps[tap_index]), np.float32(second_taps[tap_index])
        )
        table = jnp.where(tap_at == tap_index, value, table)
    return table


def library(narrow_part, broad_part):
    product = (
        narrow_part.astype(jnp.float32)[:, None, :] * broad_part.astype(jnp.float32)[None, :, :]
    )
    return product.astype(jnp.bfloat16).reshape(
        narrow_part.shape[0] * broad_part.shape[0], narrow_part.shape[1]
    )


def local(fields, stresses, planes, active_masks):
    chan_dev, plane_count, cells_x, cells_z = fields.shape
    coarse_x = cells_x // 4
    coarse_z = cells_z // 4
    row_count = plane_count * coarse_x * coarse_z
    col_devices = lax.axis_size("cols")
    column_index = lax.axis_index("cols")
    term_dev = TERMS // col_devices
    offset = column_index * term_dev
    samples = float(row_count * lax.axis_size("slab") * lax.axis_size("rep"))
    height = 2.0 * (planes.astype(jnp.float32) + 0.5) / NY - 1.0
    root_weight = jnp.sqrt(1.2 - height * height)
    padded = extended(fields, (("slab", 3), ("rep", 2)), 5)
    widened = padded.astype(jnp.float32)
    narrow_taps = kernel(1.5)
    broad_taps = kernel(3.0)
    guard = jnp.minimum(lax.axis_index("rep"), 0)
    span_table = filter_table(cells_z, narrow_taps, broad_taps, guard, (0, 1, 2))
    stream_table = filter_table(cells_x, narrow_taps, broad_taps, guard, (1, 0, 2))
    along_span = jnp.einsum("cpxz,zsn->cpxsn", widened, span_table, precision=lax.Precision.HIGHEST)
    filtered = jnp.einsum(
        "cpxsn,sxm->scpmn", along_span, stream_table, precision=lax.Precision.HIGHEST
    )
    narrow = filtered[0]
    broader = filtered[1]
    narrow_set = narrow.astype(jnp.bfloat16).reshape(chan_dev, row_count)
    broad_set = (
        (broader * root_weight[None, :, None, None])
        .astype(jnp.bfloat16)
        .reshape(chan_dev, row_count)
    )
    weighted = (stresses.astype(jnp.float32) * root_weight[None, :, None, None]).astype(
        jnp.bfloat16
    )
    weighted = weighted.reshape(STRESS, row_count)
    chunk = row_count // col_devices
    block_rows = math.gcd(chunk, 4096)
    block_count = chunk // block_rows
    both_sets = lax.all_to_all(
        jnp.stack([narrow_set, broad_set]), "cols", 2, 1, tiled=True
    )
    narrow_all, broad_all = both_sets[0], both_sets[1]
    weighted = lax.dynamic_slice_in_dim(weighted, column_index * chunk, chunk, 1)

    def gram_step(block_index, carry):
        gram_acc, rhs_acc = carry
        start = block_index * block_rows
        narrow_piece = lax.dynamic_slice_in_dim(narrow_all, start, block_rows, 1)
        broad_piece = lax.dynamic_slice_in_dim(broad_all, start, block_rows, 1)
        all_terms = library(narrow_piece, broad_piece)
        weighted_piece = lax.dynamic_slice_in_dim(weighted, start, block_rows, 1)
        gram_acc = gram_acc + jnp.einsum(
            "ir,jr->ij", all_terms, all_terms, preferred_element_type=jnp.float32
        )
        rhs_acc = rhs_acc + jnp.einsum(
            "ir,kr->ik", all_terms, weighted_piece, preferred_element_type=jnp.float32
        )
        return (gram_acc, rhs_acc)

    gram_part, rhs_part = lax.fori_loop(
        0,
        block_count,
        gram_step,
        (jnp.zeros((TERMS, TERMS), jnp.float32), jnp.zeros((TERMS, STRESS), jnp.float32)),
    )
    full_rows = tree_sum(
        jnp.concatenate([gram_part, rhs_part], axis=1), ("rep", "slab", "cols")
    )
    gram_matrix = full_rows[:, :TERMS]
    rhs_sums = full_rows[:, TERMS:]
    column_scale = 1.0 / jnp.sqrt(jnp.diagonal(gram_matrix) / samples + epsilon)
    normal_gram = column_scale[:, None] * gram_matrix * column_scale[None, :] / samples
    target_norm = column_scale[None, :] * rhs_sums.T / samples

    def apply_normal(vector, active):
        product = jnp.einsum(
            "kl,il->ki", active * vector, normal_gram, precision=lax.Precision.HIGHEST
        )
        return active * product + ridge_weight * vector

    def cg_turn(turn_index, state):
        solution_all, remain, direction, norm_now, active = state
        applied = apply_normal(direction, active)
        curve_sum = jnp.sum(direction * applied, axis=1)
        step_size = norm_now / (curve_sum + epsilon)
        solution_all = solution_all + step_size[:, None] * direction
        remain = remain - step_size[:, None] * applied
        norm_next = jnp.sum(remain * remain, axis=1)
        direction = remain + (norm_next / (norm_now + epsilon))[:, None] * direction
        return (solution_all, remain, direction, norm_next, active)

    def cg_pass(pass_index, state):
        solution_all, coefficients = state
        active = lax.dynamic_index_in_dim(active_masks, pass_index, 0, keepdims=False)
        active = active.astype(jnp.float32)
        solution_all = active * solution_all
        remain = active * target_norm - apply_normal(solution_all, active)
        norm_now = jnp.sum(remain * remain, axis=1)
        solution_all = lax.fori_loop(
            0, ITERS, cg_turn, (solution_all, remain, remain, norm_now, active)
        )[0]
        own_part = lax.dynamic_slice_in_dim(solution_all, offset, term_dev, 1)
        coefficients = lax.dynamic_update_index_in_dim(coefficients, own_part, pass_index, 0)
        return (solution_all, coefficients)

    solution_all, coefficients = lax.fori_loop(
        0,
        PASSES,
        cg_pass,
        (
            jnp.zeros((STRESS, TERMS), jnp.float32),
            jnp.zeros((PASSES, STRESS, term_dev), jnp.float32),
        ),
    )
    final_weights = (column_scale[None, :] * solution_all).astype(jnp.bfloat16)

    def misfit_step(block_index, misfit_acc):
        start = block_index * block_rows
        narrow_piece = lax.dynamic_slice_in_dim(narrow_all, start, block_rows, 1)
        broad_piece = lax.dynamic_slice_in_dim(broad_all, start, block_rows, 1)
        all_terms = library(narrow_piece, broad_piece)
        predicted = jnp.dot(final_weights, all_terms, preferred_element_type=jnp.float32)
        weighted_piece = lax.dynamic_slice_in_dim(weighted, start, block_rows, 1)
        piece_misfit = (weighted_piece.astype(jnp.float32) - predicted).astype(jnp.bfloat16)
        return lax.dynamic_update_slice_in_dim(misfit_acc, piece_misfit, start, 1)

    misfit = lax.fori_loop(
        0, block_count, misfit_step, jnp.zeros((STRESS, chunk), jnp.bfloat16)
    )
    misfit = lax.all_gather(misfit, "cols", axis=1, tiled=True)
    misfit = misfit.reshape(STRESS, plane_count, coarse_x, coarse_z)
    return (coefficients, misfit)


def solution(mesh):
    placed = (
        P("cols", "groups", "rep", "slab"),
        P(None, "groups", "rep", "slab"),
        P("groups"),
        P(),
    )
    return jax.shard_map(
        local,
        mesh=mesh,
        in_specs=placed,
        out_specs=(P(None, "groups", "cols"), P(None, "groups", "rep", "slab")),
        check_vma=False,
    )
```

```python
import math

import jax
import jax.numpy as jnp
import numpy as np
from jax import lax
from jax.sharding import PartitionSpec as P

STRESS = 6
TERMS = 256
NY = 2048
PASSES = 3
ITERS = 3


ridge_weight = 0.05
epsilon = 1e-06


def extended(array, sides, width):
    for axis, dim in sides:
        count, length = (lax.axis_size(axis), array.shape[dim])
        up = [(i, (i + 1) % count) for i in range(count)]
        down = [(j, i) for i, j in up]
        last = lax.slice_in_dim(array, length - width, length, axis=dim)
        leading = lax.slice_in_dim(array, 0, width, axis=dim)
        before = lax.ppermute(last, axis, up)
        after = lax.ppermute(leading, axis, down)
        array = jnp.concatenate([before, array, after], axis=dim)
    return array


def tree_sum(value, axes):
    for axis in axes:
        count = lax.axis_size(axis)
        if count & (count - 1):
            value = lax.psum(value, axis)
            continue
        step = 1
        while step < count:
            partner = [(i, i ^ step) for i in range(count)]
            value = value + lax.ppermute(value, axis, partner)
            step *= 2
    return value


def kernel(spread):
    offsets = np.arange(13) - 6.0
    values = np.exp(-offsets * offsets / (2.0 * spread * spread))
    return values / values.sum()


def filter_table(cells, first_taps, second_taps, guard, order):
    out_count = cells // 4
    shape = tuple((cells + 10, 2, out_count)[d] for d in order)
    where = {d: order.index(d) for d in range(3)}
    position = lax.broadcasted_iota(jnp.int32, shape, where[0])
    which = lax.broadcasted_iota(jnp.int32, shape, where[1])
    out_index = lax.broadcasted_iota(jnp.int32, shape, where[2])
    tap_at = position - 1 - 4 * out_index + guard
    table = jnp.zeros(shape, jnp.float32)
    for tap_index in range(13):
        value = jnp.where(
            which == 0, np.float32(first_taps[tap_index]), np.float32(second_taps[tap_index])
        )
        table = jnp.where(tap_at == tap_index, value, table)
    return table


def library(narrow_part, broad_part):
    product = (
        narrow_part.astype(jnp.float32)[:, None] * broad_part.astype(jnp.float32)[None, :]
    )
    return product.astype(jnp.bfloat16).reshape(
        (narrow_part.shape[0] * broad_part.shape[0],) + narrow_part.shape[1:]
    )


def local(fields, stresses, planes, active_masks):
    chan_dev, plane_count, cells_x, cells_z = fields.shape
    coarse_x = cells_x // 4
    coarse_z = cells_z // 4
    row_count = plane_count * coarse_x * coarse_z
    col_devices = lax.axis_size("cols")
    column_index = lax.axis_index("cols")
    term_dev = TERMS // col_devices
    offset = column_index * term_dev
    samples = float(row_count * lax.axis_size("slab") * lax.axis_size("rep"))
    height = 2.0 * (planes.astype(jnp.float32) + 0.5) / NY - 1.0
    root_weight = jnp.sqrt(1.2 - height * height)
    padded = extended(fields, (("slab", 3), ("rep", 2)), 5)
    widened = padded.astype(jnp.float32)
    narrow_taps = kernel(1.5)
    broad_taps = kernel(3.0)
    guard = jnp.minimum(lax.axis_index("rep"), 0)
    span_table = filter_table(cells_z, narrow_taps, broad_taps, guard, (0, 1, 2))
    stream_table = filter_table(cells_x, narrow_taps, broad_taps, guard, (1, 0, 2))
    along_span = jnp.einsum("cpxz,zsn->cpxsn", widened, span_table, precision=lax.Precision.HIGHEST)
    filtered = jnp.einsum(
        "cpxsn,sxm->scpmn", along_span, stream_table, precision=lax.Precision.HIGHEST
    )
    narrow = filtered[0]
    broader = filtered[1]
    narrow_set = narrow.astype(jnp.bfloat16).reshape(chan_dev, row_count)
    broad_set = (
        (broader * root_weight[None, :, None, None])
        .astype(jnp.bfloat16)
        .reshape(chan_dev, row_count)
    )
    weighted = (stresses.astype(jnp.float32) * root_weight[None, :, None, None]).astype(
        jnp.bfloat16
    )
    weighted = weighted.reshape(STRESS, row_count)
    chunk = row_count // col_devices
    lanes = 128
    chunk_rows = chunk // lanes
    channels = chan_dev * col_devices
    sets = jnp.stack([narrow_set, broad_set]).reshape(2, chan_dev, col_devices, chunk_rows, lanes)
    sets = jnp.transpose(sets, (2, 0, 1, 3, 4)).reshape(col_devices, 2 * chan_dev * chunk_rows, lanes)
    sets = lax.all_to_all(sets, "cols", 0, 0, tiled=True)
    sets = sets.reshape(col_devices, 2, chan_dev, chunk_rows, lanes)
    sets = jnp.transpose(sets, (1, 0, 2, 3, 4)).reshape(2, channels, chunk_rows, lanes)
    narrow_all, broad_all = sets[0], sets[1]
    weighted = weighted.reshape(STRESS, col_devices, chunk_rows, lanes)
    weighted = lax.dynamic_index_in_dim(weighted, column_index, 1, keepdims=False)
    block_rows = math.gcd(chunk_rows, 32)
    block_count = chunk_rows // block_rows

    def gram_step(block_index, carry):
        gram_acc, rhs_acc = carry
        start = block_index * block_rows
        narrow_piece = lax.dynamic_slice_in_dim(narrow_all, start, block_rows, 1)
        broad_piece = lax.dynamic_slice_in_dim(broad_all, start, block_rows, 1)
        all_terms = library(narrow_piece, broad_piece)
        weighted_piece = lax.dynamic_slice_in_dim(weighted, start, block_rows, 1)
        gram_acc = gram_acc + jnp.einsum(
            "iqr,jqr->ij", all_terms, all_terms, preferred_element_type=jnp.float32
        )
        rhs_acc = rhs_acc + jnp.einsum(
            "iqr,kqr->ik", all_terms, weighted_piece, preferred_element_type=jnp.float32
        )
        return (gram_acc, rhs_acc)

    gram_part, rhs_part = lax.fori_loop(
        0,
        block_count,
        gram_step,
        (jnp.zeros((TERMS, TERMS), jnp.float32), jnp.zeros((TERMS, STRESS), jnp.float32)),
    )
    full_rows = tree_sum(
        jnp.concatenate([gram_part, rhs_part], axis=1), ("rep", "slab", "cols")
    )
    gram_matrix = full_rows[:, :TERMS]
    rhs_sums = full_rows[:, TERMS:]
    column_scale = 1.0 / jnp.sqrt(jnp.diagonal(gram_matrix) / samples + epsilon)
    normal_gram = column_scale[:, None] * gram_matrix * column_scale[None, :] / samples
    target_norm = column_scale[None, :] * rhs_sums.T / samples

    def apply_normal(vector, active):
        product = jnp.einsum(
            "kl,il->ki", active * vector, normal_gram, precision=lax.Precision.HIGHEST
        )
        return active * product + ridge_weight * vector

    def cg_turn(turn_index, state):
        solution_all, remain, direction, norm_now, active = state
        applied = apply_normal(direction, active)
        curve_sum = jnp.sum(direction * applied, axis=1)
        step_size = norm_now / (curve_sum + epsilon)
        solution_all = solution_all + step_size[:, None] * direction
        remain = remain - step_size[:, None] * applied
        norm_next = jnp.sum(remain * remain, axis=1)
        direction = remain + (norm_next / (norm_now + epsilon))[:, None] * direction
        return (solution_all, remain, direction, norm_next, active)

    def cg_pass(pass_index, state):
        solution_all, coefficients = state
        active = lax.dynamic_index_in_dim(active_masks, pass_index, 0, keepdims=False)
        active = active.astype(jnp.float32)
        solution_all = active * solution_all
        remain = active * target_norm - apply_normal(solution_all, active)
        norm_now = jnp.sum(remain * remain, axis=1)
        solution_all = lax.fori_loop(
            0, ITERS, cg_turn, (solution_all, remain, remain, norm_now, active)
        )[0]
        own_part = lax.dynamic_slice_in_dim(solution_all, offset, term_dev, 1)
        coefficients = lax.dynamic_update_index_in_dim(coefficients, own_part, pass_index, 0)
        return (solution_all, coefficients)

    solution_all, coefficients = lax.fori_loop(
        0,
        PASSES,
        cg_pass,
        (
            jnp.zeros((STRESS, TERMS), jnp.float32),
            jnp.zeros((PASSES, STRESS, term_dev), jnp.float32),
        ),
    )
    final_weights = (column_scale[None, :] * solution_all).astype(jnp.bfloat16)

    def misfit_step(block_index, misfit_acc):
        start = block_index * block_rows
        narrow_piece = lax.dynamic_slice_in_dim(narrow_all, start, block_rows, 1)
        broad_piece = lax.dynamic_slice_in_dim(broad_all, start, block_rows, 1)
        all_terms = library(narrow_piece, broad_piece)
        predicted = jnp.einsum(
            "ki,iqr->kqr", final_weights, all_terms, preferred_element_type=jnp.float32
        )
        weighted_piece = lax.dynamic_slice_in_dim(weighted, start, block_rows, 1)
        piece_misfit = (weighted_piece.astype(jnp.float32) - predicted).astype(jnp.bfloat16)
        return lax.dynamic_update_slice_in_dim(misfit_acc, piece_misfit, start, 1)

    misfit = lax.fori_loop(
        0, block_count, misfit_step, jnp.zeros((STRESS, chunk_rows, lanes), jnp.bfloat16)
    )
    misfit = lax.all_gather(misfit, "cols", axis=1, tiled=True)
    misfit = misfit.reshape(STRESS, plane_count, coarse_x, coarse_z)
    return (coefficients, misfit)


def solution(mesh):
    placed = (
        P("cols", "groups", "rep", "slab"),
        P(None, "groups", "rep", "slab"),
        P("groups"),
        P(),
    )
    return jax.shard_map(
        local,
        mesh=mesh,
        in_specs=placed,
        out_specs=(P(None, "groups", "cols"), P(None, "groups", "rep", "slab")),
        check_vma=False,
    )
```

```python
import math

import jax
import jax.numpy as jnp
import numpy as np
from jax import lax
from jax.sharding import PartitionSpec as P

STRESS = 6
TERMS = 256
NY = 2048
PASSES = 3
ITERS = 3


ridge_weight = 0.05
epsilon = 1e-06


def extended(array, sides, width):
    for axis, dim in sides:
        count, length = (lax.axis_size(axis), array.shape[dim])
        up = [(i, (i + 1) % count) for i in range(count)]
        down = [(j, i) for i, j in up]
        last = lax.slice_in_dim(array, length - width, length, axis=dim)
        leading = lax.slice_in_dim(array, 0, width, axis=dim)
        before = lax.ppermute(last, axis, up)
        after = lax.ppermute(leading, axis, down)
        array = jnp.concatenate([before, array, after], axis=dim)
    return array


def tree_sum(value, axes):
    for axis in axes:
        count = lax.axis_size(axis)
        if count & (count - 1):
            value = lax.psum(value, axis)
            continue
        step = 1
        while step < count:
            partner = [(i, i ^ step) for i in range(count)]
            value = value + lax.ppermute(value, axis, partner)
            step *= 2
    return value


def split_sum(value, lead, axes):
    count = lax.axis_size(lead)
    if count != 2 or value.shape[0] % 2:
        return tree_sum(value, (lead,) + axes)
    swap = [(0, 1), (1, 0)]
    value = value + lax.ppermute(value, lead, swap)
    half = value.shape[0] // 2
    first = lax.axis_index(lead) == 0
    mine = jnp.where(first, value[:half], value[half:])
    mine = tree_sum(mine, axes)
    other = lax.ppermute(mine, lead, swap)
    return jnp.where(first, jnp.concatenate([mine, other]), jnp.concatenate([other, mine]))


def kernel(spread):
    offsets = np.arange(13) - 6.0
    values = np.exp(-offsets * offsets / (2.0 * spread * spread))
    return values / values.sum()


def filter_table(cells, first_taps, second_taps, guard, order):
    out_count = cells // 4
    shape = tuple((cells + 10, 2, out_count)[d] for d in order)
    where = {d: order.index(d) for d in range(3)}
    position = lax.broadcasted_iota(jnp.int32, shape, where[0])
    which = lax.broadcasted_iota(jnp.int32, shape, where[1])
    out_index = lax.broadcasted_iota(jnp.int32, shape, where[2])
    tap_at = position - 1 - 4 * out_index + guard
    table = jnp.zeros(shape, jnp.float32)
    for tap_index in range(13):
        value = jnp.where(
            which == 0, np.float32(first_taps[tap_index]), np.float32(second_taps[tap_index])
        )
        table = jnp.where(tap_at == tap_index, value, table)
    return table


def library(narrow_part, broad_part):
    product = (
        narrow_part.astype(jnp.float32)[:, None] * broad_part.astype(jnp.float32)[None, :]
    )
    return product.astype(jnp.bfloat16).reshape(
        (narrow_part.shape[0] * broad_part.shape[0],) + narrow_part.shape[1:]
    )


def local(fields, stresses, planes, active_masks):
    chan_dev, plane_count, cells_x, cells_z = fields.shape
    coarse_x = cells_x // 4
    coarse_z = cells_z // 4
    row_count = plane_count * coarse_x * coarse_z
    col_devices = lax.axis_size("cols")
    column_index = lax.axis_index("cols")
    term_dev = TERMS // col_devices
    offset = column_index * term_dev
    samples = float(row_count * lax.axis_size("slab") * lax.axis_size("rep"))
    height = 2.0 * (planes.astype(jnp.float32) + 0.5) / NY - 1.0
    root_weight = jnp.sqrt(1.2 - height * height)
    padded = extended(fields, (("slab", 3), ("rep", 2)), 5)
    widened = padded.astype(jnp.float32)
    narrow_taps = kernel(1.5)
    broad_taps = kernel(3.0)
    guard = jnp.minimum(lax.axis_index("rep"), 0)
    span_table = filter_table(cells_z, narrow_taps, broad_taps, guard, (0, 1, 2))
    stream_table = filter_table(cells_x, narrow_taps, broad_taps, guard, (1, 0, 2))
    along_span = jnp.einsum("cpxz,zsn->cpxsn", widened, span_table, precision=lax.Precision.HIGHEST)
    filtered = jnp.einsum(
        "cpxsn,sxm->scpmn", along_span, stream_table, precision=lax.Precision.HIGHEST
    )
    narrow = filtered[0]
    broader = filtered[1]
    narrow_set = narrow.astype(jnp.bfloat16).reshape(chan_dev, row_count)
    broad_set = (
        (broader * root_weight[None, :, None, None])
        .astype(jnp.bfloat16)
        .reshape(chan_dev, row_count)
    )
    weighted = (stresses.astype(jnp.float32) * root_weight[None, :, None, None]).astype(
        jnp.bfloat16
    )
    weighted = weighted.reshape(STRESS, row_count)
    chunk = row_count // col_devices
    lanes = 128
    chunk_rows = chunk // lanes
    channels = chan_dev * col_devices
    sets = jnp.stack([narrow_set, broad_set]).reshape(2, chan_dev, col_devices, chunk_rows, lanes)
    sets = jnp.transpose(sets, (2, 0, 1, 3, 4)).reshape(col_devices, 2 * chan_dev * chunk_rows, lanes)
    sets = lax.all_to_all(sets, "cols", 0, 0, tiled=True)
    sets = sets.reshape(col_devices, 2, chan_dev, chunk_rows, lanes)
    sets = jnp.transpose(sets, (1, 0, 2, 3, 4)).reshape(2, channels, chunk_rows, lanes)
    narrow_all, broad_all = sets[0], sets[1]
    weighted = weighted.reshape(STRESS, col_devices, chunk_rows, lanes)
    weighted = lax.dynamic_index_in_dim(weighted, column_index, 1, keepdims=False)
    block_rows = math.gcd(chunk_rows, 32)
    block_count = chunk_rows // block_rows

    def gram_step(block_index, carry):
        gram_acc, rhs_acc = carry
        start = block_index * block_rows
        narrow_piece = lax.dynamic_slice_in_dim(narrow_all, start, block_rows, 1)
        broad_piece = lax.dynamic_slice_in_dim(broad_all, start, block_rows, 1)
        all_terms = library(narrow_piece, broad_piece)
        weighted_piece = lax.dynamic_slice_in_dim(weighted, start, block_rows, 1)
        gram_acc = gram_acc + jnp.einsum(
            "iqr,jqr->ij", all_terms, all_terms, preferred_element_type=jnp.float32
        )
        rhs_acc = rhs_acc + jnp.einsum(
            "iqr,kqr->ik", all_terms, weighted_piece, preferred_element_type=jnp.float32
        )
        return (gram_acc, rhs_acc)

    gram_part, rhs_part = lax.fori_loop(
        0,
        block_count,
        gram_step,
        (jnp.zeros((TERMS, TERMS), jnp.float32), jnp.zeros((TERMS, STRESS), jnp.float32)),
    )
    full_rows = split_sum(jnp.concatenate([gram_part, rhs_part], axis=1), "rep", ("slab", "cols"))
    gram_matrix = full_rows[:, :TERMS]
    rhs_sums = full_rows[:, TERMS:]
    column_scale = 1.0 / jnp.sqrt(jnp.diagonal(gram_matrix) / samples + epsilon)
    normal_gram = column_scale[:, None] * gram_matrix * column_scale[None, :] / samples
    target_norm = column_scale[None, :] * rhs_sums.T / samples

    def apply_normal(vector, active):
        product = jnp.einsum(
            "kl,il->ki", active * vector, normal_gram, precision=lax.Precision.HIGHEST
        )
        return active * product + ridge_weight * vector

    def cg_turn(turn_index, state):
        solution_all, remain, direction, norm_now, active = state
        applied = apply_normal(direction, active)
        curve_sum = jnp.sum(direction * applied, axis=1)
        step_size = norm_now / (curve_sum + epsilon)
        solution_all = solution_all + step_size[:, None] * direction
        remain = remain - step_size[:, None] * applied
        norm_next = jnp.sum(remain * remain, axis=1)
        direction = remain + (norm_next / (norm_now + epsilon))[:, None] * direction
        return (solution_all, remain, direction, norm_next, active)

    def cg_pass(pass_index, state):
        solution_all, coefficients = state
        active = lax.dynamic_index_in_dim(active_masks, pass_index, 0, keepdims=False)
        active = active.astype(jnp.float32)
        solution_all = active * solution_all
        remain = active * target_norm - apply_normal(solution_all, active)
        norm_now = jnp.sum(remain * remain, axis=1)
        solution_all = lax.fori_loop(
            0, ITERS, cg_turn, (solution_all, remain, remain, norm_now, active)
        )[0]
        own_part = lax.dynamic_slice_in_dim(solution_all, offset, term_dev, 1)
        coefficients = lax.dynamic_update_index_in_dim(coefficients, own_part, pass_index, 0)
        return (solution_all, coefficients)

    solution_all, coefficients = lax.fori_loop(
        0,
        PASSES,
        cg_pass,
        (
            jnp.zeros((STRESS, TERMS), jnp.float32),
            jnp.zeros((PASSES, STRESS, term_dev), jnp.float32),
        ),
    )
    final_weights = (column_scale[None, :] * solution_all).astype(jnp.bfloat16)

    def misfit_step(block_index, misfit_acc):
        start = block_index * block_rows
        narrow_piece = lax.dynamic_slice_in_dim(narrow_all, start, block_rows, 1)
        broad_piece = lax.dynamic_slice_in_dim(broad_all, start, block_rows, 1)
        all_terms = library(narrow_piece, broad_piece)
        predicted = jnp.einsum(
            "ki,iqr->kqr", final_weights, all_terms, preferred_element_type=jnp.float32
        )
        weighted_piece = lax.dynamic_slice_in_dim(weighted, start, block_rows, 1)
        piece_misfit = (weighted_piece.astype(jnp.float32) - predicted).astype(jnp.bfloat16)
        return lax.dynamic_update_slice_in_dim(misfit_acc, piece_misfit, start, 1)

    misfit = lax.fori_loop(
        0, block_count, misfit_step, jnp.zeros((STRESS, chunk_rows, lanes), jnp.bfloat16)
    )
    misfit = lax.all_gather(misfit, "cols", axis=1, tiled=True)
    misfit = misfit.reshape(STRESS, plane_count, coarse_x, coarse_z)
    return (coefficients, misfit)


def solution(mesh):
    placed = (
        P("cols", "groups", "rep", "slab"),
        P(None, "groups", "rep", "slab"),
        P("groups"),
        P(),
    )
    return jax.shard_map(
        local,
        mesh=mesh,
        in_specs=placed,
        out_specs=(P(None, "groups", "cols"), P(None, "groups", "rep", "slab")),
        check_vma=False,
    )
```

```python
import math

import jax
import jax.numpy as jnp
import numpy as np
from jax import lax
from jax.sharding import PartitionSpec as P

STRESS = 6
TERMS = 256
NY = 2048
PASSES = 3
ITERS = 3


ridge_weight = 0.05
epsilon = 1e-06


def extended(array, sides, width):
    for axis, dim in sides:
        count, length = (lax.axis_size(axis), array.shape[dim])
        up = [(i, (i + 1) % count) for i in range(count)]
        down = [(j, i) for i, j in up]
        last = lax.slice_in_dim(array, length - width, length, axis=dim)
        leading = lax.slice_in_dim(array, 0, width, axis=dim)
        before = lax.ppermute(last, axis, up)
        after = lax.ppermute(leading, axis, down)
        array = jnp.concatenate([before, array, after], axis=dim)
    return array


def tree_sum(value, axes):
    for axis in axes:
        count = lax.axis_size(axis)
        if count & (count - 1):
            value = lax.psum(value, axis)
            continue
        step = 1
        while step < count:
            partner = [(i, i ^ step) for i in range(count)]
            value = value + lax.ppermute(value, axis, partner)
            step *= 2
    return value


def split_sum(value, lead, axes):
    count = lax.axis_size(lead)
    if count != 2 or value.shape[0] % 2:
        return tree_sum(value, (lead,) + axes)
    swap = [(0, 1), (1, 0)]
    value = value + lax.ppermute(value, lead, swap)
    half = value.shape[0] // 2
    first = lax.axis_index(lead) == 0
    mine = jnp.where(first, value[:half], value[half:])
    mine = tree_sum(mine, axes)
    other = lax.ppermute(mine, lead, swap)
    return jnp.where(first, jnp.concatenate([mine, other]), jnp.concatenate([other, mine]))


def neighbour_edges(array, axis, dim, width):
    count, length = (lax.axis_size(axis), array.shape[dim])
    up = [(i, (i + 1) % count) for i in range(count)]
    down = [(j, i) for i, j in up]
    last = lax.slice_in_dim(array, length - width, length, axis=dim)
    leading = lax.slice_in_dim(array, 0, width, axis=dim)
    return (lax.ppermute(last, axis, up), lax.ppermute(leading, axis, down))


def kernel(spread):
    offsets = np.arange(13) - 6.0
    values = np.exp(-offsets * offsets / (2.0 * spread * spread))
    return values / values.sum()


def filter_table(cells, first_taps, second_taps, guard, order):
    out_count = cells // 4
    shape = tuple((cells + 10, 2, out_count)[d] for d in order)
    where = {d: order.index(d) for d in range(3)}
    position = lax.broadcasted_iota(jnp.int32, shape, where[0])
    which = lax.broadcasted_iota(jnp.int32, shape, where[1])
    out_index = lax.broadcasted_iota(jnp.int32, shape, where[2])
    tap_at = position - 1 - 4 * out_index + guard
    table = jnp.zeros(shape, jnp.float32)
    for tap_index in range(13):
        value = jnp.where(
            which == 0, np.float32(first_taps[tap_index]), np.float32(second_taps[tap_index])
        )
        table = jnp.where(tap_at == tap_index, value, table)
    return table


def library(narrow_part, broad_part):
    product = (
        narrow_part.astype(jnp.float32)[:, None] * broad_part.astype(jnp.float32)[None, :]
    )
    return product.astype(jnp.bfloat16).reshape(
        (narrow_part.shape[0] * broad_part.shape[0],) + narrow_part.shape[1:]
    )


def local(fields, stresses, planes, active_masks):
    chan_dev, plane_count, cells_x, cells_z = fields.shape
    coarse_x = cells_x // 4
    coarse_z = cells_z // 4
    row_count = plane_count * coarse_x * coarse_z
    col_devices = lax.axis_size("cols")
    column_index = lax.axis_index("cols")
    term_dev = TERMS // col_devices
    offset = column_index * term_dev
    samples = float(row_count * lax.axis_size("slab") * lax.axis_size("rep"))
    height = 2.0 * (planes.astype(jnp.float32) + 0.5) / NY - 1.0
    root_weight = jnp.sqrt(1.2 - height * height)
    width = 5
    top, bottom = neighbour_edges(fields, "rep", 2, width)
    narrow_taps = kernel(1.5)
    broad_taps = kernel(3.0)
    guard = jnp.minimum(lax.axis_index("rep"), 0)
    span_table = filter_table(cells_z, narrow_taps, broad_taps, guard, (0, 1, 2))
    stream_table = filter_table(cells_x, narrow_taps, broad_taps, guard, (1, 0, 2))
    highest = lax.Precision.HIGHEST
    along_stream = (
        jnp.einsum(
            "cpxz,sxm->scpmz",
            fields.astype(jnp.float32),
            stream_table[:, width : width + cells_x],
            precision=highest,
        )
        + jnp.einsum(
            "cpxz,sxm->scpmz", top.astype(jnp.float32), stream_table[:, :width], precision=highest
        )
        + jnp.einsum(
            "cpxz,sxm->scpmz",
            bottom.astype(jnp.float32),
            stream_table[:, width + cells_x :],
            precision=highest,
        )
    )
    left, right = neighbour_edges(along_stream, "slab", 4, width)
    filtered = (
        jnp.einsum(
            "scpmz,zsn->scpmn",
            along_stream,
            span_table[width : width + cells_z],
            precision=highest,
        )
        + jnp.einsum("scpmz,zsn->scpmn", left, span_table[:width], precision=highest)
        + jnp.einsum("scpmz,zsn->scpmn", right, span_table[width + cells_z :], precision=highest)
    )
    narrow = filtered[0]
    broader = filtered[1]
    narrow_set = narrow.astype(jnp.bfloat16).reshape(chan_dev, row_count)
    broad_set = (
        (broader * root_weight[None, :, None, None])
        .astype(jnp.bfloat16)
        .reshape(chan_dev, row_count)
    )
    weighted = (stresses.astype(jnp.float32) * root_weight[None, :, None, None]).astype(
        jnp.bfloat16
    )
    weighted = weighted.reshape(STRESS, row_count)
    chunk = row_count // col_devices
    lanes = 128
    chunk_rows = chunk // lanes
    channels = chan_dev * col_devices
    sets = jnp.stack([narrow_set, broad_set]).reshape(2, chan_dev, col_devices, chunk_rows, lanes)
    sets = jnp.transpose(sets, (2, 0, 1, 3, 4)).reshape(col_devices, 2 * chan_dev * chunk_rows, lanes)
    sets = lax.all_to_all(sets, "cols", 0, 0, tiled=True)
    sets = sets.reshape(col_devices, 2, chan_dev, chunk_rows, lanes)
    sets = jnp.transpose(sets, (1, 0, 2, 3, 4)).reshape(2, channels, chunk_rows, lanes)
    narrow_all, broad_all = sets[0], sets[1]
    weighted = weighted.reshape(STRESS, col_devices, chunk_rows, lanes)
    weighted = lax.dynamic_index_in_dim(weighted, column_index, 1, keepdims=False)
    block_rows = math.gcd(chunk_rows, 32)
    block_count = chunk_rows // block_rows

    def gram_step(block_index, carry):
        gram_acc, rhs_acc = carry
        start = block_index * block_rows
        narrow_piece = lax.dynamic_slice_in_dim(narrow_all, start, block_rows, 1)
        broad_piece = lax.dynamic_slice_in_dim(broad_all, start, block_rows, 1)
        all_terms = library(narrow_piece, broad_piece)
        weighted_piece = lax.dynamic_slice_in_dim(weighted, start, block_rows, 1)
        gram_acc = gram_acc + jnp.einsum(
            "iqr,jqr->ij", all_terms, all_terms, preferred_element_type=jnp.float32
        )
        rhs_acc = rhs_acc + jnp.einsum(
            "iqr,kqr->ik", all_terms, weighted_piece, preferred_element_type=jnp.float32
        )
        return (gram_acc, rhs_acc)

    gram_part, rhs_part = lax.fori_loop(
        0,
        block_count,
        gram_step,
        (jnp.zeros((TERMS, TERMS), jnp.float32), jnp.zeros((TERMS, STRESS), jnp.float32)),
    )
    full_rows = split_sum(jnp.concatenate([gram_part, rhs_part], axis=1), "rep", ("slab", "cols"))
    gram_matrix = full_rows[:, :TERMS]
    rhs_sums = full_rows[:, TERMS:]
    column_scale = 1.0 / jnp.sqrt(jnp.diagonal(gram_matrix) / samples + epsilon)
    normal_gram = column_scale[:, None] * gram_matrix * column_scale[None, :] / samples
    target_norm = column_scale[None, :] * rhs_sums.T / samples

    def apply_normal(vector, active):
        product = jnp.einsum(
            "kl,il->ki", active * vector, normal_gram, precision=lax.Precision.HIGHEST
        )
        return active * product + ridge_weight * vector

    def cg_turn(turn_index, state):
        solution_all, remain, direction, norm_now, active = state
        applied = apply_normal(direction, active)
        curve_sum = jnp.sum(direction * applied, axis=1)
        step_size = norm_now / (curve_sum + epsilon)
        solution_all = solution_all + step_size[:, None] * direction
        remain = remain - step_size[:, None] * applied
        norm_next = jnp.sum(remain * remain, axis=1)
        direction = remain + (norm_next / (norm_now + epsilon))[:, None] * direction
        return (solution_all, remain, direction, norm_next, active)

    def cg_pass(pass_index, state):
        solution_all, coefficients = state
        active = lax.dynamic_index_in_dim(active_masks, pass_index, 0, keepdims=False)
        active = active.astype(jnp.float32)
        solution_all = active * solution_all
        remain = active * target_norm - apply_normal(solution_all, active)
        norm_now = jnp.sum(remain * remain, axis=1)
        solution_all = lax.fori_loop(
            0, ITERS, cg_turn, (solution_all, remain, remain, norm_now, active)
        )[0]
        own_part = lax.dynamic_slice_in_dim(solution_all, offset, term_dev, 1)
        coefficients = lax.dynamic_update_index_in_dim(coefficients, own_part, pass_index, 0)
        return (solution_all, coefficients)

    solution_all, coefficients = lax.fori_loop(
        0,
        PASSES,
        cg_pass,
        (
            jnp.zeros((STRESS, TERMS), jnp.float32),
            jnp.zeros((PASSES, STRESS, term_dev), jnp.float32),
        ),
    )
    final_weights = (column_scale[None, :] * solution_all).astype(jnp.bfloat16)

    def misfit_step(block_index, misfit_acc):
        start = block_index * block_rows
        narrow_piece = lax.dynamic_slice_in_dim(narrow_all, start, block_rows, 1)
        broad_piece = lax.dynamic_slice_in_dim(broad_all, start, block_rows, 1)
        all_terms = library(narrow_piece, broad_piece)
        predicted = jnp.einsum(
            "ki,iqr->kqr", final_weights, all_terms, preferred_element_type=jnp.float32
        )
        weighted_piece = lax.dynamic_slice_in_dim(weighted, start, block_rows, 1)
        piece_misfit = (weighted_piece.astype(jnp.float32) - predicted).astype(jnp.bfloat16)
        return lax.dynamic_update_slice_in_dim(misfit_acc, piece_misfit, start, 1)

    misfit = lax.fori_loop(
        0, block_count, misfit_step, jnp.zeros((STRESS, chunk_rows, lanes), jnp.bfloat16)
    )
    misfit = lax.all_gather(misfit, "cols", axis=1, tiled=True)
    misfit = misfit.reshape(STRESS, plane_count, coarse_x, coarse_z)
    return (coefficients, misfit)


def solution(mesh):
    placed = (
        P("cols", "groups", "rep", "slab"),
        P(None, "groups", "rep", "slab"),
        P("groups"),
        P(),
    )
    return jax.shard_map(
        local,
        mesh=mesh,
        in_specs=placed,
        out_specs=(P(None, "groups", "cols"), P(None, "groups", "rep", "slab")),
        check_vma=False,
    )
```

```python
import math

import jax
import jax.numpy as jnp
import ml_dtypes
import numpy as np
from jax import lax
from jax.sharding import PartitionSpec as P

STRESS = 6
TERMS = 256
NY = 2048
PASSES = 3
ITERS = 3


ridge_weight = 0.05
epsilon = 1e-06


def extended(array, sides, width):
    for axis, dim in sides:
        count, length = (lax.axis_size(axis), array.shape[dim])
        up = [(i, (i + 1) % count) for i in range(count)]
        down = [(j, i) for i, j in up]
        last = lax.slice_in_dim(array, length - width, length, axis=dim)
        leading = lax.slice_in_dim(array, 0, width, axis=dim)
        before = lax.ppermute(last, axis, up)
        after = lax.ppermute(leading, axis, down)
        array = jnp.concatenate([before, array, after], axis=dim)
    return array


def tree_sum(value, axes):
    for axis in axes:
        count = lax.axis_size(axis)
        if count & (count - 1):
            value = lax.psum(value, axis)
            continue
        step = 1
        while step < count:
            partner = [(i, i ^ step) for i in range(count)]
            value = value + lax.ppermute(value, axis, partner)
            step *= 2
    return value


def split_sum(value, lead, axes):
    count = lax.axis_size(lead)
    if count != 2 or value.shape[0] % 2:
        return tree_sum(value, (lead,) + axes)
    swap = [(0, 1), (1, 0)]
    value = value + lax.ppermute(value, lead, swap)
    half = value.shape[0] // 2
    first = lax.axis_index(lead) == 0
    mine = jnp.where(first, value[:half], value[half:])
    mine = tree_sum(mine, axes)
    other = lax.ppermute(mine, lead, swap)
    return jnp.where(first, jnp.concatenate([mine, other]), jnp.concatenate([other, mine]))


def neighbour_edges(array, axis, dim, width):
    count, length = (lax.axis_size(axis), array.shape[dim])
    up = [(i, (i + 1) % count) for i in range(count)]
    down = [(j, i) for i, j in up]
    last = lax.slice_in_dim(array, length - width, length, axis=dim)
    leading = lax.slice_in_dim(array, 0, width, axis=dim)
    return (lax.ppermute(last, axis, up), lax.ppermute(leading, axis, down))


def split_taps(taps):
    high = np.asarray(np.float32(taps), dtype=ml_dtypes.bfloat16)
    rest = np.float32(taps) - high.astype(np.float32)
    return (high.astype(np.float32), np.asarray(rest, dtype=ml_dtypes.bfloat16).astype(np.float32))


def kernel(spread):
    offsets = np.arange(13) - 6.0
    values = np.exp(-offsets * offsets / (2.0 * spread * spread))
    return values / values.sum()


def filter_table(cells, first_taps, second_taps, guard, order):
    out_count = cells // 4
    shape = tuple((cells + 10, 2, out_count)[d] for d in order)
    where = {d: order.index(d) for d in range(3)}
    position = lax.broadcasted_iota(jnp.int32, shape, where[0])
    which = lax.broadcasted_iota(jnp.int32, shape, where[1])
    out_index = lax.broadcasted_iota(jnp.int32, shape, where[2])
    tap_at = position - 1 - 4 * out_index + guard
    table = jnp.zeros(shape, jnp.float32)
    for tap_index in range(13):
        value = jnp.where(
            which == 0, np.float32(first_taps[tap_index]), np.float32(second_taps[tap_index])
        )
        table = jnp.where(tap_at == tap_index, value, table)
    return table


def library(narrow_part, broad_part):
    product = (
        narrow_part.astype(jnp.float32)[:, None] * broad_part.astype(jnp.float32)[None, :]
    )
    return product.astype(jnp.bfloat16).reshape(
        (narrow_part.shape[0] * broad_part.shape[0],) + narrow_part.shape[1:]
    )


def local(fields, stresses, planes, active_masks):
    chan_dev, plane_count, cells_x, cells_z = fields.shape
    coarse_x = cells_x // 4
    coarse_z = cells_z // 4
    row_count = plane_count * coarse_x * coarse_z
    col_devices = lax.axis_size("cols")
    column_index = lax.axis_index("cols")
    term_dev = TERMS // col_devices
    offset = column_index * term_dev
    samples = float(row_count * lax.axis_size("slab") * lax.axis_size("rep"))
    height = 2.0 * (planes.astype(jnp.float32) + 0.5) / NY - 1.0
    root_weight = jnp.sqrt(1.2 - height * height)
    width = 5
    top, bottom = neighbour_edges(fields, "rep", 2, width)
    narrow_taps = kernel(1.5)
    broad_taps = kernel(3.0)
    guard = jnp.minimum(lax.axis_index("rep"), 0)
    span_table = filter_table(cells_z, narrow_taps, broad_taps, guard, (0, 1, 2))
    highest = lax.Precision.HIGHEST
    stream_pieces = [
        filter_table(cells_x, first, second, guard, (1, 0, 2)).astype(jnp.bfloat16)
        for first, second in zip(split_taps(narrow_taps), split_taps(broad_taps))
    ]
    stream_input = (top, fields, bottom)
    stream_bounds = (0, width, width + cells_x, 2 * width + cells_x)
    along_stream = None
    for piece in stream_pieces:
        for part, low, high in zip(stream_input, stream_bounds[:-1], stream_bounds[1:]):
            term = jnp.einsum(
                "cpxz,sxm->scpmz", part, piece[:, low:high], preferred_element_type=jnp.float32
            )
            along_stream = term if along_stream is None else along_stream + term
    left, right = neighbour_edges(along_stream, "slab", 4, width)
    filtered = (
        jnp.einsum(
            "scpmz,zsn->scpmn",
            along_stream,
            span_table[width : width + cells_z],
            precision=highest,
        )
        + jnp.einsum("scpmz,zsn->scpmn", left, span_table[:width], precision=highest)
        + jnp.einsum("scpmz,zsn->scpmn", right, span_table[width + cells_z :], precision=highest)
    )
    narrow = filtered[0]
    broader = filtered[1]
    narrow_set = narrow.astype(jnp.bfloat16).reshape(chan_dev, row_count)
    broad_set = (
        (broader * root_weight[None, :, None, None])
        .astype(jnp.bfloat16)
        .reshape(chan_dev, row_count)
    )
    weighted = (stresses.astype(jnp.float32) * root_weight[None, :, None, None]).astype(
        jnp.bfloat16
    )
    weighted = weighted.reshape(STRESS, row_count)
    chunk = row_count // col_devices
    lanes = 128
    chunk_rows = chunk // lanes
    channels = chan_dev * col_devices
    sets = jnp.stack([narrow_set, broad_set]).reshape(2, chan_dev, col_devices, chunk_rows, lanes)
    sets = jnp.transpose(sets, (2, 0, 1, 3, 4)).reshape(col_devices, 2 * chan_dev * chunk_rows, lanes)
    sets = lax.all_to_all(sets, "cols", 0, 0, tiled=True)
    sets = sets.reshape(col_devices, 2, chan_dev, chunk_rows, lanes)
    sets = jnp.transpose(sets, (1, 0, 2, 3, 4)).reshape(2, channels, chunk_rows, lanes)
    narrow_all, broad_all = sets[0], sets[1]
    weighted = weighted.reshape(STRESS, col_devices, chunk_rows, lanes)
    weighted = lax.dynamic_index_in_dim(weighted, column_index, 1, keepdims=False)
    block_rows = math.gcd(chunk_rows, 32)
    block_count = chunk_rows // block_rows

    def gram_step(block_index, carry):
        gram_acc, rhs_acc = carry
        start = block_index * block_rows
        narrow_piece = lax.dynamic_slice_in_dim(narrow_all, start, block_rows, 1)
        broad_piece = lax.dynamic_slice_in_dim(broad_all, start, block_rows, 1)
        all_terms = library(narrow_piece, broad_piece)
        weighted_piece = lax.dynamic_slice_in_dim(weighted, start, block_rows, 1)
        gram_acc = gram_acc + jnp.einsum(
            "iqr,jqr->ij", all_terms, all_terms, preferred_element_type=jnp.float32
        )
        rhs_acc = rhs_acc + jnp.einsum(
            "iqr,kqr->ik", all_terms, weighted_piece, preferred_element_type=jnp.float32
        )
        return (gram_acc, rhs_acc)

    gram_part, rhs_part = lax.fori_loop(
        0,
        block_count,
        gram_step,
        (jnp.zeros((TERMS, TERMS), jnp.float32), jnp.zeros((TERMS, STRESS), jnp.float32)),
    )
    full_rows = split_sum(jnp.concatenate([gram_part, rhs_part], axis=1), "rep", ("slab", "cols"))
    gram_matrix = full_rows[:, :TERMS]
    rhs_sums = full_rows[:, TERMS:]
    column_scale = 1.0 / jnp.sqrt(jnp.diagonal(gram_matrix) / samples + epsilon)
    normal_gram = column_scale[:, None] * gram_matrix * column_scale[None, :] / samples
    target_norm = column_scale[None, :] * rhs_sums.T / samples

    def apply_normal(vector, active):
        product = jnp.einsum(
            "kl,il->ki", active * vector, normal_gram, precision=lax.Precision.HIGHEST
        )
        return active * product + ridge_weight * vector

    def cg_turn(turn_index, state):
        solution_all, remain, direction, norm_now, active = state
        applied = apply_normal(direction, active)
        curve_sum = jnp.sum(direction * applied, axis=1)
        step_size = norm_now / (curve_sum + epsilon)
        solution_all = solution_all + step_size[:, None] * direction
        remain = remain - step_size[:, None] * applied
        norm_next = jnp.sum(remain * remain, axis=1)
        direction = remain + (norm_next / (norm_now + epsilon))[:, None] * direction
        return (solution_all, remain, direction, norm_next, active)

    def cg_pass(pass_index, state):
        solution_all, coefficients = state
        active = lax.dynamic_index_in_dim(active_masks, pass_index, 0, keepdims=False)
        active = active.astype(jnp.float32)
        solution_all = active * solution_all
        remain = active * target_norm - apply_normal(solution_all, active)
        norm_now = jnp.sum(remain * remain, axis=1)
        solution_all = lax.fori_loop(
            0, ITERS, cg_turn, (solution_all, remain, remain, norm_now, active)
        )[0]
        own_part = lax.dynamic_slice_in_dim(solution_all, offset, term_dev, 1)
        coefficients = lax.dynamic_update_index_in_dim(coefficients, own_part, pass_index, 0)
        return (solution_all, coefficients)

    solution_all, coefficients = lax.fori_loop(
        0,
        PASSES,
        cg_pass,
        (
            jnp.zeros((STRESS, TERMS), jnp.float32),
            jnp.zeros((PASSES, STRESS, term_dev), jnp.float32),
        ),
    )
    final_weights = (column_scale[None, :] * solution_all).astype(jnp.bfloat16)

    def misfit_step(block_index, misfit_acc):
        start = block_index * block_rows
        narrow_piece = lax.dynamic_slice_in_dim(narrow_all, start, block_rows, 1)
        broad_piece = lax.dynamic_slice_in_dim(broad_all, start, block_rows, 1)
        all_terms = library(narrow_piece, broad_piece)
        predicted = jnp.einsum(
            "ki,iqr->kqr", final_weights, all_terms, preferred_element_type=jnp.float32
        )
        weighted_piece = lax.dynamic_slice_in_dim(weighted, start, block_rows, 1)
        piece_misfit = (weighted_piece.astype(jnp.float32) - predicted).astype(jnp.bfloat16)
        return lax.dynamic_update_slice_in_dim(misfit_acc, piece_misfit, start, 1)

    misfit = lax.fori_loop(
        0, block_count, misfit_step, jnp.zeros((STRESS, chunk_rows, lanes), jnp.bfloat16)
    )
    pieces = [misfit] + [
        lax.ppermute(misfit, "cols", [(i, (i - k) % col_devices) for i in range(col_devices)])
        for k in range(1, col_devices)
    ]
    doubled = jnp.stack(pieces + pieces)
    misfit = lax.dynamic_slice_in_dim(
        doubled, (col_devices - column_index) % col_devices, col_devices, 0
    )
    misfit = jnp.moveaxis(misfit, 0, 1).reshape(STRESS, col_devices * chunk_rows, lanes)
    misfit = misfit.reshape(STRESS, plane_count, coarse_x, coarse_z)
    return (coefficients, misfit)


def solution(mesh):
    placed = (
        P("cols", "groups", "rep", "slab"),
        P(None, "groups", "rep", "slab"),
        P("groups"),
        P(),
    )
    return jax.shard_map(
        local,
        mesh=mesh,
        in_specs=placed,
        out_specs=(P(None, "groups", "cols"), P(None, "groups", "rep", "slab")),
        check_vma=False,
    )
```

```python
import math

import jax
import jax.numpy as jnp
import numpy as np
from jax import lax
from jax.experimental import pallas as pl
from jax.sharding import PartitionSpec as P

STRESS = 6
TERMS = 256
NY = 2048
PASSES = 3
ITERS = 3


ridge_weight = 0.05
epsilon = 1e-06


def extended(array, sides, width):
    for axis, dim in sides:
        count, length = (lax.axis_size(axis), array.shape[dim])
        up = [(i, (i + 1) % count) for i in range(count)]
        down = [(j, i) for i, j in up]
        last = lax.slice_in_dim(array, length - width, length, axis=dim)
        leading = lax.slice_in_dim(array, 0, width, axis=dim)
        before = lax.ppermute(last, axis, up)
        after = lax.ppermute(leading, axis, down)
        array = jnp.concatenate([before, array, after], axis=dim)
    return array


def tree_sum(value, axes):
    for axis in axes:
        count = lax.axis_size(axis)
        if count & (count - 1):
            value = lax.psum(value, axis)
            continue
        step = 1
        while step < count:
            partner = [(i, i ^ step) for i in range(count)]
            value = value + lax.ppermute(value, axis, partner)
            step *= 2
    return value


def split_sum(value, lead, axes):
    count = lax.axis_size(lead)
    if count != 2 or value.shape[0] % 2:
        return tree_sum(value, (lead,) + axes)
    swap = [(0, 1), (1, 0)]
    value = value + lax.ppermute(value, lead, swap)
    half = value.shape[0] // 2
    first = lax.axis_index(lead) == 0
    mine = jnp.where(first, value[:half], value[half:])
    mine = tree_sum(mine, axes)
    other = lax.ppermute(mine, lead, swap)
    return jnp.where(first, jnp.concatenate([mine, other]), jnp.concatenate([other, mine]))


def neighbour_edges(array, axis, dim, width):
    count, length = (lax.axis_size(axis), array.shape[dim])
    up = [(i, (i + 1) % count) for i in range(count)]
    down = [(j, i) for i, j in up]
    last = lax.slice_in_dim(array, length - width, length, axis=dim)
    leading = lax.slice_in_dim(array, 0, width, axis=dim)
    return (lax.ppermute(last, axis, up), lax.ppermute(leading, axis, down))


def conjugate_passes(gram_ref, target_ref, mask_ref, out_ref):
    gram = gram_ref[...]
    target = target_ref[...]

    def apply_normal(vector, active):
        product = lax.dot_general(
            active * vector,
            gram,
            (((1,), (1,)), ((), ())),
            precision=lax.Precision.HIGHEST,
            preferred_element_type=jnp.float32,
        )
        return active * product + ridge_weight * vector

    solution_all = jnp.zeros(target.shape, jnp.float32)
    for pass_index in range(PASSES):
        active = mask_ref[pass_index]
        solution_all = active * solution_all
        remain = active * target - apply_normal(solution_all, active)
        direction = remain
        norm_now = jnp.sum(remain * remain, axis=1, keepdims=True)
        for turn_index in range(ITERS):
            applied = apply_normal(direction, active)
            curve_sum = jnp.sum(direction * applied, axis=1, keepdims=True)
            step_size = norm_now / (curve_sum + epsilon)
            solution_all = solution_all + step_size * direction
            remain = remain - step_size * applied
            norm_next = jnp.sum(remain * remain, axis=1, keepdims=True)
            direction = remain + (norm_next / (norm_now + epsilon)) * direction
            norm_now = norm_next
        out_ref[pass_index] = solution_all


def kernel(spread):
    offsets = np.arange(13) - 6.0
    values = np.exp(-offsets * offsets / (2.0 * spread * spread))
    return values / values.sum()


def filter_table(cells, first_taps, second_taps, guard, order):
    out_count = cells // 4
    shape = tuple((cells + 10, 2, out_count)[d] for d in order)
    where = {d: order.index(d) for d in range(3)}
    position = lax.broadcasted_iota(jnp.int32, shape, where[0])
    which = lax.broadcasted_iota(jnp.int32, shape, where[1])
    out_index = lax.broadcasted_iota(jnp.int32, shape, where[2])
    tap_at = position - 1 - 4 * out_index + guard
    table = jnp.zeros(shape, jnp.float32)
    for tap_index in range(13):
        value = jnp.where(
            which == 0, np.float32(first_taps[tap_index]), np.float32(second_taps[tap_index])
        )
        table = jnp.where(tap_at == tap_index, value, table)
    return table


def library(narrow_part, broad_part):
    product = (
        narrow_part.astype(jnp.float32)[:, None] * broad_part.astype(jnp.float32)[None, :]
    )
    return product.astype(jnp.bfloat16).reshape(
        (narrow_part.shape[0] * broad_part.shape[0],) + narrow_part.shape[1:]
    )


def local(fields, stresses, planes, active_masks):
    chan_dev, plane_count, cells_x, cells_z = fields.shape
    coarse_x = cells_x // 4
    coarse_z = cells_z // 4
    row_count = plane_count * coarse_x * coarse_z
    col_devices = lax.axis_size("cols")
    column_index = lax.axis_index("cols")
    term_dev = TERMS // col_devices
    offset = column_index * term_dev
    samples = float(row_count * lax.axis_size("slab") * lax.axis_size("rep"))
    height = 2.0 * (planes.astype(jnp.float32) + 0.5) / NY - 1.0
    root_weight = jnp.sqrt(1.2 - height * height)
    width = 5
    top, bottom = neighbour_edges(fields, "rep", 2, width)
    narrow_taps = kernel(1.5)
    broad_taps = kernel(3.0)
    guard = jnp.minimum(lax.axis_index("rep"), 0)
    span_table = filter_table(cells_z, narrow_taps, broad_taps, guard, (0, 1, 2))
    stream_table = filter_table(cells_x, narrow_taps, broad_taps, guard, (1, 0, 2))
    highest = lax.Precision.HIGHEST
    along_stream = (
        jnp.einsum(
            "cpxz,sxm->scpmz",
            fields.astype(jnp.float32),
            stream_table[:, width : width + cells_x],
            precision=highest,
        )
        + jnp.einsum(
            "cpxz,sxm->scpmz", top.astype(jnp.float32), stream_table[:, :width], precision=highest
        )
        + jnp.einsum(
            "cpxz,sxm->scpmz",
            bottom.astype(jnp.float32),
            stream_table[:, width + cells_x :],
            precision=highest,
        )
    )
    left, right = neighbour_edges(along_stream, "slab", 4, width)
    filtered = (
        jnp.einsum(
            "scpmz,zsn->scpmn",
            along_stream,
            span_table[width : width + cells_z],
            precision=highest,
        )
        + jnp.einsum("scpmz,zsn->scpmn", left, span_table[:width], precision=highest)
        + jnp.einsum("scpmz,zsn->scpmn", right, span_table[width + cells_z :], precision=highest)
    )
    narrow = filtered[0]
    broader = filtered[1]
    narrow_set = narrow.astype(jnp.bfloat16).reshape(chan_dev, row_count)
    broad_set = (
        (broader * root_weight[None, :, None, None])
        .astype(jnp.bfloat16)
        .reshape(chan_dev, row_count)
    )
    weighted = (stresses.astype(jnp.float32) * root_weight[None, :, None, None]).astype(
        jnp.bfloat16
    )
    weighted = weighted.reshape(STRESS, row_count)
    chunk = row_count // col_devices
    lanes = 128
    chunk_rows = chunk // lanes
    channels = chan_dev * col_devices
    sets = jnp.stack([narrow_set, broad_set]).reshape(2, chan_dev, col_devices, chunk_rows, lanes)
    sets = jnp.transpose(sets, (2, 0, 1, 3, 4)).reshape(col_devices, 2 * chan_dev * chunk_rows, lanes)
    sets = lax.all_to_all(sets, "cols", 0, 0, tiled=True)
    sets = sets.reshape(col_devices, 2, chan_dev, chunk_rows, lanes)
    sets = jnp.transpose(sets, (1, 0, 2, 3, 4)).reshape(2, channels, chunk_rows, lanes)
    narrow_all, broad_all = sets[0], sets[1]
    weighted = weighted.reshape(STRESS, col_devices, chunk_rows, lanes)
    weighted = lax.dynamic_index_in_dim(weighted, column_index, 1, keepdims=False)
    block_rows = math.gcd(chunk_rows, 32)
    block_count = chunk_rows // block_rows

    def gram_step(block_index, carry):
        gram_acc, rhs_acc = carry
        start = block_index * block_rows
        narrow_piece = lax.dynamic_slice_in_dim(narrow_all, start, block_rows, 1)
        broad_piece = lax.dynamic_slice_in_dim(broad_all, start, block_rows, 1)
        all_terms = library(narrow_piece, broad_piece)
        weighted_piece = lax.dynamic_slice_in_dim(weighted, start, block_rows, 1)
        gram_acc = gram_acc + jnp.einsum(
            "iqr,jqr->ij", all_terms, all_terms, preferred_element_type=jnp.float32
        )
        rhs_acc = rhs_acc + jnp.einsum(
            "iqr,kqr->ik", all_terms, weighted_piece, preferred_element_type=jnp.float32
        )
        return (gram_acc, rhs_acc)

    gram_part, rhs_part = lax.fori_loop(
        0,
        block_count,
        gram_step,
        (jnp.zeros((TERMS, TERMS), jnp.float32), jnp.zeros((TERMS, STRESS), jnp.float32)),
    )
    full_rows = split_sum(jnp.concatenate([gram_part, rhs_part], axis=1), "rep", ("slab", "cols"))
    gram_matrix = full_rows[:, :TERMS]
    rhs_sums = full_rows[:, TERMS:]
    column_scale = 1.0 / jnp.sqrt(jnp.diagonal(gram_matrix) / samples + epsilon)
    normal_gram = column_scale[:, None] * gram_matrix * column_scale[None, :] / samples
    target_norm = column_scale[None, :] * rhs_sums.T / samples

    padded_rows = -(-STRESS // 8) * 8
    target_padded = jnp.zeros((padded_rows, TERMS), jnp.float32).at[:STRESS].set(target_norm)
    masks_padded = (
        jnp.zeros((PASSES, padded_rows, TERMS), jnp.float32)
        .at[:, :STRESS]
        .set(active_masks.astype(jnp.float32))
    )
    passes = pl.pallas_call(
        conjugate_passes,
        out_shape=jax.ShapeDtypeStruct((PASSES, padded_rows, TERMS), jnp.float32),
    )(normal_gram, target_padded, masks_padded)
    coefficients = lax.dynamic_slice_in_dim(passes[:, :STRESS], offset, term_dev, 2)
    solution_all = passes[PASSES - 1, :STRESS]
    final_weights = (column_scale[None, :] * solution_all).astype(jnp.bfloat16)

    def misfit_step(block_index, misfit_acc):
        start = block_index * block_rows
        narrow_piece = lax.dynamic_slice_in_dim(narrow_all, start, block_rows, 1)
        broad_piece = lax.dynamic_slice_in_dim(broad_all, start, block_rows, 1)
        all_terms = library(narrow_piece, broad_piece)
        predicted = jnp.einsum(
            "ki,iqr->kqr", final_weights, all_terms, preferred_element_type=jnp.float32
        )
        weighted_piece = lax.dynamic_slice_in_dim(weighted, start, block_rows, 1)
        piece_misfit = (weighted_piece.astype(jnp.float32) - predicted).astype(jnp.bfloat16)
        return lax.dynamic_update_slice_in_dim(misfit_acc, piece_misfit, start, 1)

    misfit = lax.fori_loop(
        0, block_count, misfit_step, jnp.zeros((STRESS, chunk_rows, lanes), jnp.bfloat16)
    )
    misfit = lax.all_gather(misfit, "cols", axis=1, tiled=True)
    misfit = misfit.reshape(STRESS, plane_count, coarse_x, coarse_z)
    return (coefficients, misfit)


def solution(mesh):
    placed = (
        P("cols", "groups", "rep", "slab"),
        P(None, "groups", "rep", "slab"),
        P("groups"),
        P(),
    )
    return jax.shard_map(
        local,
        mesh=mesh,
        in_specs=placed,
        out_specs=(P(None, "groups", "cols"), P(None, "groups", "rep", "slab")),
        check_vma=False,
    )
```

```python
import math

import jax
import jax.numpy as jnp
import numpy as np
from jax import lax
from jax.experimental import pallas as pl
from jax.sharding import PartitionSpec as P

STRESS = 6
TERMS = 256
NY = 2048
PASSES = 3
ITERS = 3


ridge_weight = 0.05
epsilon = 1e-06


def extended(array, sides, width):
    for axis, dim in sides:
        count, length = (lax.axis_size(axis), array.shape[dim])
        up = [(i, (i + 1) % count) for i in range(count)]
        down = [(j, i) for i, j in up]
        last = lax.slice_in_dim(array, length - width, length, axis=dim)
        leading = lax.slice_in_dim(array, 0, width, axis=dim)
        before = lax.ppermute(last, axis, up)
        after = lax.ppermute(leading, axis, down)
        array = jnp.concatenate([before, array, after], axis=dim)
    return array


def tree_sum(value, axes):
    for axis in axes:
        count = lax.axis_size(axis)
        if count & (count - 1):
            value = lax.psum(value, axis)
            continue
        step = 1
        while step < count:
            partner = [(i, i ^ step) for i in range(count)]
            value = value + lax.ppermute(value, axis, partner)
            step *= 2
    return value


def split_sum(value, lead, axes):
    count = lax.axis_size(lead)
    if count != 2 or value.shape[0] % 2:
        return tree_sum(value, (lead,) + axes)
    swap = [(0, 1), (1, 0)]
    value = value + lax.ppermute(value, lead, swap)
    half = value.shape[0] // 2
    first = lax.axis_index(lead) == 0
    mine = jnp.where(first, value[:half], value[half:])
    mine = tree_sum(mine, axes)
    other = lax.ppermute(mine, lead, swap)
    return jnp.where(first, jnp.concatenate([mine, other]), jnp.concatenate([other, mine]))


def neighbour_edges(array, axis, dim, width):
    count, length = (lax.axis_size(axis), array.shape[dim])
    up = [(i, (i + 1) % count) for i in range(count)]
    down = [(j, i) for i, j in up]
    last = lax.slice_in_dim(array, length - width, length, axis=dim)
    leading = lax.slice_in_dim(array, 0, width, axis=dim)
    return (lax.ppermute(last, axis, up), lax.ppermute(leading, axis, down))


def conjugate_passes(gram_ref, target_ref, mask_ref, out_ref):
    gram = gram_ref[...]
    target = target_ref[...]

    def apply_normal(vector, active):
        product = lax.dot_general(
            active * vector,
            gram,
            (((1,), (1,)), ((), ())),
            precision=lax.Precision.HIGHEST,
            preferred_element_type=jnp.float32,
        )
        return active * product + ridge_weight * vector

    solution_all = jnp.zeros(target.shape, jnp.float32)
    for pass_index in range(PASSES):
        active = mask_ref[pass_index]
        solution_all = active * solution_all
        remain = active * target - apply_normal(solution_all, active)
        direction = remain
        norm_now = jnp.sum(remain * remain, axis=1, keepdims=True)
        for turn_index in range(ITERS):
            applied = apply_normal(direction, active)
            curve_sum = jnp.sum(direction * applied, axis=1, keepdims=True)
            step_size = norm_now / (curve_sum + epsilon)
            solution_all = solution_all + step_size * direction
            remain = remain - step_size * applied
            norm_next = jnp.sum(remain * remain, axis=1, keepdims=True)
            direction = remain + (norm_next / (norm_now + epsilon)) * direction
            norm_now = norm_next
        out_ref[pass_index] = solution_all


def filter_fields(fields, stream_table, span_table):
    width = 5
    cells_x, cells_z = fields.shape[2:]
    highest = lax.Precision.HIGHEST
    top, bottom = neighbour_edges(fields, "rep", 2, width)
    along_stream = (
        jnp.einsum(
            "cpxz,sxm->scpmz",
            fields.astype(jnp.float32),
            stream_table[:, width : width + cells_x],
            precision=highest,
        )
        + jnp.einsum(
            "cpxz,sxm->scpmz", top.astype(jnp.float32), stream_table[:, :width], precision=highest
        )
        + jnp.einsum(
            "cpxz,sxm->scpmz",
            bottom.astype(jnp.float32),
            stream_table[:, width + cells_x :],
            precision=highest,
        )
    )
    left, right = neighbour_edges(along_stream, "slab", 4, width)
    filtered = (
        jnp.einsum(
            "scpmz,zsn->scpmn",
            along_stream,
            span_table[width : width + cells_z],
            precision=highest,
        )
        + jnp.einsum("scpmz,zsn->scpmn", left, span_table[:width], precision=highest)
        + jnp.einsum("scpmz,zsn->scpmn", right, span_table[width + cells_z :], precision=highest)
    )
    return (filtered[0], filtered[1])


def kernel(spread):
    offsets = np.arange(13) - 6.0
    values = np.exp(-offsets * offsets / (2.0 * spread * spread))
    return values / values.sum()


def filter_table(cells, first_taps, second_taps, guard, order):
    out_count = cells // 4
    shape = tuple((cells + 10, 2, out_count)[d] for d in order)
    where = {d: order.index(d) for d in range(3)}
    position = lax.broadcasted_iota(jnp.int32, shape, where[0])
    which = lax.broadcasted_iota(jnp.int32, shape, where[1])
    out_index = lax.broadcasted_iota(jnp.int32, shape, where[2])
    tap_at = position - 1 - 4 * out_index + guard
    table = jnp.zeros(shape, jnp.float32)
    for tap_index in range(13):
        value = jnp.where(
            which == 0, np.float32(first_taps[tap_index]), np.float32(second_taps[tap_index])
        )
        table = jnp.where(tap_at == tap_index, value, table)
    return table


def library(narrow_part, broad_part):
    product = (
        narrow_part.astype(jnp.float32)[:, None] * broad_part.astype(jnp.float32)[None, :]
    )
    return product.astype(jnp.bfloat16).reshape(
        (narrow_part.shape[0] * broad_part.shape[0],) + narrow_part.shape[1:]
    )


def local(fields, stresses, planes, active_masks):
    chan_dev, plane_count, cells_x, cells_z = fields.shape
    coarse_x = cells_x // 4
    coarse_z = cells_z // 4
    row_count = plane_count * coarse_x * coarse_z
    col_devices = lax.axis_size("cols")
    column_index = lax.axis_index("cols")
    term_dev = TERMS // col_devices
    offset = column_index * term_dev
    samples = float(row_count * lax.axis_size("slab") * lax.axis_size("rep"))
    height = 2.0 * (planes.astype(jnp.float32) + 0.5) / NY - 1.0
    root_weight = jnp.sqrt(1.2 - height * height)
    narrow_taps = kernel(1.5)
    broad_taps = kernel(3.0)
    guard = jnp.minimum(lax.axis_index("rep"), 0)
    span_table = filter_table(cells_z, narrow_taps, broad_taps, guard, (0, 1, 2))
    stream_table = filter_table(cells_x, narrow_taps, broad_taps, guard, (1, 0, 2))
    stages = 2 if plane_count % 2 == 0 and (row_count // 2) % (col_devices * 128) == 0 else 1
    stage_planes = plane_count // stages
    stage_rows = row_count // stages
    lanes = 128
    stage_chunk_rows = stage_rows // col_devices // lanes
    chunk_rows = stages * stage_chunk_rows
    channels = chan_dev * col_devices
    exchanged = []
    for stage in range(stages):
        plane_slice = slice(stage * stage_planes, (stage + 1) * stage_planes)
        narrow, broader = filter_fields(fields[:, plane_slice], stream_table, span_table)
        narrow_set = narrow.astype(jnp.bfloat16).reshape(chan_dev, stage_rows)
        broad_set = (
            (broader * root_weight[plane_slice][None, :, None, None])
            .astype(jnp.bfloat16)
            .reshape(chan_dev, stage_rows)
        )
        sets = jnp.stack([narrow_set, broad_set])
        sets = sets.reshape(2, chan_dev, col_devices, stage_chunk_rows, lanes)
        sets = jnp.transpose(sets, (2, 0, 1, 3, 4))
        sets = sets.reshape(col_devices, 2 * chan_dev * stage_chunk_rows, lanes)
        sets = lax.all_to_all(sets, "cols", 0, 0, tiled=True)
        sets = sets.reshape(col_devices, 2, chan_dev, stage_chunk_rows, lanes)
        sets = jnp.transpose(sets, (1, 0, 2, 3, 4))
        exchanged.append(sets.reshape(2, channels, stage_chunk_rows, lanes))
    sets = jnp.concatenate(exchanged, axis=2)
    narrow_all, broad_all = sets[0], sets[1]
    weighted = (stresses.astype(jnp.float32) * root_weight[None, :, None, None]).astype(
        jnp.bfloat16
    )
    weighted = weighted.reshape(STRESS, stages, col_devices, stage_chunk_rows, lanes)
    weighted = lax.dynamic_index_in_dim(weighted, column_index, 2, keepdims=False)
    weighted = weighted.reshape(STRESS, chunk_rows, lanes)
    block_rows = math.gcd(chunk_rows, 32)
    block_count = chunk_rows // block_rows

    def gram_step(block_index, carry):
        gram_acc, rhs_acc = carry
        start = block_index * block_rows
        narrow_piece = lax.dynamic_slice_in_dim(narrow_all, start, block_rows, 1)
        broad_piece = lax.dynamic_slice_in_dim(broad_all, start, block_rows, 1)
        all_terms = library(narrow_piece, broad_piece)
        weighted_piece = lax.dynamic_slice_in_dim(weighted, start, block_rows, 1)
        gram_acc = gram_acc + jnp.einsum(
            "iqr,jqr->ij", all_terms, all_terms, preferred_element_type=jnp.float32
        )
        rhs_acc = rhs_acc + jnp.einsum(
            "iqr,kqr->ik", all_terms, weighted_piece, preferred_element_type=jnp.float32
        )
        return (gram_acc, rhs_acc)

    gram_part, rhs_part = lax.fori_loop(
        0,
        block_count,
        gram_step,
        (jnp.zeros((TERMS, TERMS), jnp.float32), jnp.zeros((TERMS, STRESS), jnp.float32)),
    )
    full_rows = split_sum(jnp.concatenate([gram_part, rhs_part], axis=1), "rep", ("slab", "cols"))
    gram_matrix = full_rows[:, :TERMS]
    rhs_sums = full_rows[:, TERMS:]
    column_scale = 1.0 / jnp.sqrt(jnp.diagonal(gram_matrix) / samples + epsilon)
    normal_gram = column_scale[:, None] * gram_matrix * column_scale[None, :] / samples
    target_norm = column_scale[None, :] * rhs_sums.T / samples

    padded_rows = -(-STRESS // 8) * 8
    target_padded = jnp.zeros((padded_rows, TERMS), jnp.float32).at[:STRESS].set(target_norm)
    masks_padded = (
        jnp.zeros((PASSES, padded_rows, TERMS), jnp.float32)
        .at[:, :STRESS]
        .set(active_masks.astype(jnp.float32))
    )
    passes = pl.pallas_call(
        conjugate_passes,
        out_shape=jax.ShapeDtypeStruct((PASSES, padded_rows, TERMS), jnp.float32),
    )(normal_gram, target_padded, masks_padded)
    coefficients = lax.dynamic_slice_in_dim(passes[:, :STRESS], offset, term_dev, 2)
    solution_all = passes[PASSES - 1, :STRESS]
    final_weights = (column_scale[None, :] * solution_all).astype(jnp.bfloat16)

    def misfit_step(block_index, misfit_acc):
        start = block_index * block_rows
        narrow_piece = lax.dynamic_slice_in_dim(narrow_all, start, block_rows, 1)
        broad_piece = lax.dynamic_slice_in_dim(broad_all, start, block_rows, 1)
        all_terms = library(narrow_piece, broad_piece)
        predicted = jnp.einsum(
            "ki,iqr->kqr", final_weights, all_terms, preferred_element_type=jnp.float32
        )
        weighted_piece = lax.dynamic_slice_in_dim(weighted, start, block_rows, 1)
        piece_misfit = (weighted_piece.astype(jnp.float32) - predicted).astype(jnp.bfloat16)
        return lax.dynamic_update_slice_in_dim(misfit_acc, piece_misfit, start, 1)

    misfit = lax.fori_loop(
        0, block_count, misfit_step, jnp.zeros((STRESS, chunk_rows, lanes), jnp.bfloat16)
    )
    misfit = misfit.reshape(STRESS, stages, stage_chunk_rows, lanes)
    misfit = lax.all_gather(misfit, "cols", axis=2)
    misfit = misfit.reshape(STRESS, plane_count, coarse_x, coarse_z)
    return (coefficients, misfit)


def solution(mesh):
    placed = (
        P("cols", "groups", "rep", "slab"),
        P(None, "groups", "rep", "slab"),
        P("groups"),
        P(),
    )
    return jax.shard_map(
        local,
        mesh=mesh,
        in_specs=placed,
        out_specs=(P(None, "groups", "cols"), P(None, "groups", "rep", "slab")),
        check_vma=False,
    )
```

```python
import math

import jax
import jax.numpy as jnp
import numpy as np
from jax import lax
from jax.experimental import pallas as pl
from jax.sharding import PartitionSpec as P

STRESS = 6
TERMS = 256
NY = 2048
PASSES = 3
ITERS = 3


ridge_weight = 0.05
epsilon = 1e-06


def extended(array, sides, width):
    for axis, dim in sides:
        count, length = (lax.axis_size(axis), array.shape[dim])
        up = [(i, (i + 1) % count) for i in range(count)]
        down = [(j, i) for i, j in up]
        last = lax.slice_in_dim(array, length - width, length, axis=dim)
        leading = lax.slice_in_dim(array, 0, width, axis=dim)
        before = lax.ppermute(last, axis, up)
        after = lax.ppermute(leading, axis, down)
        array = jnp.concatenate([before, array, after], axis=dim)
    return array


def tree_sum(value, axes):
    for axis in axes:
        count = lax.axis_size(axis)
        if count & (count - 1):
            value = lax.psum(value, axis)
            continue
        step = 1
        while step < count:
            partner = [(i, i ^ step) for i in range(count)]
            value = value + lax.ppermute(value, axis, partner)
            step *= 2
    return value


def split_sum(value, lead, axes):
    count = lax.axis_size(lead)
    if count != 2 or value.shape[0] % 2:
        return tree_sum(value, (lead,) + axes)
    swap = [(0, 1), (1, 0)]
    value = value + lax.ppermute(value, lead, swap)
    half = value.shape[0] // 2
    first = lax.axis_index(lead) == 0
    mine = jnp.where(first, value[:half], value[half:])
    mine = tree_sum(mine, axes)
    other = lax.ppermute(mine, lead, swap)
    return jnp.where(first, jnp.concatenate([mine, other]), jnp.concatenate([other, mine]))


def neighbour_edges(array, axis, dim, width):
    count, length = (lax.axis_size(axis), array.shape[dim])
    up = [(i, (i + 1) % count) for i in range(count)]
    down = [(j, i) for i, j in up]
    last = lax.slice_in_dim(array, length - width, length, axis=dim)
    leading = lax.slice_in_dim(array, 0, width, axis=dim)
    return (lax.ppermute(last, axis, up), lax.ppermute(leading, axis, down))


def conjugate_passes(gram_ref, target_ref, mask_ref, out_ref):
    gram = gram_ref[...]
    target = target_ref[...]

    def apply_normal(vector, active):
        product = lax.dot_general(
            active * vector,
            gram,
            (((1,), (1,)), ((), ())),
            precision=lax.Precision.HIGHEST,
            preferred_element_type=jnp.float32,
        )
        return active * product + ridge_weight * vector

    solution_all = jnp.zeros(target.shape, jnp.float32)
    for pass_index in range(PASSES):
        active = mask_ref[pass_index]
        solution_all = active * solution_all
        remain = active * target - apply_normal(solution_all, active)
        direction = remain
        norm_now = jnp.sum(remain * remain, axis=1, keepdims=True)
        for turn_index in range(ITERS):
            applied = apply_normal(direction, active)
            curve_sum = jnp.sum(direction * applied, axis=1, keepdims=True)
            step_size = norm_now / (curve_sum + epsilon)
            solution_all = solution_all + step_size * direction
            remain = remain - step_size * applied
            norm_next = jnp.sum(remain * remain, axis=1, keepdims=True)
            direction = remain + (norm_next / (norm_now + epsilon)) * direction
            norm_now = norm_next
        out_ref[pass_index] = solution_all


def banded_table(out_count, rows, first_taps, second_taps, guard):
    shape = (2, out_count, rows)
    which = lax.broadcasted_iota(jnp.int32, shape, 0)
    out_index = lax.broadcasted_iota(jnp.int32, shape, 1)
    position = lax.broadcasted_iota(jnp.int32, shape, 2)
    tap_at = position - 4 * out_index + guard
    table = jnp.zeros(shape, jnp.float32)
    for tap_index in range(13):
        value = jnp.where(
            which == 0, np.float32(first_taps[tap_index]), np.float32(second_taps[tap_index])
        )
        table = jnp.where(tap_at == tap_index, value, table)
    return table


def kernel(spread):
    offsets = np.arange(13) - 6.0
    values = np.exp(-offsets * offsets / (2.0 * spread * spread))
    return values / values.sum()


def filter_table(cells, first_taps, second_taps, guard, order):
    out_count = cells // 4
    shape = tuple((cells + 10, 2, out_count)[d] for d in order)
    where = {d: order.index(d) for d in range(3)}
    position = lax.broadcasted_iota(jnp.int32, shape, where[0])
    which = lax.broadcasted_iota(jnp.int32, shape, where[1])
    out_index = lax.broadcasted_iota(jnp.int32, shape, where[2])
    tap_at = position - 1 - 4 * out_index + guard
    table = jnp.zeros(shape, jnp.float32)
    for tap_index in range(13):
        value = jnp.where(
            which == 0, np.float32(first_taps[tap_index]), np.float32(second_taps[tap_index])
        )
        table = jnp.where(tap_at == tap_index, value, table)
    return table


def library(narrow_part, broad_part):
    product = (
        narrow_part.astype(jnp.float32)[:, None] * broad_part.astype(jnp.float32)[None, :]
    )
    return product.astype(jnp.bfloat16).reshape(
        (narrow_part.shape[0] * broad_part.shape[0],) + narrow_part.shape[1:]
    )


def local(fields, stresses, planes, active_masks):
    chan_dev, plane_count, cells_x, cells_z = fields.shape
    coarse_x = cells_x // 4
    coarse_z = cells_z // 4
    row_count = plane_count * coarse_x * coarse_z
    col_devices = lax.axis_size("cols")
    column_index = lax.axis_index("cols")
    term_dev = TERMS // col_devices
    offset = column_index * term_dev
    samples = float(row_count * lax.axis_size("slab") * lax.axis_size("rep"))
    height = 2.0 * (planes.astype(jnp.float32) + 0.5) / NY - 1.0
    root_weight = jnp.sqrt(1.2 - height * height)
    width = 5
    top, bottom = neighbour_edges(fields, "rep", 2, width)
    narrow_taps = kernel(1.5)
    broad_taps = kernel(3.0)
    guard = jnp.minimum(lax.axis_index("rep"), 0)
    span_table = filter_table(cells_z, narrow_taps, broad_taps, guard, (0, 1, 2))
    stream_table = filter_table(cells_x, narrow_taps, broad_taps, guard, (1, 0, 2))
    highest = lax.Precision.HIGHEST
    block = 128
    if cells_x % block == 0:
        block_count_x = cells_x // block
        blocked = fields.reshape(chan_dev, plane_count, block_count_x, block, cells_z)
        before = jnp.concatenate(
            [top[:, :, None, 1:width], blocked[:, :, :-1, block - width + 1 :]], axis=2
        )
        after = jnp.concatenate([blocked[:, :, 1:, :width], bottom[:, :, None]], axis=2)
        spare = jnp.zeros((chan_dev, plane_count, block_count_x, 7, cells_z), fields.dtype)
        windows = jnp.concatenate([before, blocked, after, spare], axis=3)
        window_rows = windows.shape[3]
        window_table = banded_table(block // 4, window_rows, narrow_taps, broad_taps, guard)
        along_stream = jnp.einsum(
            "cpbrz,sir->scpbiz", windows.astype(jnp.float32), window_table, precision=highest
        ).reshape(2, chan_dev, plane_count, coarse_x, cells_z)
    else:
        along_stream = (
            jnp.einsum(
                "cpxz,sxm->scpmz",
                fields.astype(jnp.float32),
                stream_table[:, width : width + cells_x],
                precision=highest,
            )
            + jnp.einsum(
                "cpxz,sxm->scpmz",
                top.astype(jnp.float32),
                stream_table[:, :width],
                precision=highest,
            )
            + jnp.einsum(
                "cpxz,sxm->scpmz",
                bottom.astype(jnp.float32),
                stream_table[:, width + cells_x :],
                precision=highest,
            )
        )
    left, right = neighbour_edges(along_stream, "slab", 4, width)
    filtered = (
        jnp.einsum(
            "scpmz,zsn->scpmn",
            along_stream,
            span_table[width : width + cells_z],
            precision=highest,
        )
        + jnp.einsum("scpmz,zsn->scpmn", left, span_table[:width], precision=highest)
        + jnp.einsum("scpmz,zsn->scpmn", right, span_table[width + cells_z :], precision=highest)
    )
    narrow = filtered[0]
    broader = filtered[1]
    narrow_set = narrow.astype(jnp.bfloat16).reshape(chan_dev, row_count)
    broad_set = (
        (broader * root_weight[None, :, None, None])
        .astype(jnp.bfloat16)
        .reshape(chan_dev, row_count)
    )
    weighted = (stresses.astype(jnp.float32) * root_weight[None, :, None, None]).astype(
        jnp.bfloat16
    )
    weighted = weighted.reshape(STRESS, row_count)
    chunk = row_count // col_devices
    lanes = 128
    chunk_rows = chunk // lanes
    channels = chan_dev * col_devices
    sets = jnp.stack([narrow_set, broad_set]).reshape(2, chan_dev, col_devices, chunk_rows, lanes)
    sets = jnp.transpose(sets, (2, 0, 1, 3, 4)).reshape(col_devices, 2 * chan_dev * chunk_rows, lanes)
    sets = lax.all_to_all(sets, "cols", 0, 0, tiled=True)
    sets = sets.reshape(col_devices, 2, chan_dev, chunk_rows, lanes)
    sets = jnp.transpose(sets, (1, 0, 2, 3, 4)).reshape(2, channels, chunk_rows, lanes)
    narrow_all, broad_all = sets[0], sets[1]
    weighted = weighted.reshape(STRESS, col_devices, chunk_rows, lanes)
    weighted = lax.dynamic_index_in_dim(weighted, column_index, 1, keepdims=False)
    block_rows = math.gcd(chunk_rows, 32)
    block_count = chunk_rows // block_rows

    def gram_step(block_index, carry):
        gram_acc, rhs_acc = carry
        start = block_index * block_rows
        narrow_piece = lax.dynamic_slice_in_dim(narrow_all, start, block_rows, 1)
        broad_piece = lax.dynamic_slice_in_dim(broad_all, start, block_rows, 1)
        all_terms = library(narrow_piece, broad_piece)
        weighted_piece = lax.dynamic_slice_in_dim(weighted, start, block_rows, 1)
        gram_acc = gram_acc + jnp.einsum(
            "iqr,jqr->ij", all_terms, all_terms, preferred_element_type=jnp.float32
        )
        rhs_acc = rhs_acc + jnp.einsum(
            "iqr,kqr->ik", all_terms, weighted_piece, preferred_element_type=jnp.float32
        )
        return (gram_acc, rhs_acc)

    gram_part, rhs_part = lax.fori_loop(
        0,
        block_count,
        gram_step,
        (jnp.zeros((TERMS, TERMS), jnp.float32), jnp.zeros((TERMS, STRESS), jnp.float32)),
    )
    full_rows = split_sum(jnp.concatenate([gram_part, rhs_part], axis=1), "rep", ("slab", "cols"))
    gram_matrix = full_rows[:, :TERMS]
    rhs_sums = full_rows[:, TERMS:]
    column_scale = 1.0 / jnp.sqrt(jnp.diagonal(gram_matrix) / samples + epsilon)
    normal_gram = column_scale[:, None] * gram_matrix * column_scale[None, :] / samples
    target_norm = column_scale[None, :] * rhs_sums.T / samples

    padded_rows = -(-STRESS // 8) * 8
    target_padded = jnp.zeros((padded_rows, TERMS), jnp.float32).at[:STRESS].set(target_norm)
    masks_padded = (
        jnp.zeros((PASSES, padded_rows, TERMS), jnp.float32)
        .at[:, :STRESS]
        .set(active_masks.astype(jnp.float32))
    )
    passes = pl.pallas_call(
        conjugate_passes,
        out_shape=jax.ShapeDtypeStruct((PASSES, padded_rows, TERMS), jnp.float32),
    )(normal_gram, target_padded, masks_padded)
    coefficients = lax.dynamic_slice_in_dim(passes[:, :STRESS], offset, term_dev, 2)
    solution_all = passes[PASSES - 1, :STRESS]
    final_weights = (column_scale[None, :] * solution_all).astype(jnp.bfloat16)

    def misfit_step(block_index, misfit_acc):
        start = block_index * block_rows
        narrow_piece = lax.dynamic_slice_in_dim(narrow_all, start, block_rows, 1)
        broad_piece = lax.dynamic_slice_in_dim(broad_all, start, block_rows, 1)
        all_terms = library(narrow_piece, broad_piece)
        predicted = jnp.einsum(
            "ki,iqr->kqr", final_weights, all_terms, preferred_element_type=jnp.float32
        )
        weighted_piece = lax.dynamic_slice_in_dim(weighted, start, block_rows, 1)
        piece_misfit = (weighted_piece.astype(jnp.float32) - predicted).astype(jnp.bfloat16)
        return lax.dynamic_update_slice_in_dim(misfit_acc, piece_misfit, start, 1)

    misfit = lax.fori_loop(
        0, block_count, misfit_step, jnp.zeros((STRESS, chunk_rows, lanes), jnp.bfloat16)
    )
    misfit = lax.all_gather(misfit, "cols", axis=1, tiled=True)
    misfit = misfit.reshape(STRESS, plane_count, coarse_x, coarse_z)
    return (coefficients, misfit)


def solution(mesh):
    placed = (
        P("cols", "groups", "rep", "slab"),
        P(None, "groups", "rep", "slab"),
        P("groups"),
        P(),
    )
    return jax.shard_map(
        local,
        mesh=mesh,
        in_specs=placed,
        out_specs=(P(None, "groups", "cols"), P(None, "groups", "rep", "slab")),
        check_vma=False,
    )
```

```python
import math

import jax
import jax.numpy as jnp
import numpy as np
from jax import lax
from jax.experimental import pallas as pl
from jax.sharding import PartitionSpec as P

STRESS = 6
TERMS = 256
NY = 2048
PASSES = 3
ITERS = 3


ridge_weight = 0.05
epsilon = 1e-06


def extended(array, sides, width):
    for axis, dim in sides:
        count, length = (lax.axis_size(axis), array.shape[dim])
        up = [(i, (i + 1) % count) for i in range(count)]
        down = [(j, i) for i, j in up]
        last = lax.slice_in_dim(array, length - width, length, axis=dim)
        leading = lax.slice_in_dim(array, 0, width, axis=dim)
        before = lax.ppermute(last, axis, up)
        after = lax.ppermute(leading, axis, down)
        array = jnp.concatenate([before, array, after], axis=dim)
    return array


def tree_sum(value, axes):
    for axis in axes:
        count = lax.axis_size(axis)
        if count & (count - 1):
            value = lax.psum(value, axis)
            continue
        step = 1
        while step < count:
            partner = [(i, i ^ step) for i in range(count)]
            value = value + lax.ppermute(value, axis, partner)
            step *= 2
    return value


def split_sum(value, lead, axes):
    count = lax.axis_size(lead)
    if count != 2 or value.shape[0] % 2:
        return tree_sum(value, (lead,) + axes)
    swap = [(0, 1), (1, 0)]
    value = value + lax.ppermute(value, lead, swap)
    half = value.shape[0] // 2
    first = lax.axis_index(lead) == 0
    mine = jnp.where(first, value[:half], value[half:])
    mine = tree_sum(mine, axes)
    other = lax.ppermute(mine, lead, swap)
    return jnp.where(first, jnp.concatenate([mine, other]), jnp.concatenate([other, mine]))


def neighbour_edges(array, axis, dim, width):
    count, length = (lax.axis_size(axis), array.shape[dim])
    up = [(i, (i + 1) % count) for i in range(count)]
    down = [(j, i) for i, j in up]
    last = lax.slice_in_dim(array, length - width, length, axis=dim)
    leading = lax.slice_in_dim(array, 0, width, axis=dim)
    return (lax.ppermute(last, axis, up), lax.ppermute(leading, axis, down))


def conjugate_passes(gram_ref, target_ref, mask_ref, out_ref):
    gram = gram_ref[...]
    target = target_ref[...]

    def apply_normal(vector, active):
        product = lax.dot_general(
            active * vector,
            gram,
            (((1,), (1,)), ((), ())),
            precision=lax.Precision.HIGHEST,
            preferred_element_type=jnp.float32,
        )
        return active * product + ridge_weight * vector

    solution_all = jnp.zeros(target.shape, jnp.float32)
    for pass_index in range(PASSES):
        active = mask_ref[pass_index]
        solution_all = active * solution_all
        remain = active * target - apply_normal(solution_all, active)
        direction = remain
        norm_now = jnp.sum(remain * remain, axis=1, keepdims=True)
        for turn_index in range(ITERS):
            applied = apply_normal(direction, active)
            curve_sum = jnp.sum(direction * applied, axis=1, keepdims=True)
            step_size = norm_now / (curve_sum + epsilon)
            solution_all = solution_all + step_size * direction
            remain = remain - step_size * applied
            norm_next = jnp.sum(remain * remain, axis=1, keepdims=True)
            direction = remain + (norm_next / (norm_now + epsilon)) * direction
            norm_now = norm_next
        out_ref[pass_index] = solution_all


def kernel(spread):
    offsets = np.arange(13) - 6.0
    values = np.exp(-offsets * offsets / (2.0 * spread * spread))
    return values / values.sum()


def filter_table(cells, first_taps, second_taps, guard, order):
    out_count = cells // 4
    shape = tuple((cells + 10, 2, out_count)[d] for d in order)
    where = {d: order.index(d) for d in range(3)}
    position = lax.broadcasted_iota(jnp.int32, shape, where[0])
    which = lax.broadcasted_iota(jnp.int32, shape, where[1])
    out_index = lax.broadcasted_iota(jnp.int32, shape, where[2])
    tap_at = position - 1 - 4 * out_index + guard
    table = jnp.zeros(shape, jnp.float32)
    for tap_index in range(13):
        value = jnp.where(
            which == 0, np.float32(first_taps[tap_index]), np.float32(second_taps[tap_index])
        )
        table = jnp.where(tap_at == tap_index, value, table)
    return table


def library(narrow_part, broad_part):
    product = (
        narrow_part.astype(jnp.float32)[:, None] * broad_part.astype(jnp.float32)[None, :]
    )
    return product.astype(jnp.bfloat16).reshape(
        (narrow_part.shape[0] * broad_part.shape[0],) + narrow_part.shape[1:]
    )


def local(fields, stresses, planes, active_masks):
    chan_dev, plane_count, cells_x, cells_z = fields.shape
    coarse_x = cells_x // 4
    coarse_z = cells_z // 4
    row_count = plane_count * coarse_x * coarse_z
    col_devices = lax.axis_size("cols")
    column_index = lax.axis_index("cols")
    term_dev = TERMS // col_devices
    offset = column_index * term_dev
    samples = float(row_count * lax.axis_size("slab") * lax.axis_size("rep"))
    height = 2.0 * (planes.astype(jnp.float32) + 0.5) / NY - 1.0
    root_weight = jnp.sqrt(1.2 - height * height)
    width = 5
    top, bottom = neighbour_edges(fields, "rep", 2, width)
    narrow_taps = kernel(1.5)
    broad_taps = kernel(3.0)
    guard = jnp.minimum(lax.axis_index("rep"), 0)
    span_table = filter_table(cells_z, narrow_taps, broad_taps, guard, (0, 1, 2))
    stream_table = filter_table(cells_x, narrow_taps, broad_taps, guard, (1, 0, 2))
    highest = lax.Precision.HIGHEST
    along_stream = (
        jnp.einsum(
            "cpxz,sxm->scpmz",
            fields.astype(jnp.float32),
            stream_table[:, width : width + cells_x],
            precision=highest,
        )
        + jnp.einsum(
            "cpxz,sxm->scpmz", top.astype(jnp.float32), stream_table[:, :width], precision=highest
        )
        + jnp.einsum(
            "cpxz,sxm->scpmz",
            bottom.astype(jnp.float32),
            stream_table[:, width + cells_x :],
            precision=highest,
        )
    )
    left, right = neighbour_edges(along_stream, "slab", 4, width)
    filtered = (
        jnp.einsum(
            "scpmz,zsn->scpmn",
            along_stream,
            span_table[width : width + cells_z],
            precision=highest,
        )
        + jnp.einsum("scpmz,zsn->scpmn", left, span_table[:width], precision=highest)
        + jnp.einsum("scpmz,zsn->scpmn", right, span_table[width + cells_z :], precision=highest)
    )
    narrow = filtered[0]
    broader = filtered[1]
    narrow_set = narrow.astype(jnp.bfloat16).reshape(chan_dev, row_count)
    broad_set = (
        (broader * root_weight[None, :, None, None])
        .astype(jnp.bfloat16)
        .reshape(chan_dev, row_count)
    )
    weighted = (stresses.astype(jnp.float32) * root_weight[None, :, None, None]).astype(
        jnp.bfloat16
    )
    weighted = weighted.reshape(STRESS, row_count)
    chunk = row_count // col_devices
    lanes = 128
    chunk_rows = chunk // lanes
    channels = chan_dev * col_devices
    sets = jnp.stack([narrow_set, broad_set]).reshape(2, chan_dev, col_devices, chunk_rows, lanes)
    sets = jnp.transpose(sets, (2, 0, 1, 3, 4)).reshape(col_devices, 2 * chan_dev * chunk_rows, lanes)
    sets = lax.all_to_all(sets, "cols", 0, 0, tiled=True)
    sets = sets.reshape(col_devices, 2, chan_dev, chunk_rows, lanes)
    sets = jnp.transpose(sets, (1, 0, 2, 3, 4)).reshape(2, channels, chunk_rows, lanes)
    narrow_all, broad_all = sets[0], sets[1]
    weighted = weighted.reshape(STRESS, col_devices, chunk_rows, lanes)
    weighted = lax.dynamic_index_in_dim(weighted, column_index, 1, keepdims=False)
    block_rows = math.gcd(chunk_rows, 32)
    block_count = chunk_rows // block_rows

    def gram_step(block_index, carry):
        gram_acc, rhs_acc = carry
        start = block_index * block_rows
        narrow_piece = lax.dynamic_slice_in_dim(narrow_all, start, block_rows, 1)
        broad_piece = lax.dynamic_slice_in_dim(broad_all, start, block_rows, 1)
        all_terms = library(narrow_piece, broad_piece)
        weighted_piece = lax.dynamic_slice_in_dim(weighted, start, block_rows, 1)
        gram_acc = gram_acc + jnp.einsum(
            "iqr,jqr->ij", all_terms, all_terms, preferred_element_type=jnp.float32
        )
        rhs_acc = rhs_acc + jnp.einsum(
            "iqr,kqr->ik", all_terms, weighted_piece, preferred_element_type=jnp.float32
        )
        return (gram_acc, rhs_acc)

    gram_part, rhs_part = lax.fori_loop(
        0,
        block_count,
        gram_step,
        (jnp.zeros((TERMS, TERMS), jnp.float32), jnp.zeros((TERMS, STRESS), jnp.float32)),
    )
    full_rows = split_sum(jnp.concatenate([gram_part, rhs_part], axis=1), "rep", ("slab", "cols"))
    gram_matrix = full_rows[:, :TERMS]
    rhs_sums = full_rows[:, TERMS:]
    column_scale = 1.0 / jnp.sqrt(jnp.diagonal(gram_matrix) / samples + epsilon)
    normal_gram = column_scale[:, None] * gram_matrix * column_scale[None, :] / samples
    target_norm = column_scale[None, :] * rhs_sums.T / samples

    padded_rows = -(-STRESS // 8) * 8
    target_padded = jnp.zeros((padded_rows, TERMS), jnp.float32).at[:STRESS].set(target_norm)
    masks_padded = (
        jnp.zeros((PASSES, padded_rows, TERMS), jnp.float32)
        .at[:, :STRESS]
        .set(active_masks.astype(jnp.float32))
    )
    passes = pl.pallas_call(
        conjugate_passes,
        out_shape=jax.ShapeDtypeStruct((PASSES, padded_rows, TERMS), jnp.float32),
    )(normal_gram, target_padded, masks_padded)
    coefficients = lax.dynamic_slice_in_dim(passes[:, :STRESS], offset, term_dev, 2)
    solution_all = passes[PASSES - 1, :STRESS]
    final_weights = (column_scale[None, :] * solution_all).astype(jnp.bfloat16)

    def misfit_step(block_index, misfit_acc):
        start = block_index * block_rows
        narrow_piece = lax.dynamic_slice_in_dim(narrow_all, start, block_rows, 1)
        broad_piece = lax.dynamic_slice_in_dim(broad_all, start, block_rows, 1)
        all_terms = library(narrow_piece, broad_piece)
        predicted = jnp.einsum(
            "ki,iqr->kqr", final_weights, all_terms, preferred_element_type=jnp.float32
        )
        weighted_piece = lax.dynamic_slice_in_dim(weighted, start, block_rows, 1)
        piece_misfit = (weighted_piece.astype(jnp.float32) - predicted).astype(jnp.bfloat16)
        return lax.dynamic_update_slice_in_dim(misfit_acc, piece_misfit, start, 1)

    misfit = lax.fori_loop(
        0, block_count, misfit_step, jnp.zeros((STRESS, chunk_rows, lanes), jnp.bfloat16)
    )
    pieces = [misfit] + [
        lax.ppermute(misfit, "cols", [(i, (i - k) % col_devices) for i in range(col_devices)])
        for k in range(1, col_devices)
    ]
    doubled = jnp.stack(pieces + pieces)
    misfit = lax.dynamic_slice_in_dim(
        doubled, (col_devices - column_index) % col_devices, col_devices, 0
    )
    misfit = jnp.moveaxis(misfit, 0, 1).reshape(STRESS, col_devices * chunk_rows, lanes)
    misfit = misfit.reshape(STRESS, plane_count, coarse_x, coarse_z)
    return (coefficients, misfit)


def solution(mesh):
    placed = (
        P("cols", "groups", "rep", "slab"),
        P(None, "groups", "rep", "slab"),
        P("groups"),
        P(),
    )
    return jax.shard_map(
        local,
        mesh=mesh,
        in_specs=placed,
        out_specs=(P(None, "groups", "cols"), P(None, "groups", "rep", "slab")),
        check_vma=False,
    )
```

```python
import math

import jax
import jax.numpy as jnp
import numpy as np
from jax import lax
from jax.experimental import pallas as pl
from jax.sharding import PartitionSpec as P

STRESS = 6
TERMS = 256
NY = 2048
PASSES = 3
ITERS = 3


ridge_weight = 0.05
epsilon = 1e-06


def extended(array, sides, width):
    for axis, dim in sides:
        count, length = (lax.axis_size(axis), array.shape[dim])
        up = [(i, (i + 1) % count) for i in range(count)]
        down = [(j, i) for i, j in up]
        last = lax.slice_in_dim(array, length - width, length, axis=dim)
        leading = lax.slice_in_dim(array, 0, width, axis=dim)
        before = lax.ppermute(last, axis, up)
        after = lax.ppermute(leading, axis, down)
        array = jnp.concatenate([before, array, after], axis=dim)
    return array


def tree_sum(value, axes):
    for axis in axes:
        count = lax.axis_size(axis)
        if count & (count - 1):
            value = lax.psum(value, axis)
            continue
        step = 1
        while step < count:
            partner = [(i, i ^ step) for i in range(count)]
            value = value + lax.ppermute(value, axis, partner)
            step *= 2
    return value


def split_sum(value, lead, axes):
    count = lax.axis_size(lead)
    if count != 2 or value.shape[0] % 2:
        return tree_sum(value, (lead,) + axes)
    swap = [(0, 1), (1, 0)]
    value = value + lax.ppermute(value, lead, swap)
    half = value.shape[0] // 2
    first = lax.axis_index(lead) == 0
    mine = jnp.where(first, value[:half], value[half:])
    mine = tree_sum(mine, axes)
    other = lax.ppermute(mine, lead, swap)
    return jnp.where(first, jnp.concatenate([mine, other]), jnp.concatenate([other, mine]))


def neighbour_edges(array, axis, dim, width):
    count, length = (lax.axis_size(axis), array.shape[dim])
    up = [(i, (i + 1) % count) for i in range(count)]
    down = [(j, i) for i, j in up]
    last = lax.slice_in_dim(array, length - width, length, axis=dim)
    leading = lax.slice_in_dim(array, 0, width, axis=dim)
    return (lax.ppermute(last, axis, up), lax.ppermute(leading, axis, down))


def conjugate_passes(gram_ref, target_ref, mask_ref, out_ref):
    gram = gram_ref[...]
    target = target_ref[...]

    def apply_normal(vector, active):
        product = lax.dot_general(
            active * vector,
            gram,
            (((1,), (1,)), ((), ())),
            precision=lax.Precision.HIGHEST,
            preferred_element_type=jnp.float32,
        )
        return active * product + ridge_weight * vector

    solution_all = jnp.zeros(target.shape, jnp.float32)
    for pass_index in range(PASSES):
        active = mask_ref[pass_index]
        solution_all = active * solution_all
        remain = active * target - apply_normal(solution_all, active)
        direction = remain
        norm_now = jnp.sum(remain * remain, axis=1, keepdims=True)
        for turn_index in range(ITERS):
            applied = apply_normal(direction, active)
            curve_sum = jnp.sum(direction * applied, axis=1, keepdims=True)
            step_size = norm_now / (curve_sum + epsilon)
            solution_all = solution_all + step_size * direction
            remain = remain - step_size * applied
            norm_next = jnp.sum(remain * remain, axis=1, keepdims=True)
            direction = remain + (norm_next / (norm_now + epsilon)) * direction
            norm_now = norm_next
        out_ref[pass_index] = solution_all


def kernel(spread):
    offsets = np.arange(13) - 6.0
    values = np.exp(-offsets * offsets / (2.0 * spread * spread))
    return values / values.sum()


def filter_table(cells, first_taps, second_taps, guard, order):
    out_count = cells // 4
    shape = tuple((cells + 10, 2, out_count)[d] for d in order)
    where = {d: order.index(d) for d in range(3)}
    position = lax.broadcasted_iota(jnp.int32, shape, where[0])
    which = lax.broadcasted_iota(jnp.int32, shape, where[1])
    out_index = lax.broadcasted_iota(jnp.int32, shape, where[2])
    tap_at = position - 1 - 4 * out_index + guard
    table = jnp.zeros(shape, jnp.float32)
    for tap_index in range(13):
        value = jnp.where(
            which == 0, np.float32(first_taps[tap_index]), np.float32(second_taps[tap_index])
        )
        table = jnp.where(tap_at == tap_index, value, table)
    return table


def library(narrow_part, broad_part):
    product = (
        narrow_part.astype(jnp.float32)[:, None] * broad_part.astype(jnp.float32)[None, :]
    )
    return product.astype(jnp.bfloat16).reshape(
        (narrow_part.shape[0] * broad_part.shape[0],) + narrow_part.shape[1:]
    )


def local(fields, stresses, planes, active_masks):
    chan_dev, plane_count, cells_x, cells_z = fields.shape
    coarse_x = cells_x // 4
    coarse_z = cells_z // 4
    row_count = plane_count * coarse_x * coarse_z
    col_devices = lax.axis_size("cols")
    column_index = lax.axis_index("cols")
    term_dev = TERMS // col_devices
    offset = column_index * term_dev
    samples = float(row_count * lax.axis_size("slab") * lax.axis_size("rep"))
    height = 2.0 * (planes.astype(jnp.float32) + 0.5) / NY - 1.0
    root_weight = jnp.sqrt(1.2 - height * height)
    width = 5
    top, bottom = neighbour_edges(fields, "rep", 2, width)
    narrow_taps = kernel(1.5)
    broad_taps = kernel(3.0)
    guard = jnp.minimum(lax.axis_index("rep"), 0)
    span_table = filter_table(cells_z, narrow_taps, broad_taps, guard, (0, 1, 2))
    stream_table = filter_table(cells_x, narrow_taps, broad_taps, guard, (1, 0, 2))
    highest = lax.Precision.HIGHEST
    along_stream = (
        jnp.einsum(
            "cpxz,sxm->scpmz",
            fields.astype(jnp.float32),
            stream_table[:, width : width + cells_x],
            precision=highest,
        )
        + jnp.einsum(
            "cpxz,sxm->scpmz", top.astype(jnp.float32), stream_table[:, :width], precision=highest
        )
        + jnp.einsum(
            "cpxz,sxm->scpmz",
            bottom.astype(jnp.float32),
            stream_table[:, width + cells_x :],
            precision=highest,
        )
    )
    left, right = neighbour_edges(along_stream, "slab", 4, width)
    filtered = (
        jnp.einsum(
            "scpmz,zsn->scpmn",
            along_stream,
            span_table[width : width + cells_z],
            precision=highest,
        )
        + jnp.einsum("scpmz,zsn->scpmn", left, span_table[:width], precision=highest)
        + jnp.einsum("scpmz,zsn->scpmn", right, span_table[width + cells_z :], precision=highest)
    )
    narrow = filtered[0]
    broader = filtered[1]
    narrow_set = narrow.astype(jnp.bfloat16).reshape(chan_dev, row_count)
    broad_set = (
        (broader * root_weight[None, :, None, None])
        .astype(jnp.bfloat16)
        .reshape(chan_dev, row_count)
    )
    weighted = (stresses.astype(jnp.float32) * root_weight[None, :, None, None]).astype(
        jnp.bfloat16
    )
    weighted = weighted.reshape(STRESS, row_count)
    chunk = row_count // col_devices
    lanes = 128
    chunk_rows = chunk // lanes
    channels = chan_dev * col_devices
    sets = jnp.stack([narrow_set, broad_set]).reshape(2, chan_dev, col_devices, chunk_rows, lanes)
    sets = jnp.transpose(sets, (2, 0, 1, 3, 4)).reshape(col_devices, 2 * chan_dev * chunk_rows, lanes)
    sets = lax.all_to_all(sets, "cols", 0, 0, tiled=True)
    sets = sets.reshape(col_devices, 2, chan_dev, chunk_rows, lanes)
    sets = jnp.transpose(sets, (1, 0, 2, 3, 4)).reshape(2, channels, chunk_rows, lanes)
    narrow_all, broad_all = sets[0], sets[1]
    weighted = weighted.reshape(STRESS, col_devices, chunk_rows, lanes)
    weighted = lax.dynamic_index_in_dim(weighted, column_index, 1, keepdims=False)
    block_rows = chunk_rows
    block_count = chunk_rows // block_rows

    def gram_step(block_index, carry):
        gram_acc, rhs_acc = carry
        start = block_index * block_rows
        narrow_piece = lax.dynamic_slice_in_dim(narrow_all, start, block_rows, 1)
        broad_piece = lax.dynamic_slice_in_dim(broad_all, start, block_rows, 1)
        all_terms = library(narrow_piece, broad_piece)
        weighted_piece = lax.dynamic_slice_in_dim(weighted, start, block_rows, 1)
        gram_acc = gram_acc + jnp.einsum(
            "iqr,jqr->ij", all_terms, all_terms, preferred_element_type=jnp.float32
        )
        rhs_acc = rhs_acc + jnp.einsum(
            "iqr,kqr->ik", all_terms, weighted_piece, preferred_element_type=jnp.float32
        )
        return (gram_acc, rhs_acc)

    gram_part, rhs_part = lax.fori_loop(
        0,
        block_count,
        gram_step,
        (jnp.zeros((TERMS, TERMS), jnp.float32), jnp.zeros((TERMS, STRESS), jnp.float32)),
    )
    full_rows = split_sum(jnp.concatenate([gram_part, rhs_part], axis=1), "rep", ("slab", "cols"))
    gram_matrix = full_rows[:, :TERMS]
    rhs_sums = full_rows[:, TERMS:]
    column_scale = 1.0 / jnp.sqrt(jnp.diagonal(gram_matrix) / samples + epsilon)
    normal_gram = column_scale[:, None] * gram_matrix * column_scale[None, :] / samples
    target_norm = column_scale[None, :] * rhs_sums.T / samples

    padded_rows = -(-STRESS // 8) * 8
    target_padded = jnp.zeros((padded_rows, TERMS), jnp.float32).at[:STRESS].set(target_norm)
    masks_padded = (
        jnp.zeros((PASSES, padded_rows, TERMS), jnp.float32)
        .at[:, :STRESS]
        .set(active_masks.astype(jnp.float32))
    )
    passes = pl.pallas_call(
        conjugate_passes,
        out_shape=jax.ShapeDtypeStruct((PASSES, padded_rows, TERMS), jnp.float32),
    )(normal_gram, target_padded, masks_padded)
    coefficients = lax.dynamic_slice_in_dim(passes[:, :STRESS], offset, term_dev, 2)
    solution_all = passes[PASSES - 1, :STRESS]
    final_weights = (column_scale[None, :] * solution_all).astype(jnp.bfloat16)

    def misfit_step(block_index, misfit_acc):
        start = block_index * block_rows
        narrow_piece = lax.dynamic_slice_in_dim(narrow_all, start, block_rows, 1)
        broad_piece = lax.dynamic_slice_in_dim(broad_all, start, block_rows, 1)
        all_terms = library(narrow_piece, broad_piece)
        predicted = jnp.einsum(
            "ki,iqr->kqr", final_weights, all_terms, preferred_element_type=jnp.float32
        )
        weighted_piece = lax.dynamic_slice_in_dim(weighted, start, block_rows, 1)
        piece_misfit = (weighted_piece.astype(jnp.float32) - predicted).astype(jnp.bfloat16)
        return lax.dynamic_update_slice_in_dim(misfit_acc, piece_misfit, start, 1)

    misfit = lax.fori_loop(
        0, block_count, misfit_step, jnp.zeros((STRESS, chunk_rows, lanes), jnp.bfloat16)
    )
    misfit = lax.all_gather(misfit, "cols", axis=1, tiled=True)
    misfit = misfit.reshape(STRESS, plane_count, coarse_x, coarse_z)
    return (coefficients, misfit)


def solution(mesh):
    placed = (
        P("cols", "groups", "rep", "slab"),
        P(None, "groups", "rep", "slab"),
        P("groups"),
        P(),
    )
    return jax.shard_map(
        local,
        mesh=mesh,
        in_specs=placed,
        out_specs=(P(None, "groups", "cols"), P(None, "groups", "rep", "slab")),
        check_vma=False,
    )
```

```python
import math

import jax
import jax.numpy as jnp
import numpy as np
from jax import lax
from jax.experimental import pallas as pl
from jax.sharding import PartitionSpec as P

STRESS = 6
TERMS = 256
NY = 2048
PASSES = 3
ITERS = 3


ridge_weight = 0.05
epsilon = 1e-06


def extended(array, sides, width):
    for axis, dim in sides:
        count, length = (lax.axis_size(axis), array.shape[dim])
        up = [(i, (i + 1) % count) for i in range(count)]
        down = [(j, i) for i, j in up]
        last = lax.slice_in_dim(array, length - width, length, axis=dim)
        leading = lax.slice_in_dim(array, 0, width, axis=dim)
        before = lax.ppermute(last, axis, up)
        after = lax.ppermute(leading, axis, down)
        array = jnp.concatenate([before, array, after], axis=dim)
    return array


def tree_sum(value, axes):
    for axis in axes:
        count = lax.axis_size(axis)
        if count & (count - 1):
            value = lax.psum(value, axis)
            continue
        step = 1
        while step < count:
            partner = [(i, i ^ step) for i in range(count)]
            value = value + lax.ppermute(value, axis, partner)
            step *= 2
    return value


def split_sum(value, lead, axes):
    count = lax.axis_size(lead)
    if count != 2 or value.shape[0] % 2:
        return tree_sum(value, (lead,) + axes)
    swap = [(0, 1), (1, 0)]
    value = value + lax.ppermute(value, lead, swap)
    half = value.shape[0] // 2
    first = lax.axis_index(lead) == 0
    mine = jnp.where(first, value[:half], value[half:])
    mine = tree_sum(mine, axes)
    other = lax.ppermute(mine, lead, swap)
    return jnp.where(first, jnp.concatenate([mine, other]), jnp.concatenate([other, mine]))


def neighbour_edges(array, axis, dim, width):
    count, length = (lax.axis_size(axis), array.shape[dim])
    up = [(i, (i + 1) % count) for i in range(count)]
    down = [(j, i) for i, j in up]
    last = lax.slice_in_dim(array, length - width, length, axis=dim)
    leading = lax.slice_in_dim(array, 0, width, axis=dim)
    return (lax.ppermute(last, axis, up), lax.ppermute(leading, axis, down))


def conjugate_passes(gram_ref, target_ref, mask_ref, out_ref):
    gram = gram_ref[...]
    target = target_ref[...]
    gram_high = gram.astype(jnp.bfloat16)
    gram_low = (gram - gram_high.astype(jnp.float32)).astype(jnp.bfloat16)

    def product_with(left, right):
        return lax.dot_general(
            left, right, (((1,), (1,)), ((), ())), preferred_element_type=jnp.float32
        )

    def apply_normal(vector, active):
        masked = active * vector
        masked_high = masked.astype(jnp.bfloat16)
        masked_low = (masked - masked_high.astype(jnp.float32)).astype(jnp.bfloat16)
        product = (
            product_with(masked_high, gram_high)
            + product_with(masked_low, gram_high)
            + product_with(masked_high, gram_low)
        )
        return active * product + ridge_weight * vector

    solution_all = jnp.zeros(target.shape, jnp.float32)
    for pass_index in range(PASSES):
        active = mask_ref[pass_index]
        solution_all = active * solution_all
        remain = active * target - apply_normal(solution_all, active)
        direction = remain
        norm_now = jnp.sum(remain * remain, axis=1, keepdims=True)
        for turn_index in range(ITERS):
            applied = apply_normal(direction, active)
            curve_sum = jnp.sum(direction * applied, axis=1, keepdims=True)
            step_size = norm_now / (curve_sum + epsilon)
            solution_all = solution_all + step_size * direction
            remain = remain - step_size * applied
            norm_next = jnp.sum(remain * remain, axis=1, keepdims=True)
            direction = remain + (norm_next / (norm_now + epsilon)) * direction
            norm_now = norm_next
        out_ref[pass_index] = solution_all


def kernel(spread):
    offsets = np.arange(13) - 6.0
    values = np.exp(-offsets * offsets / (2.0 * spread * spread))
    return values / values.sum()


def filter_table(cells, first_taps, second_taps, guard, order):
    out_count = cells // 4
    shape = tuple((cells + 10, 2, out_count)[d] for d in order)
    where = {d: order.index(d) for d in range(3)}
    position = lax.broadcasted_iota(jnp.int32, shape, where[0])
    which = lax.broadcasted_iota(jnp.int32, shape, where[1])
    out_index = lax.broadcasted_iota(jnp.int32, shape, where[2])
    tap_at = position - 1 - 4 * out_index + guard
    table = jnp.zeros(shape, jnp.float32)
    for tap_index in range(13):
        value = jnp.where(
            which == 0, np.float32(first_taps[tap_index]), np.float32(second_taps[tap_index])
        )
        table = jnp.where(tap_at == tap_index, value, table)
    return table


def library(narrow_part, broad_part):
    product = (
        narrow_part.astype(jnp.float32)[:, None] * broad_part.astype(jnp.float32)[None, :]
    )
    return product.astype(jnp.bfloat16).reshape(
        (narrow_part.shape[0] * broad_part.shape[0],) + narrow_part.shape[1:]
    )


def local(fields, stresses, planes, active_masks):
    chan_dev, plane_count, cells_x, cells_z = fields.shape
    coarse_x = cells_x // 4
    coarse_z = cells_z // 4
    row_count = plane_count * coarse_x * coarse_z
    col_devices = lax.axis_size("cols")
    column_index = lax.axis_index("cols")
    term_dev = TERMS // col_devices
    offset = column_index * term_dev
    samples = float(row_count * lax.axis_size("slab") * lax.axis_size("rep"))
    height = 2.0 * (planes.astype(jnp.float32) + 0.5) / NY - 1.0
    root_weight = jnp.sqrt(1.2 - height * height)
    width = 5
    top, bottom = neighbour_edges(fields, "rep", 2, width)
    narrow_taps = kernel(1.5)
    broad_taps = kernel(3.0)
    guard = jnp.minimum(lax.axis_index("rep"), 0)
    span_table = filter_table(cells_z, narrow_taps, broad_taps, guard, (0, 1, 2))
    stream_table = filter_table(cells_x, narrow_taps, broad_taps, guard, (1, 0, 2))
    highest = lax.Precision.HIGHEST
    along_stream = (
        jnp.einsum(
            "cpxz,sxm->scpmz",
            fields.astype(jnp.float32),
            stream_table[:, width : width + cells_x],
            precision=highest,
        )
        + jnp.einsum(
            "cpxz,sxm->scpmz", top.astype(jnp.float32), stream_table[:, :width], precision=highest
        )
        + jnp.einsum(
            "cpxz,sxm->scpmz",
            bottom.astype(jnp.float32),
            stream_table[:, width + cells_x :],
            precision=highest,
        )
    )
    left, right = neighbour_edges(along_stream, "slab", 4, width)
    filtered = (
        jnp.einsum(
            "scpmz,zsn->scpmn",
            along_stream,
            span_table[width : width + cells_z],
            precision=highest,
        )
        + jnp.einsum("scpmz,zsn->scpmn", left, span_table[:width], precision=highest)
        + jnp.einsum("scpmz,zsn->scpmn", right, span_table[width + cells_z :], precision=highest)
    )
    narrow = filtered[0]
    broader = filtered[1]
    narrow_set = narrow.astype(jnp.bfloat16).reshape(chan_dev, row_count)
    broad_set = (
        (broader * root_weight[None, :, None, None])
        .astype(jnp.bfloat16)
        .reshape(chan_dev, row_count)
    )
    weighted = (stresses.astype(jnp.float32) * root_weight[None, :, None, None]).astype(
        jnp.bfloat16
    )
    weighted = weighted.reshape(STRESS, row_count)
    chunk = row_count // col_devices
    lanes = 128
    chunk_rows = chunk // lanes
    channels = chan_dev * col_devices
    sets = jnp.stack([narrow_set, broad_set]).reshape(2, chan_dev, col_devices, chunk_rows, lanes)
    sets = jnp.transpose(sets, (2, 0, 1, 3, 4)).reshape(col_devices, 2 * chan_dev * chunk_rows, lanes)
    sets = lax.all_to_all(sets, "cols", 0, 0, tiled=True)
    sets = sets.reshape(col_devices, 2, chan_dev, chunk_rows, lanes)
    sets = jnp.transpose(sets, (1, 0, 2, 3, 4)).reshape(2, channels, chunk_rows, lanes)
    narrow_all, broad_all = sets[0], sets[1]
    weighted = weighted.reshape(STRESS, col_devices, chunk_rows, lanes)
    weighted = lax.dynamic_index_in_dim(weighted, column_index, 1, keepdims=False)
    block_rows = chunk_rows
    block_count = chunk_rows // block_rows

    def gram_step(block_index, carry):
        gram_acc, rhs_acc = carry
        start = block_index * block_rows
        narrow_piece = lax.dynamic_slice_in_dim(narrow_all, start, block_rows, 1)
        broad_piece = lax.dynamic_slice_in_dim(broad_all, start, block_rows, 1)
        all_terms = library(narrow_piece, broad_piece)
        weighted_piece = lax.dynamic_slice_in_dim(weighted, start, block_rows, 1)
        gram_acc = gram_acc + jnp.einsum(
            "iqr,jqr->ij", all_terms, all_terms, preferred_element_type=jnp.float32
        )
        rhs_acc = rhs_acc + jnp.einsum(
            "iqr,kqr->ik", all_terms, weighted_piece, preferred_element_type=jnp.float32
        )
        return (gram_acc, rhs_acc)

    gram_part, rhs_part = lax.fori_loop(
        0,
        block_count,
        gram_step,
        (jnp.zeros((TERMS, TERMS), jnp.float32), jnp.zeros((TERMS, STRESS), jnp.float32)),
    )
    full_rows = split_sum(jnp.concatenate([gram_part, rhs_part], axis=1), "rep", ("slab", "cols"))
    gram_matrix = full_rows[:, :TERMS]
    rhs_sums = full_rows[:, TERMS:]
    column_scale = 1.0 / jnp.sqrt(jnp.diagonal(gram_matrix) / samples + epsilon)
    normal_gram = column_scale[:, None] * gram_matrix * column_scale[None, :] / samples
    target_norm = column_scale[None, :] * rhs_sums.T / samples

    padded_rows = -(-STRESS // 8) * 8
    target_padded = jnp.zeros((padded_rows, TERMS), jnp.float32).at[:STRESS].set(target_norm)
    masks_padded = (
        jnp.zeros((PASSES, padded_rows, TERMS), jnp.float32)
        .at[:, :STRESS]
        .set(active_masks.astype(jnp.float32))
    )
    passes = pl.pallas_call(
        conjugate_passes,
        out_shape=jax.ShapeDtypeStruct((PASSES, padded_rows, TERMS), jnp.float32),
    )(normal_gram, target_padded, masks_padded)
    coefficients = lax.dynamic_slice_in_dim(passes[:, :STRESS], offset, term_dev, 2)
    solution_all = passes[PASSES - 1, :STRESS]
    final_weights = (column_scale[None, :] * solution_all).astype(jnp.bfloat16)

    def misfit_step(block_index, misfit_acc):
        start = block_index * block_rows
        narrow_piece = lax.dynamic_slice_in_dim(narrow_all, start, block_rows, 1)
        broad_piece = lax.dynamic_slice_in_dim(broad_all, start, block_rows, 1)
        all_terms = library(narrow_piece, broad_piece)
        predicted = jnp.einsum(
            "ki,iqr->kqr", final_weights, all_terms, preferred_element_type=jnp.float32
        )
        weighted_piece = lax.dynamic_slice_in_dim(weighted, start, block_rows, 1)
        piece_misfit = (weighted_piece.astype(jnp.float32) - predicted).astype(jnp.bfloat16)
        return lax.dynamic_update_slice_in_dim(misfit_acc, piece_misfit, start, 1)

    misfit = lax.fori_loop(
        0, block_count, misfit_step, jnp.zeros((STRESS, chunk_rows, lanes), jnp.bfloat16)
    )
    misfit = lax.all_gather(misfit, "cols", axis=1, tiled=True)
    misfit = misfit.reshape(STRESS, plane_count, coarse_x, coarse_z)
    return (coefficients, misfit)


def solution(mesh):
    placed = (
        P("cols", "groups", "rep", "slab"),
        P(None, "groups", "rep", "slab"),
        P("groups"),
        P(),
    )
    return jax.shard_map(
        local,
        mesh=mesh,
        in_specs=placed,
        out_specs=(P(None, "groups", "cols"), P(None, "groups", "rep", "slab")),
        check_vma=False,
    )
```

```python
import math

import jax
import jax.numpy as jnp
import numpy as np
from jax import lax
from jax.experimental import pallas as pl
from jax.sharding import PartitionSpec as P

STRESS = 6
TERMS = 256
NY = 2048
PASSES = 3
ITERS = 3


ridge_weight = 0.05
epsilon = 1e-06


def extended(array, sides, width):
    for axis, dim in sides:
        count, length = (lax.axis_size(axis), array.shape[dim])
        up = [(i, (i + 1) % count) for i in range(count)]
        down = [(j, i) for i, j in up]
        last = lax.slice_in_dim(array, length - width, length, axis=dim)
        leading = lax.slice_in_dim(array, 0, width, axis=dim)
        before = lax.ppermute(last, axis, up)
        after = lax.ppermute(leading, axis, down)
        array = jnp.concatenate([before, array, after], axis=dim)
    return array


def tree_sum(value, axes):
    for axis in axes:
        count = lax.axis_size(axis)
        if count & (count - 1):
            value = lax.psum(value, axis)
            continue
        step = 1
        while step < count:
            partner = [(i, i ^ step) for i in range(count)]
            value = value + lax.ppermute(value, axis, partner)
            step *= 2
    return value


def split_sum(value, lead, axes):
    count = lax.axis_size(lead)
    if count != 2 or value.shape[0] % 2:
        return tree_sum(value, (lead,) + axes)
    swap = [(0, 1), (1, 0)]
    value = value + lax.ppermute(value, lead, swap)
    half = value.shape[0] // 2
    first = lax.axis_index(lead) == 0
    mine = jnp.where(first, value[:half], value[half:])
    mine = tree_sum(mine, axes)
    other = lax.ppermute(mine, lead, swap)
    return jnp.where(first, jnp.concatenate([mine, other]), jnp.concatenate([other, mine]))


def neighbour_edges(array, axis, dim, width):
    count, length = (lax.axis_size(axis), array.shape[dim])
    up = [(i, (i + 1) % count) for i in range(count)]
    down = [(j, i) for i, j in up]
    last = lax.slice_in_dim(array, length - width, length, axis=dim)
    leading = lax.slice_in_dim(array, 0, width, axis=dim)
    return (lax.ppermute(last, axis, up), lax.ppermute(leading, axis, down))


def conjugate_passes(gram_ref, target_ref, mask_ref, out_ref):
    gram = gram_ref[...]
    target = target_ref[...]
    gram_high = gram.astype(jnp.bfloat16)
    gram_low = (gram - gram_high.astype(jnp.float32)).astype(jnp.bfloat16)

    def product_with(left, right):
        return lax.dot_general(
            left, right, (((1,), (1,)), ((), ())), preferred_element_type=jnp.float32
        )

    def apply_normal(vector, active):
        masked = active * vector
        masked_high = masked.astype(jnp.bfloat16)
        masked_low = (masked - masked_high.astype(jnp.float32)).astype(jnp.bfloat16)
        product = (
            product_with(masked_high, gram_high)
            + product_with(masked_low, gram_high)
            + product_with(masked_high, gram_low)
        )
        return active * product + ridge_weight * vector

    solution_all = jnp.zeros(target.shape, jnp.float32)
    for pass_index in range(PASSES):
        active = mask_ref[pass_index]
        solution_all = active * solution_all
        remain = active * target - apply_normal(solution_all, active)
        direction = remain
        norm_now = jnp.sum(remain * remain, axis=1, keepdims=True)
        for turn_index in range(ITERS):
            applied = apply_normal(direction, active)
            curve_sum = jnp.sum(direction * applied, axis=1, keepdims=True)
            step_size = norm_now / (curve_sum + epsilon)
            solution_all = solution_all + step_size * direction
            remain = remain - step_size * applied
            norm_next = jnp.sum(remain * remain, axis=1, keepdims=True)
            direction = remain + (norm_next / (norm_now + epsilon)) * direction
            norm_now = norm_next
        out_ref[pass_index] = solution_all


def kernel(spread):
    offsets = np.arange(13) - 6.0
    values = np.exp(-offsets * offsets / (2.0 * spread * spread))
    return values / values.sum()


def filter_table(cells, first_taps, second_taps, guard, order):
    out_count = cells // 4
    shape = tuple((cells + 10, 2, out_count)[d] for d in order)
    where = {d: order.index(d) for d in range(3)}
    position = lax.broadcasted_iota(jnp.int32, shape, where[0])
    which = lax.broadcasted_iota(jnp.int32, shape, where[1])
    out_index = lax.broadcasted_iota(jnp.int32, shape, where[2])
    tap_at = position - 1 - 4 * out_index + guard
    table = jnp.zeros(shape, jnp.float32)
    for tap_index in range(13):
        value = jnp.where(
            which == 0, np.float32(first_taps[tap_index]), np.float32(second_taps[tap_index])
        )
        table = jnp.where(tap_at == tap_index, value, table)
    return table


def library(narrow_part, broad_part):
    product = (
        narrow_part.astype(jnp.float32)[:, None] * broad_part.astype(jnp.float32)[None, :]
    )
    return product.astype(jnp.bfloat16).reshape(
        (narrow_part.shape[0] * broad_part.shape[0],) + narrow_part.shape[1:]
    )


def local(fields, stresses, planes, active_masks):
    chan_dev, plane_count, cells_x, cells_z = fields.shape
    coarse_x = cells_x // 4
    coarse_z = cells_z // 4
    row_count = plane_count * coarse_x * coarse_z
    col_devices = lax.axis_size("cols")
    column_index = lax.axis_index("cols")
    term_dev = TERMS // col_devices
    offset = column_index * term_dev
    samples = float(row_count * lax.axis_size("slab") * lax.axis_size("rep"))
    height = 2.0 * (planes.astype(jnp.float32) + 0.5) / NY - 1.0
    root_weight = jnp.sqrt(1.2 - height * height)
    width = 5
    top, bottom = neighbour_edges(fields, "rep", 2, width)
    narrow_taps = kernel(1.5)
    broad_taps = kernel(3.0)
    guard = jnp.minimum(lax.axis_index("rep"), 0)
    span_table = filter_table(cells_z, narrow_taps, broad_taps, guard, (0, 1, 2))
    stream_table = filter_table(cells_x, narrow_taps, broad_taps, guard, (1, 0, 2))
    highest = lax.Precision.HIGHEST
    along_stream = (
        jnp.einsum(
            "cpxz,sxm->scpmz",
            fields.astype(jnp.float32),
            stream_table[:, width : width + cells_x],
            precision=highest,
        )
        + jnp.einsum(
            "cpxz,sxm->scpmz", top.astype(jnp.float32), stream_table[:, :width], precision=highest
        )
        + jnp.einsum(
            "cpxz,sxm->scpmz",
            bottom.astype(jnp.float32),
            stream_table[:, width + cells_x :],
            precision=highest,
        )
    )
    left, right = neighbour_edges(jnp.swapaxes(along_stream, 3, 4), "slab", 3, width)
    filtered = (
        jnp.einsum(
            "scpmz,zsn->scpmn",
            along_stream,
            span_table[width : width + cells_z],
            precision=highest,
        )
        + jnp.einsum("scpzm,zsn->scpmn", left, span_table[:width], precision=highest)
        + jnp.einsum("scpzm,zsn->scpmn", right, span_table[width + cells_z :], precision=highest)
    )
    narrow = filtered[0]
    broader = filtered[1]
    narrow_set = narrow.astype(jnp.bfloat16).reshape(chan_dev, row_count)
    broad_set = (
        (broader * root_weight[None, :, None, None])
        .astype(jnp.bfloat16)
        .reshape(chan_dev, row_count)
    )
    weighted = (stresses.astype(jnp.float32) * root_weight[None, :, None, None]).astype(
        jnp.bfloat16
    )
    weighted = weighted.reshape(STRESS, row_count)
    chunk = row_count // col_devices
    lanes = 128
    chunk_rows = chunk // lanes
    channels = chan_dev * col_devices
    sets = jnp.stack([narrow_set, broad_set]).reshape(2, chan_dev, col_devices, chunk_rows, lanes)
    sets = jnp.transpose(sets, (2, 0, 1, 3, 4)).reshape(col_devices, 2 * chan_dev * chunk_rows, lanes)
    sets = lax.all_to_all(sets, "cols", 0, 0, tiled=True)
    sets = sets.reshape(col_devices, 2, chan_dev, chunk_rows, lanes)
    sets = jnp.transpose(sets, (1, 0, 2, 3, 4)).reshape(2, channels, chunk_rows, lanes)
    narrow_all, broad_all = sets[0], sets[1]
    weighted = weighted.reshape(STRESS, col_devices, chunk_rows, lanes)
    weighted = lax.dynamic_index_in_dim(weighted, column_index, 1, keepdims=False)
    block_rows = chunk_rows
    block_count = chunk_rows // block_rows

    def gram_step(block_index, carry):
        gram_acc, rhs_acc = carry
        start = block_index * block_rows
        narrow_piece = lax.dynamic_slice_in_dim(narrow_all, start, block_rows, 1)
        broad_piece = lax.dynamic_slice_in_dim(broad_all, start, block_rows, 1)
        all_terms = library(narrow_piece, broad_piece)
        weighted_piece = lax.dynamic_slice_in_dim(weighted, start, block_rows, 1)
        gram_acc = gram_acc + jnp.einsum(
            "iqr,jqr->ij", all_terms, all_terms, preferred_element_type=jnp.float32
        )
        rhs_acc = rhs_acc + jnp.einsum(
            "iqr,kqr->ik", all_terms, weighted_piece, preferred_element_type=jnp.float32
        )
        return (gram_acc, rhs_acc)

    gram_part, rhs_part = lax.fori_loop(
        0,
        block_count,
        gram_step,
        (jnp.zeros((TERMS, TERMS), jnp.float32), jnp.zeros((TERMS, STRESS), jnp.float32)),
    )
    full_rows = split_sum(jnp.concatenate([gram_part, rhs_part], axis=1), "rep", ("slab", "cols"))
    gram_matrix = full_rows[:, :TERMS]
    rhs_sums = full_rows[:, TERMS:]
    on_diagonal = lax.broadcasted_iota(jnp.int32, (TERMS, TERMS), 0) == lax.broadcasted_iota(
        jnp.int32, (TERMS, TERMS), 1
    )
    diagonal = jnp.sum(jnp.where(on_diagonal, gram_matrix, 0.0), axis=1)
    column_scale = 1.0 / jnp.sqrt(diagonal / samples + epsilon)
    normal_gram = column_scale[:, None] * gram_matrix * column_scale[None, :] / samples
    target_norm = column_scale[None, :] * rhs_sums.T / samples

    padded_rows = -(-STRESS // 8) * 8
    target_padded = jnp.zeros((padded_rows, TERMS), jnp.float32).at[:STRESS].set(target_norm)
    masks_padded = (
        jnp.zeros((PASSES, padded_rows, TERMS), jnp.float32)
        .at[:, :STRESS]
        .set(active_masks.astype(jnp.float32))
    )
    passes = pl.pallas_call(
        conjugate_passes,
        out_shape=jax.ShapeDtypeStruct((PASSES, padded_rows, TERMS), jnp.float32),
    )(normal_gram, target_padded, masks_padded)
    coefficients = lax.dynamic_slice_in_dim(passes[:, :STRESS], offset, term_dev, 2)
    solution_all = passes[PASSES - 1, :STRESS]
    final_weights = (column_scale[None, :] * solution_all).astype(jnp.bfloat16)

    def misfit_step(block_index, misfit_acc):
        start = block_index * block_rows
        narrow_piece = lax.dynamic_slice_in_dim(narrow_all, start, block_rows, 1)
        broad_piece = lax.dynamic_slice_in_dim(broad_all, start, block_rows, 1)
        all_terms = library(narrow_piece, broad_piece)
        predicted = jnp.einsum(
            "ki,iqr->kqr", final_weights, all_terms, preferred_element_type=jnp.float32
        )
        weighted_piece = lax.dynamic_slice_in_dim(weighted, start, block_rows, 1)
        piece_misfit = (weighted_piece.astype(jnp.float32) - predicted).astype(jnp.bfloat16)
        return lax.dynamic_update_slice_in_dim(misfit_acc, piece_misfit, start, 1)

    misfit = lax.fori_loop(
        0, block_count, misfit_step, jnp.zeros((STRESS, chunk_rows, lanes), jnp.bfloat16)
    )
    misfit = lax.all_gather(misfit, "cols", axis=1, tiled=True)
    misfit = misfit.reshape(STRESS, plane_count, coarse_x, coarse_z)
    return (coefficients, misfit)


def solution(mesh):
    placed = (
        P("cols", "groups", "rep", "slab"),
        P(None, "groups", "rep", "slab"),
        P("groups"),
        P(),
    )
    return jax.shard_map(
        local,
        mesh=mesh,
        in_specs=placed,
        out_specs=(P(None, "groups", "cols"), P(None, "groups", "rep", "slab")),
        check_vma=False,
    )
```

```python
import math

import jax
import jax.numpy as jnp
import numpy as np
from jax import lax
from jax.experimental import pallas as pl
from jax.sharding import PartitionSpec as P

STRESS = 6
TERMS = 256
NY = 2048
PASSES = 3
ITERS = 3


ridge_weight = 0.05
epsilon = 1e-06


def extended(array, sides, width):
    for axis, dim in sides:
        count, length = (lax.axis_size(axis), array.shape[dim])
        up = [(i, (i + 1) % count) for i in range(count)]
        down = [(j, i) for i, j in up]
        last = lax.slice_in_dim(array, length - width, length, axis=dim)
        leading = lax.slice_in_dim(array, 0, width, axis=dim)
        before = lax.ppermute(last, axis, up)
        after = lax.ppermute(leading, axis, down)
        array = jnp.concatenate([before, array, after], axis=dim)
    return array


def tree_sum(value, axes):
    for axis in axes:
        count = lax.axis_size(axis)
        if count & (count - 1):
            value = lax.psum(value, axis)
            continue
        step = 1
        while step < count:
            partner = [(i, i ^ step) for i in range(count)]
            value = value + lax.ppermute(value, axis, partner)
            step *= 2
    return value


def split_sum(value, lead, axes):
    count = lax.axis_size(lead)
    if count != 2 or value.shape[0] % 2:
        return tree_sum(value, (lead,) + axes)
    swap = [(0, 1), (1, 0)]
    value = value + lax.ppermute(value, lead, swap)
    half = value.shape[0] // 2
    first = lax.axis_index(lead) == 0
    mine = jnp.where(first, value[:half], value[half:])
    mine = tree_sum(mine, axes)
    other = lax.ppermute(mine, lead, swap)
    return jnp.where(first, jnp.concatenate([mine, other]), jnp.concatenate([other, mine]))


def neighbour_edges(array, axis, dim, width):
    count, length = (lax.axis_size(axis), array.shape[dim])
    up = [(i, (i + 1) % count) for i in range(count)]
    down = [(j, i) for i, j in up]
    last = lax.slice_in_dim(array, length - width, length, axis=dim)
    leading = lax.slice_in_dim(array, 0, width, axis=dim)
    return (lax.ppermute(last, axis, up), lax.ppermute(leading, axis, down))


def conjugate_passes(gram_ref, target_ref, mask_ref, out_ref):
    gram = gram_ref[...]
    target = target_ref[...]
    gram_high = gram.astype(jnp.bfloat16)
    gram_low = (gram - gram_high.astype(jnp.float32)).astype(jnp.bfloat16)

    def product_with(left, right):
        return lax.dot_general(
            left, right, (((1,), (1,)), ((), ())), preferred_element_type=jnp.float32
        )

    def apply_normal(vector, active):
        masked = active * vector
        masked_high = masked.astype(jnp.bfloat16)
        masked_low = (masked - masked_high.astype(jnp.float32)).astype(jnp.bfloat16)
        product = (
            product_with(masked_high, gram_high)
            + product_with(masked_low, gram_high)
            + product_with(masked_high, gram_low)
        )
        return active * product + ridge_weight * vector

    solution_all = jnp.zeros(target.shape, jnp.float32)
    for pass_index in range(PASSES):
        active = mask_ref[pass_index]
        solution_all = active * solution_all
        remain = active * target - apply_normal(solution_all, active)
        direction = remain
        norm_now = jnp.sum(remain * remain, axis=1, keepdims=True)
        for turn_index in range(ITERS):
            applied = apply_normal(direction, active)
            curve_sum = jnp.sum(direction * applied, axis=1, keepdims=True)
            step_size = norm_now / (curve_sum + epsilon)
            solution_all = solution_all + step_size * direction
            remain = remain - step_size * applied
            norm_next = jnp.sum(remain * remain, axis=1, keepdims=True)
            direction = remain + (norm_next / (norm_now + epsilon)) * direction
            norm_now = norm_next
        out_ref[pass_index] = solution_all


def halving_sum(value, scatter_axes, rest_axes):
    if not scatter_axes:
        return tree_sum(value, rest_axes)
    axis = scatter_axes[0]
    if lax.axis_size(axis) != 2 or value.shape[0] % 16:
        return tree_sum(value, scatter_axes + rest_axes)
    swap = [(0, 1), (1, 0)]
    first = lax.axis_index(axis) == 0
    half = value.shape[0] // 2
    keep = jnp.where(first, value[:half], value[half:])
    give = jnp.where(first, value[half:], value[:half])
    keep = keep + lax.ppermute(give, axis, swap)
    keep = halving_sum(keep, scatter_axes[1:], rest_axes)
    other = lax.ppermute(keep, axis, swap)
    return jnp.where(first, jnp.concatenate([keep, other]), jnp.concatenate([other, keep]))


def kernel(spread):
    offsets = np.arange(13) - 6.0
    values = np.exp(-offsets * offsets / (2.0 * spread * spread))
    return values / values.sum()


def filter_table(cells, first_taps, second_taps, guard, order):
    out_count = cells // 4
    shape = tuple((cells + 10, 2, out_count)[d] for d in order)
    where = {d: order.index(d) for d in range(3)}
    position = lax.broadcasted_iota(jnp.int32, shape, where[0])
    which = lax.broadcasted_iota(jnp.int32, shape, where[1])
    out_index = lax.broadcasted_iota(jnp.int32, shape, where[2])
    tap_at = position - 1 - 4 * out_index + guard
    table = jnp.zeros(shape, jnp.float32)
    for tap_index in range(13):
        value = jnp.where(
            which == 0, np.float32(first_taps[tap_index]), np.float32(second_taps[tap_index])
        )
        table = jnp.where(tap_at == tap_index, value, table)
    return table


def library(narrow_part, broad_part):
    product = (
        narrow_part.astype(jnp.float32)[:, None] * broad_part.astype(jnp.float32)[None, :]
    )
    return product.astype(jnp.bfloat16).reshape(
        (narrow_part.shape[0] * broad_part.shape[0],) + narrow_part.shape[1:]
    )


def local(fields, stresses, planes, active_masks):
    chan_dev, plane_count, cells_x, cells_z = fields.shape
    coarse_x = cells_x // 4
    coarse_z = cells_z // 4
    row_count = plane_count * coarse_x * coarse_z
    col_devices = lax.axis_size("cols")
    column_index = lax.axis_index("cols")
    term_dev = TERMS // col_devices
    offset = column_index * term_dev
    samples = float(row_count * lax.axis_size("slab") * lax.axis_size("rep"))
    height = 2.0 * (planes.astype(jnp.float32) + 0.5) / NY - 1.0
    root_weight = jnp.sqrt(1.2 - height * height)
    width = 5
    top, bottom = neighbour_edges(fields, "rep", 2, width)
    narrow_taps = kernel(1.5)
    broad_taps = kernel(3.0)
    guard = jnp.minimum(lax.axis_index("rep"), 0)
    span_table = filter_table(cells_z, narrow_taps, broad_taps, guard, (0, 1, 2))
    stream_table = filter_table(cells_x, narrow_taps, broad_taps, guard, (1, 0, 2))
    highest = lax.Precision.HIGHEST
    along_stream = (
        jnp.einsum(
            "cpxz,sxm->scpmz",
            fields.astype(jnp.float32),
            stream_table[:, width : width + cells_x],
            precision=highest,
        )
        + jnp.einsum(
            "cpxz,sxm->scpmz", top.astype(jnp.float32), stream_table[:, :width], precision=highest
        )
        + jnp.einsum(
            "cpxz,sxm->scpmz",
            bottom.astype(jnp.float32),
            stream_table[:, width + cells_x :],
            precision=highest,
        )
    )
    left, right = neighbour_edges(jnp.swapaxes(along_stream, 3, 4), "slab", 3, width)
    filtered = (
        jnp.einsum(
            "scpmz,zsn->scpmn",
            along_stream,
            span_table[width : width + cells_z],
            precision=highest,
        )
        + jnp.einsum("scpzm,zsn->scpmn", left, span_table[:width], precision=highest)
        + jnp.einsum("scpzm,zsn->scpmn", right, span_table[width + cells_z :], precision=highest)
    )
    narrow = filtered[0]
    broader = filtered[1]
    narrow_set = narrow.astype(jnp.bfloat16).reshape(chan_dev, row_count)
    broad_set = (
        (broader * root_weight[None, :, None, None])
        .astype(jnp.bfloat16)
        .reshape(chan_dev, row_count)
    )
    weighted = (stresses.astype(jnp.float32) * root_weight[None, :, None, None]).astype(
        jnp.bfloat16
    )
    weighted = weighted.reshape(STRESS, row_count)
    chunk = row_count // col_devices
    lanes = 128
    chunk_rows = chunk // lanes
    channels = chan_dev * col_devices
    sets = jnp.stack([narrow_set, broad_set]).reshape(2, chan_dev, col_devices, chunk_rows, lanes)
    sets = jnp.transpose(sets, (2, 0, 1, 3, 4)).reshape(col_devices, 2 * chan_dev * chunk_rows, lanes)
    sets = lax.all_to_all(sets, "cols", 0, 0, tiled=True)
    sets = sets.reshape(col_devices, 2, chan_dev, chunk_rows, lanes)
    sets = jnp.transpose(sets, (1, 0, 2, 3, 4)).reshape(2, channels, chunk_rows, lanes)
    narrow_all, broad_all = sets[0], sets[1]
    weighted = weighted.reshape(STRESS, col_devices, chunk_rows, lanes)
    weighted = lax.dynamic_index_in_dim(weighted, column_index, 1, keepdims=False)
    block_rows = chunk_rows
    block_count = chunk_rows // block_rows

    def gram_step(block_index, carry):
        gram_acc, rhs_acc = carry
        start = block_index * block_rows
        narrow_piece = lax.dynamic_slice_in_dim(narrow_all, start, block_rows, 1)
        broad_piece = lax.dynamic_slice_in_dim(broad_all, start, block_rows, 1)
        all_terms = library(narrow_piece, broad_piece)
        weighted_piece = lax.dynamic_slice_in_dim(weighted, start, block_rows, 1)
        gram_acc = gram_acc + jnp.einsum(
            "iqr,jqr->ij", all_terms, all_terms, preferred_element_type=jnp.float32
        )
        rhs_acc = rhs_acc + jnp.einsum(
            "iqr,kqr->ik", all_terms, weighted_piece, preferred_element_type=jnp.float32
        )
        return (gram_acc, rhs_acc)

    gram_part, rhs_part = lax.fori_loop(
        0,
        block_count,
        gram_step,
        (jnp.zeros((TERMS, TERMS), jnp.float32), jnp.zeros((TERMS, STRESS), jnp.float32)),
    )
    full_rows = halving_sum(
        jnp.concatenate([gram_part, rhs_part], axis=1), ("rep", "slab"), ("cols",)
    )
    gram_matrix = full_rows[:, :TERMS]
    rhs_sums = full_rows[:, TERMS:]
    on_diagonal = lax.broadcasted_iota(jnp.int32, (TERMS, TERMS), 0) == lax.broadcasted_iota(
        jnp.int32, (TERMS, TERMS), 1
    )
    diagonal = jnp.sum(jnp.where(on_diagonal, gram_matrix, 0.0), axis=1)
    column_scale = 1.0 / jnp.sqrt(diagonal / samples + epsilon)
    normal_gram = column_scale[:, None] * gram_matrix * column_scale[None, :] / samples
    target_norm = column_scale[None, :] * rhs_sums.T / samples

    padded_rows = -(-STRESS // 8) * 8
    target_padded = jnp.zeros((padded_rows, TERMS), jnp.float32).at[:STRESS].set(target_norm)
    masks_padded = (
        jnp.zeros((PASSES, padded_rows, TERMS), jnp.float32)
        .at[:, :STRESS]
        .set(active_masks.astype(jnp.float32))
    )
    passes = pl.pallas_call(
        conjugate_passes,
        out_shape=jax.ShapeDtypeStruct((PASSES, padded_rows, TERMS), jnp.float32),
    )(normal_gram, target_padded, masks_padded)
    coefficients = lax.dynamic_slice_in_dim(passes[:, :STRESS], offset, term_dev, 2)
    solution_all = passes[PASSES - 1, :STRESS]
    final_weights = (column_scale[None, :] * solution_all).astype(jnp.bfloat16)

    def misfit_step(block_index, misfit_acc):
        start = block_index * block_rows
        narrow_piece = lax.dynamic_slice_in_dim(narrow_all, start, block_rows, 1)
        broad_piece = lax.dynamic_slice_in_dim(broad_all, start, block_rows, 1)
        all_terms = library(narrow_piece, broad_piece)
        predicted = jnp.einsum(
            "ki,iqr->kqr", final_weights, all_terms, preferred_element_type=jnp.float32
        )
        weighted_piece = lax.dynamic_slice_in_dim(weighted, start, block_rows, 1)
        piece_misfit = (weighted_piece.astype(jnp.float32) - predicted).astype(jnp.bfloat16)
        return lax.dynamic_update_slice_in_dim(misfit_acc, piece_misfit, start, 1)

    misfit = lax.fori_loop(
        0, block_count, misfit_step, jnp.zeros((STRESS, chunk_rows, lanes), jnp.bfloat16)
    )
    misfit = lax.all_gather(misfit, "cols", axis=1, tiled=True)
    misfit = misfit.reshape(STRESS, plane_count, coarse_x, coarse_z)
    return (coefficients, misfit)


def solution(mesh):
    placed = (
        P("cols", "groups", "rep", "slab"),
        P(None, "groups", "rep", "slab"),
        P("groups"),
        P(),
    )
    return jax.shard_map(
        local,
        mesh=mesh,
        in_specs=placed,
        out_specs=(P(None, "groups", "cols"), P(None, "groups", "rep", "slab")),
        check_vma=False,
    )
```

```python
import math

import jax
import jax.numpy as jnp
import numpy as np
from jax import lax
from jax.experimental import pallas as pl
from jax.sharding import PartitionSpec as P

STRESS = 6
TERMS = 256
NY = 2048
PASSES = 3
ITERS = 3


ridge_weight = 0.05
epsilon = 1e-06


def extended(array, sides, width):
    for axis, dim in sides:
        count, length = (lax.axis_size(axis), array.shape[dim])
        up = [(i, (i + 1) % count) for i in range(count)]
        down = [(j, i) for i, j in up]
        last = lax.slice_in_dim(array, length - width, length, axis=dim)
        leading = lax.slice_in_dim(array, 0, width, axis=dim)
        before = lax.ppermute(last, axis, up)
        after = lax.ppermute(leading, axis, down)
        array = jnp.concatenate([before, array, after], axis=dim)
    return array


def tree_sum(value, axes):
    for axis in axes:
        count = lax.axis_size(axis)
        if count & (count - 1):
            value = lax.psum(value, axis)
            continue
        step = 1
        while step < count:
            partner = [(i, i ^ step) for i in range(count)]
            value = value + lax.ppermute(value, axis, partner)
            step *= 2
    return value


def split_sum(value, lead, axes):
    count = lax.axis_size(lead)
    if count != 2 or value.shape[0] % 2:
        return tree_sum(value, (lead,) + axes)
    swap = [(0, 1), (1, 0)]
    value = value + lax.ppermute(value, lead, swap)
    half = value.shape[0] // 2
    first = lax.axis_index(lead) == 0
    mine = jnp.where(first, value[:half], value[half:])
    mine = tree_sum(mine, axes)
    other = lax.ppermute(mine, lead, swap)
    return jnp.where(first, jnp.concatenate([mine, other]), jnp.concatenate([other, mine]))


def neighbour_edges(array, axis, dim, width):
    count, length = (lax.axis_size(axis), array.shape[dim])
    up = [(i, (i + 1) % count) for i in range(count)]
    down = [(j, i) for i, j in up]
    last = lax.slice_in_dim(array, length - width, length, axis=dim)
    leading = lax.slice_in_dim(array, 0, width, axis=dim)
    if count == 2:
        both = lax.ppermute(jnp.stack([last, leading]), axis, up)
        return (both[0], both[1])
    return (lax.ppermute(last, axis, up), lax.ppermute(leading, axis, down))


def conjugate_passes(gram_ref, target_ref, mask_ref, out_ref):
    gram = gram_ref[...]
    target = target_ref[...]
    gram_high = gram.astype(jnp.bfloat16)
    gram_low = (gram - gram_high.astype(jnp.float32)).astype(jnp.bfloat16)

    def product_with(left, right):
        return lax.dot_general(
            left, right, (((1,), (1,)), ((), ())), preferred_element_type=jnp.float32
        )

    def apply_normal(vector, active):
        masked = active * vector
        masked_high = masked.astype(jnp.bfloat16)
        masked_low = (masked - masked_high.astype(jnp.float32)).astype(jnp.bfloat16)
        product = (
            product_with(masked_high, gram_high)
            + product_with(masked_low, gram_high)
            + product_with(masked_high, gram_low)
        )
        return active * product + ridge_weight * vector

    solution_all = jnp.zeros(target.shape, jnp.float32)
    for pass_index in range(PASSES):
        active = mask_ref[pass_index]
        solution_all = active * solution_all
        remain = active * target - apply_normal(solution_all, active)
        direction = remain
        norm_now = jnp.sum(remain * remain, axis=1, keepdims=True)
        for turn_index in range(ITERS):
            applied = apply_normal(direction, active)
            curve_sum = jnp.sum(direction * applied, axis=1, keepdims=True)
            step_size = norm_now / (curve_sum + epsilon)
            solution_all = solution_all + step_size * direction
            remain = remain - step_size * applied
            norm_next = jnp.sum(remain * remain, axis=1, keepdims=True)
            direction = remain + (norm_next / (norm_now + epsilon)) * direction
            norm_now = norm_next
        out_ref[pass_index] = solution_all


def kernel(spread):
    offsets = np.arange(13) - 6.0
    values = np.exp(-offsets * offsets / (2.0 * spread * spread))
    return values / values.sum()


def filter_table(cells, first_taps, second_taps, guard, order):
    out_count = cells // 4
    shape = tuple((cells + 10, 2, out_count)[d] for d in order)
    where = {d: order.index(d) for d in range(3)}
    position = lax.broadcasted_iota(jnp.int32, shape, where[0])
    which = lax.broadcasted_iota(jnp.int32, shape, where[1])
    out_index = lax.broadcasted_iota(jnp.int32, shape, where[2])
    tap_at = position - 1 - 4 * out_index + guard
    table = jnp.zeros(shape, jnp.float32)
    for tap_index in range(13):
        value = jnp.where(
            which == 0, np.float32(first_taps[tap_index]), np.float32(second_taps[tap_index])
        )
        table = jnp.where(tap_at == tap_index, value, table)
    return table


def library(narrow_part, broad_part):
    product = (
        narrow_part.astype(jnp.float32)[:, None] * broad_part.astype(jnp.float32)[None, :]
    )
    return product.astype(jnp.bfloat16).reshape(
        (narrow_part.shape[0] * broad_part.shape[0],) + narrow_part.shape[1:]
    )


def local(fields, stresses, planes, active_masks):
    chan_dev, plane_count, cells_x, cells_z = fields.shape
    coarse_x = cells_x // 4
    coarse_z = cells_z // 4
    row_count = plane_count * coarse_x * coarse_z
    col_devices = lax.axis_size("cols")
    column_index = lax.axis_index("cols")
    term_dev = TERMS // col_devices
    offset = column_index * term_dev
    samples = float(row_count * lax.axis_size("slab") * lax.axis_size("rep"))
    height = 2.0 * (planes.astype(jnp.float32) + 0.5) / NY - 1.0
    root_weight = jnp.sqrt(1.2 - height * height)
    width = 5
    top, bottom = neighbour_edges(fields, "rep", 2, width)
    narrow_taps = kernel(1.5)
    broad_taps = kernel(3.0)
    guard = jnp.minimum(lax.axis_index("rep"), 0)
    span_table = filter_table(cells_z, narrow_taps, broad_taps, guard, (0, 1, 2))
    stream_table = filter_table(cells_x, narrow_taps, broad_taps, guard, (1, 0, 2))
    highest = lax.Precision.HIGHEST
    along_stream = (
        jnp.einsum(
            "cpxz,sxm->scpmz",
            fields.astype(jnp.float32),
            stream_table[:, width : width + cells_x],
            precision=highest,
        )
        + jnp.einsum(
            "cpxz,sxm->scpmz", top.astype(jnp.float32), stream_table[:, :width], precision=highest
        )
        + jnp.einsum(
            "cpxz,sxm->scpmz",
            bottom.astype(jnp.float32),
            stream_table[:, width + cells_x :],
            precision=highest,
        )
    )
    left, right = neighbour_edges(jnp.swapaxes(along_stream, 3, 4), "slab", 3, width)
    filtered = (
        jnp.einsum(
            "scpmz,zsn->scpmn",
            along_stream,
            span_table[width : width + cells_z],
            precision=highest,
        )
        + jnp.einsum("scpzm,zsn->scpmn", left, span_table[:width], precision=highest)
        + jnp.einsum("scpzm,zsn->scpmn", right, span_table[width + cells_z :], precision=highest)
    )
    narrow = filtered[0]
    broader = filtered[1]
    narrow_set = narrow.astype(jnp.bfloat16).reshape(chan_dev, row_count)
    broad_set = (
        (broader * root_weight[None, :, None, None])
        .astype(jnp.bfloat16)
        .reshape(chan_dev, row_count)
    )
    weighted = (stresses.astype(jnp.float32) * root_weight[None, :, None, None]).astype(
        jnp.bfloat16
    )
    weighted = weighted.reshape(STRESS, row_count)
    chunk = row_count // col_devices
    lanes = 128
    chunk_rows = chunk // lanes
    channels = chan_dev * col_devices
    sets = jnp.stack([narrow_set, broad_set]).reshape(2, chan_dev, col_devices, chunk_rows, lanes)
    sets = jnp.transpose(sets, (2, 0, 1, 3, 4)).reshape(col_devices, 2 * chan_dev * chunk_rows, lanes)
    sets = lax.all_to_all(sets, "cols", 0, 0, tiled=True)
    sets = sets.reshape(col_devices, 2, chan_dev, chunk_rows, lanes)
    sets = jnp.transpose(sets, (1, 0, 2, 3, 4)).reshape(2, channels, chunk_rows, lanes)
    narrow_all, broad_all = sets[0], sets[1]
    weighted = weighted.reshape(STRESS, col_devices, chunk_rows, lanes)
    weighted = lax.dynamic_index_in_dim(weighted, column_index, 1, keepdims=False)
    block_rows = chunk_rows
    block_count = chunk_rows // block_rows

    def gram_step(block_index, carry):
        gram_acc, rhs_acc = carry
        start = block_index * block_rows
        narrow_piece = lax.dynamic_slice_in_dim(narrow_all, start, block_rows, 1)
        broad_piece = lax.dynamic_slice_in_dim(broad_all, start, block_rows, 1)
        all_terms = library(narrow_piece, broad_piece)
        weighted_piece = lax.dynamic_slice_in_dim(weighted, start, block_rows, 1)
        gram_acc = gram_acc + jnp.einsum(
            "iqr,jqr->ij", all_terms, all_terms, preferred_element_type=jnp.float32
        )
        rhs_acc = rhs_acc + jnp.einsum(
            "iqr,kqr->ik", all_terms, weighted_piece, preferred_element_type=jnp.float32
        )
        return (gram_acc, rhs_acc)

    gram_part, rhs_part = lax.fori_loop(
        0,
        block_count,
        gram_step,
        (jnp.zeros((TERMS, TERMS), jnp.float32), jnp.zeros((TERMS, STRESS), jnp.float32)),
    )
    full_rows = split_sum(jnp.concatenate([gram_part, rhs_part], axis=1), "rep", ("slab", "cols"))
    gram_matrix = full_rows[:, :TERMS]
    rhs_sums = full_rows[:, TERMS:]
    on_diagonal = lax.broadcasted_iota(jnp.int32, (TERMS, TERMS), 0) == lax.broadcasted_iota(
        jnp.int32, (TERMS, TERMS), 1
    )
    diagonal = jnp.sum(jnp.where(on_diagonal, gram_matrix, 0.0), axis=1)
    column_scale = 1.0 / jnp.sqrt(diagonal / samples + epsilon)
    normal_gram = column_scale[:, None] * gram_matrix * column_scale[None, :] / samples
    target_norm = column_scale[None, :] * rhs_sums.T / samples

    padded_rows = -(-STRESS // 8) * 8
    target_padded = jnp.zeros((padded_rows, TERMS), jnp.float32).at[:STRESS].set(target_norm)
    masks_padded = (
        jnp.zeros((PASSES, padded_rows, TERMS), jnp.float32)
        .at[:, :STRESS]
        .set(active_masks.astype(jnp.float32))
    )
    passes = pl.pallas_call(
        conjugate_passes,
        out_shape=jax.ShapeDtypeStruct((PASSES, padded_rows, TERMS), jnp.float32),
    )(normal_gram, target_padded, masks_padded)
    coefficients = lax.dynamic_slice_in_dim(passes[:, :STRESS], offset, term_dev, 2)
    solution_all = passes[PASSES - 1, :STRESS]
    final_weights = (column_scale[None, :] * solution_all).astype(jnp.bfloat16)

    def misfit_step(block_index, misfit_acc):
        start = block_index * block_rows
        narrow_piece = lax.dynamic_slice_in_dim(narrow_all, start, block_rows, 1)
        broad_piece = lax.dynamic_slice_in_dim(broad_all, start, block_rows, 1)
        all_terms = library(narrow_piece, broad_piece)
        predicted = jnp.einsum(
            "ki,iqr->kqr", final_weights, all_terms, preferred_element_type=jnp.float32
        )
        weighted_piece = lax.dynamic_slice_in_dim(weighted, start, block_rows, 1)
        piece_misfit = (weighted_piece.astype(jnp.float32) - predicted).astype(jnp.bfloat16)
        return lax.dynamic_update_slice_in_dim(misfit_acc, piece_misfit, start, 1)

    misfit = lax.fori_loop(
        0, block_count, misfit_step, jnp.zeros((STRESS, chunk_rows, lanes), jnp.bfloat16)
    )
    misfit = lax.all_gather(misfit, "cols", axis=1, tiled=True)
    misfit = misfit.reshape(STRESS, plane_count, coarse_x, coarse_z)
    return (coefficients, misfit)


def solution(mesh):
    placed = (
        P("cols", "groups", "rep", "slab"),
        P(None, "groups", "rep", "slab"),
        P("groups"),
        P(),
    )
    return jax.shard_map(
        local,
        mesh=mesh,
        in_specs=placed,
        out_specs=(P(None, "groups", "cols"), P(None, "groups", "rep", "slab")),
        check_vma=False,
    )
```

```python
import math

import jax
import jax.numpy as jnp
import numpy as np
from jax import lax
from jax.experimental import pallas as pl
from jax.sharding import PartitionSpec as P

STRESS = 6
TERMS = 256
NY = 2048
PASSES = 3
ITERS = 3


ridge_weight = 0.05
epsilon = 1e-06


def extended(array, sides, width):
    for axis, dim in sides:
        count, length = (lax.axis_size(axis), array.shape[dim])
        up = [(i, (i + 1) % count) for i in range(count)]
        down = [(j, i) for i, j in up]
        last = lax.slice_in_dim(array, length - width, length, axis=dim)
        leading = lax.slice_in_dim(array, 0, width, axis=dim)
        before = lax.ppermute(last, axis, up)
        after = lax.ppermute(leading, axis, down)
        array = jnp.concatenate([before, array, after], axis=dim)
    return array


def tree_sum(value, axes):
    for axis in axes:
        count = lax.axis_size(axis)
        if count & (count - 1):
            value = lax.psum(value, axis)
            continue
        step = 1
        while step < count:
            partner = [(i, i ^ step) for i in range(count)]
            value = value + lax.ppermute(value, axis, partner)
            step *= 2
    return value


def split_sum(value, lead, axes):
    count = lax.axis_size(lead)
    if count != 2 or value.shape[0] % 2:
        return tree_sum(value, (lead,) + axes)
    swap = [(0, 1), (1, 0)]
    value = value + lax.ppermute(value, lead, swap)
    half = value.shape[0] // 2
    first = lax.axis_index(lead) == 0
    mine = jnp.where(first, value[:half], value[half:])
    mine = tree_sum(mine, axes)
    other = lax.ppermute(mine, lead, swap)
    return jnp.where(first, jnp.concatenate([mine, other]), jnp.concatenate([other, mine]))


def neighbour_edges(array, axis, dim, width):
    count, length = (lax.axis_size(axis), array.shape[dim])
    up = [(i, (i + 1) % count) for i in range(count)]
    down = [(j, i) for i, j in up]
    last = lax.slice_in_dim(array, length - width, length, axis=dim)
    leading = lax.slice_in_dim(array, 0, width, axis=dim)
    return (lax.ppermute(last, axis, up), lax.ppermute(leading, axis, down))


def conjugate_passes(gram_ref, target_ref, mask_ref, out_ref):
    gram = gram_ref[...]
    target = target_ref[...]
    gram_high = gram.astype(jnp.bfloat16)
    gram_low = (gram - gram_high.astype(jnp.float32)).astype(jnp.bfloat16)

    def product_with(left, right):
        return lax.dot_general(
            left, right, (((1,), (1,)), ((), ())), preferred_element_type=jnp.float32
        )

    def apply_normal(vector, active):
        masked = active * vector
        masked_high = masked.astype(jnp.bfloat16)
        masked_low = (masked - masked_high.astype(jnp.float32)).astype(jnp.bfloat16)
        product = (
            product_with(masked_high, gram_high)
            + product_with(masked_low, gram_high)
            + product_with(masked_high, gram_low)
        )
        return active * product + ridge_weight * vector

    solution_all = jnp.zeros(target.shape, jnp.float32)
    for pass_index in range(PASSES):
        active = mask_ref[pass_index]
        solution_all = active * solution_all
        remain = active * target - apply_normal(solution_all, active)
        direction = remain
        norm_now = jnp.sum(remain * remain, axis=1, keepdims=True)
        for turn_index in range(ITERS):
            applied = apply_normal(direction, active)
            curve_sum = jnp.sum(direction * applied, axis=1, keepdims=True)
            step_size = norm_now / (curve_sum + epsilon)
            solution_all = solution_all + step_size * direction
            remain = remain - step_size * applied
            norm_next = jnp.sum(remain * remain, axis=1, keepdims=True)
            direction = remain + (norm_next / (norm_now + epsilon)) * direction
            norm_now = norm_next
        out_ref[pass_index] = solution_all


def kernel(spread):
    offsets = np.arange(13) - 6.0
    values = np.exp(-offsets * offsets / (2.0 * spread * spread))
    return values / values.sum()


def filter_table(cells, first_taps, second_taps, guard, order):
    out_count = cells // 4
    shape = tuple((cells + 10, 2, out_count)[d] for d in order)
    where = {d: order.index(d) for d in range(3)}
    position = lax.broadcasted_iota(jnp.int32, shape, where[0])
    which = lax.broadcasted_iota(jnp.int32, shape, where[1])
    out_index = lax.broadcasted_iota(jnp.int32, shape, where[2])
    tap_at = position - 1 - 4 * out_index + guard
    table = jnp.zeros(shape, jnp.float32)
    for tap_index in range(13):
        value = jnp.where(
            which == 0, np.float32(first_taps[tap_index]), np.float32(second_taps[tap_index])
        )
        table = jnp.where(tap_at == tap_index, value, table)
    return table


def library(narrow_part, broad_part):
    product = (
        narrow_part.astype(jnp.float32)[:, None] * broad_part.astype(jnp.float32)[None, :]
    )
    return product.astype(jnp.bfloat16).reshape(
        (narrow_part.shape[0] * broad_part.shape[0],) + narrow_part.shape[1:]
    )


def local(fields, stresses, planes, active_masks):
    chan_dev, plane_count, cells_x, cells_z = fields.shape
    coarse_x = cells_x // 4
    coarse_z = cells_z // 4
    row_count = plane_count * coarse_x * coarse_z
    col_devices = lax.axis_size("cols")
    column_index = lax.axis_index("cols")
    term_dev = TERMS // col_devices
    offset = column_index * term_dev
    samples = float(row_count * lax.axis_size("slab") * lax.axis_size("rep"))
    height = 2.0 * (planes.astype(jnp.float32) + 0.5) / NY - 1.0
    root_weight = jnp.sqrt(1.2 - height * height)
    width = 5
    top, bottom = neighbour_edges(fields, "rep", 2, width)
    narrow_taps = kernel(1.5)
    broad_taps = kernel(3.0)
    guard = jnp.minimum(lax.axis_index("rep"), 0)
    span_table = filter_table(cells_z, narrow_taps, broad_taps, guard, (0, 1, 2))
    stream_table = filter_table(cells_x, narrow_taps, broad_taps, guard, (1, 0, 2))
    highest = lax.Precision.HIGHEST
    along_stream = (
        jnp.einsum(
            "cpxz,sxm->scpmz",
            fields.astype(jnp.float32),
            stream_table[:, width : width + cells_x],
            precision=lax.Precision.HIGH,
        )
        + jnp.einsum(
            "cpxz,sxm->scpmz", top.astype(jnp.float32), stream_table[:, :width], precision=lax.Precision.HIGH
        )
        + jnp.einsum(
            "cpxz,sxm->scpmz",
            bottom.astype(jnp.float32),
            stream_table[:, width + cells_x :],
            precision=lax.Precision.HIGH,
        )
    )
    left, right = neighbour_edges(jnp.swapaxes(along_stream, 3, 4), "slab", 3, width)
    filtered = (
        jnp.einsum(
            "scpmz,zsn->scpmn",
            along_stream,
            span_table[width : width + cells_z],
            precision=highest,
        )
        + jnp.einsum("scpzm,zsn->scpmn", left, span_table[:width], precision=highest)
        + jnp.einsum("scpzm,zsn->scpmn", right, span_table[width + cells_z :], precision=highest)
    )
    narrow = filtered[0]
    broader = filtered[1]
    narrow_set = narrow.astype(jnp.bfloat16).reshape(chan_dev, row_count)
    broad_set = (
        (broader * root_weight[None, :, None, None])
        .astype(jnp.bfloat16)
        .reshape(chan_dev, row_count)
    )
    weighted = (stresses.astype(jnp.float32) * root_weight[None, :, None, None]).astype(
        jnp.bfloat16
    )
    weighted = weighted.reshape(STRESS, row_count)
    chunk = row_count // col_devices
    lanes = 128
    chunk_rows = chunk // lanes
    channels = chan_dev * col_devices
    sets = jnp.stack([narrow_set, broad_set]).reshape(2, chan_dev, col_devices, chunk_rows, lanes)
    sets = jnp.transpose(sets, (2, 0, 1, 3, 4)).reshape(col_devices, 2 * chan_dev * chunk_rows, lanes)
    sets = lax.all_to_all(sets, "cols", 0, 0, tiled=True)
    sets = sets.reshape(col_devices, 2, chan_dev, chunk_rows, lanes)
    sets = jnp.transpose(sets, (1, 0, 2, 3, 4)).reshape(2, channels, chunk_rows, lanes)
    narrow_all, broad_all = sets[0], sets[1]
    weighted = weighted.reshape(STRESS, col_devices, chunk_rows, lanes)
    weighted = lax.dynamic_index_in_dim(weighted, column_index, 1, keepdims=False)
    block_rows = chunk_rows
    block_count = chunk_rows // block_rows

    def gram_step(block_index, carry):
        gram_acc, rhs_acc = carry
        start = block_index * block_rows
        narrow_piece = lax.dynamic_slice_in_dim(narrow_all, start, block_rows, 1)
        broad_piece = lax.dynamic_slice_in_dim(broad_all, start, block_rows, 1)
        all_terms = library(narrow_piece, broad_piece)
        weighted_piece = lax.dynamic_slice_in_dim(weighted, start, block_rows, 1)
        gram_acc = gram_acc + jnp.einsum(
            "iqr,jqr->ij", all_terms, all_terms, preferred_element_type=jnp.float32
        )
        rhs_acc = rhs_acc + jnp.einsum(
            "iqr,kqr->ik", all_terms, weighted_piece, preferred_element_type=jnp.float32
        )
        return (gram_acc, rhs_acc)

    gram_part, rhs_part = lax.fori_loop(
        0,
        block_count,
        gram_step,
        (jnp.zeros((TERMS, TERMS), jnp.float32), jnp.zeros((TERMS, STRESS), jnp.float32)),
    )
    full_rows = split_sum(jnp.concatenate([gram_part, rhs_part], axis=1), "rep", ("slab", "cols"))
    gram_matrix = full_rows[:, :TERMS]
    rhs_sums = full_rows[:, TERMS:]
    on_diagonal = lax.broadcasted_iota(jnp.int32, (TERMS, TERMS), 0) == lax.broadcasted_iota(
        jnp.int32, (TERMS, TERMS), 1
    )
    diagonal = jnp.sum(jnp.where(on_diagonal, gram_matrix, 0.0), axis=1)
    column_scale = 1.0 / jnp.sqrt(diagonal / samples + epsilon)
    normal_gram = column_scale[:, None] * gram_matrix * column_scale[None, :] / samples
    target_norm = column_scale[None, :] * rhs_sums.T / samples

    padded_rows = -(-STRESS // 8) * 8
    target_padded = jnp.zeros((padded_rows, TERMS), jnp.float32).at[:STRESS].set(target_norm)
    masks_padded = (
        jnp.zeros((PASSES, padded_rows, TERMS), jnp.float32)
        .at[:, :STRESS]
        .set(active_masks.astype(jnp.float32))
    )
    passes = pl.pallas_call(
        conjugate_passes,
        out_shape=jax.ShapeDtypeStruct((PASSES, padded_rows, TERMS), jnp.float32),
    )(normal_gram, target_padded, masks_padded)
    coefficients = lax.dynamic_slice_in_dim(passes[:, :STRESS], offset, term_dev, 2)
    solution_all = passes[PASSES - 1, :STRESS]
    final_weights = (column_scale[None, :] * solution_all).astype(jnp.bfloat16)

    def misfit_step(block_index, misfit_acc):
        start = block_index * block_rows
        narrow_piece = lax.dynamic_slice_in_dim(narrow_all, start, block_rows, 1)
        broad_piece = lax.dynamic_slice_in_dim(broad_all, start, block_rows, 1)
        all_terms = library(narrow_piece, broad_piece)
        predicted = jnp.einsum(
            "ki,iqr->kqr", final_weights, all_terms, preferred_element_type=jnp.float32
        )
        weighted_piece = lax.dynamic_slice_in_dim(weighted, start, block_rows, 1)
        piece_misfit = (weighted_piece.astype(jnp.float32) - predicted).astype(jnp.bfloat16)
        return lax.dynamic_update_slice_in_dim(misfit_acc, piece_misfit, start, 1)

    misfit = lax.fori_loop(
        0, block_count, misfit_step, jnp.zeros((STRESS, chunk_rows, lanes), jnp.bfloat16)
    )
    misfit = lax.all_gather(misfit, "cols", axis=1, tiled=True)
    misfit = misfit.reshape(STRESS, plane_count, coarse_x, coarse_z)
    return (coefficients, misfit)


def solution(mesh):
    placed = (
        P("cols", "groups", "rep", "slab"),
        P(None, "groups", "rep", "slab"),
        P("groups"),
        P(),
    )
    return jax.shard_map(
        local,
        mesh=mesh,
        in_specs=placed,
        out_specs=(P(None, "groups", "cols"), P(None, "groups", "rep", "slab")),
        check_vma=False,
    )
```

```python
import math

import jax
import jax.numpy as jnp
import numpy as np
from jax import lax
from jax.experimental import pallas as pl
from jax.sharding import PartitionSpec as P

STRESS = 6
TERMS = 256
NY = 2048
PASSES = 3
ITERS = 3


ridge_weight = 0.05
epsilon = 1e-06


def extended(array, sides, width):
    for axis, dim in sides:
        count, length = (lax.axis_size(axis), array.shape[dim])
        up = [(i, (i + 1) % count) for i in range(count)]
        down = [(j, i) for i, j in up]
        last = lax.slice_in_dim(array, length - width, length, axis=dim)
        leading = lax.slice_in_dim(array, 0, width, axis=dim)
        before = lax.ppermute(last, axis, up)
        after = lax.ppermute(leading, axis, down)
        array = jnp.concatenate([before, array, after], axis=dim)
    return array


def tree_sum(value, axes):
    for axis in axes:
        count = lax.axis_size(axis)
        if count & (count - 1):
            value = lax.psum(value, axis)
            continue
        step = 1
        while step < count:
            partner = [(i, i ^ step) for i in range(count)]
            value = value + lax.ppermute(value, axis, partner)
            step *= 2
    return value


def split_sum(value, lead, axes):
    count = lax.axis_size(lead)
    if count != 2 or value.shape[0] % 2:
        return tree_sum(value, (lead,) + axes)
    swap = [(0, 1), (1, 0)]
    value = value + lax.ppermute(value, lead, swap)
    half = value.shape[0] // 2
    first = lax.axis_index(lead) == 0
    mine = jnp.where(first, value[:half], value[half:])
    mine = tree_sum(mine, axes)
    other = lax.ppermute(mine, lead, swap)
    return jnp.where(first, jnp.concatenate([mine, other]), jnp.concatenate([other, mine]))


def neighbour_edges(array, axis, dim, width):
    count, length = (lax.axis_size(axis), array.shape[dim])
    up = [(i, (i + 1) % count) for i in range(count)]
    down = [(j, i) for i, j in up]
    last = lax.slice_in_dim(array, length - width, length, axis=dim)
    leading = lax.slice_in_dim(array, 0, width, axis=dim)
    return (lax.ppermute(last, axis, up), lax.ppermute(leading, axis, down))


def conjugate_passes(gram_ref, target_ref, mask_ref, out_ref):
    gram = gram_ref[...]
    target = target_ref[...]
    gram_high = gram.astype(jnp.bfloat16)
    gram_low = (gram - gram_high.astype(jnp.float32)).astype(jnp.bfloat16)

    def product_with(left, right):
        return lax.dot_general(
            left, right, (((1,), (1,)), ((), ())), preferred_element_type=jnp.float32
        )

    def apply_normal(vector, active):
        masked = active * vector
        masked_high = masked.astype(jnp.bfloat16)
        masked_low = (masked - masked_high.astype(jnp.float32)).astype(jnp.bfloat16)
        product = (
            product_with(masked_high, gram_high)
            + product_with(masked_low, gram_high)
            + product_with(masked_high, gram_low)
        )
        return active * product + ridge_weight * vector

    solution_all = jnp.zeros(target.shape, jnp.float32)
    for pass_index in range(PASSES):
        active = mask_ref[pass_index]
        solution_all = active * solution_all
        remain = active * target - apply_normal(solution_all, active)
        direction = remain
        norm_now = jnp.sum(remain * remain, axis=1, keepdims=True)
        for turn_index in range(ITERS):
            applied = apply_normal(direction, active)
            curve_sum = jnp.sum(direction * applied, axis=1, keepdims=True)
            step_size = norm_now / (curve_sum + epsilon)
            solution_all = solution_all + step_size * direction
            remain = remain - step_size * applied
            norm_next = jnp.sum(remain * remain, axis=1, keepdims=True)
            direction = remain + (norm_next / (norm_now + epsilon)) * direction
            norm_now = norm_next
        out_ref[pass_index] = solution_all


def kernel(spread):
    offsets = np.arange(13) - 6.0
    values = np.exp(-offsets * offsets / (2.0 * spread * spread))
    return values / values.sum()


def filter_table(cells, first_taps, second_taps, guard, order):
    out_count = cells // 4
    shape = tuple((cells + 10, 2, out_count)[d] for d in order)
    where = {d: order.index(d) for d in range(3)}
    position = lax.broadcasted_iota(jnp.int32, shape, where[0])
    which = lax.broadcasted_iota(jnp.int32, shape, where[1])
    out_index = lax.broadcasted_iota(jnp.int32, shape, where[2])
    tap_at = position - 1 - 4 * out_index + guard
    table = jnp.zeros(shape, jnp.float32)
    for tap_index in range(13):
        value = jnp.where(
            which == 0, np.float32(first_taps[tap_index]), np.float32(second_taps[tap_index])
        )
        table = jnp.where(tap_at == tap_index, value, table)
    return table


def library(narrow_part, broad_part):
    product = (
        narrow_part.astype(jnp.float32)[:, None] * broad_part.astype(jnp.float32)[None, :]
    )
    return product.astype(jnp.bfloat16).reshape(
        (narrow_part.shape[0] * broad_part.shape[0],) + narrow_part.shape[1:]
    )


def local(fields, stresses, planes, active_masks):
    chan_dev, plane_count, cells_x, cells_z = fields.shape
    coarse_x = cells_x // 4
    coarse_z = cells_z // 4
    row_count = plane_count * coarse_x * coarse_z
    col_devices = lax.axis_size("cols")
    column_index = lax.axis_index("cols")
    term_dev = TERMS // col_devices
    offset = column_index * term_dev
    samples = float(row_count * lax.axis_size("slab") * lax.axis_size("rep"))
    height = 2.0 * (planes.astype(jnp.float32) + 0.5) / NY - 1.0
    root_weight = jnp.sqrt(1.2 - height * height)
    width = 5
    top, bottom = neighbour_edges(fields, "rep", 2, width)
    narrow_taps = kernel(1.5)
    broad_taps = kernel(3.0)
    guard = jnp.minimum(lax.axis_index("rep"), 0)
    span_table = filter_table(cells_z, narrow_taps, broad_taps, guard, (0, 1, 2))
    stream_table = filter_table(cells_x, narrow_taps, broad_taps, guard, (1, 0, 2))
    highest = lax.Precision.HIGHEST
    along_stream = (
        jnp.einsum(
            "cpxz,sxm->scpmz",
            fields.astype(jnp.float32),
            stream_table[:, width : width + cells_x],
            precision=lax.Precision.HIGH,
        )
        + jnp.einsum(
            "cpxz,sxm->scpmz", top.astype(jnp.float32), stream_table[:, :width], precision=lax.Precision.HIGH
        )
        + jnp.einsum(
            "cpxz,sxm->scpmz",
            bottom.astype(jnp.float32),
            stream_table[:, width + cells_x :],
            precision=lax.Precision.HIGH,
        )
    )
    left, right = neighbour_edges(jnp.swapaxes(along_stream, 3, 4), "slab", 3, width)
    filtered = (
        jnp.einsum(
            "scpmz,zsn->scpmn",
            along_stream,
            span_table[width : width + cells_z],
            precision=lax.Precision.HIGH,
        )
        + jnp.einsum("scpzm,zsn->scpmn", left, span_table[:width], precision=lax.Precision.HIGH)
        + jnp.einsum("scpzm,zsn->scpmn", right, span_table[width + cells_z :], precision=lax.Precision.HIGH)
    )
    narrow = filtered[0]
    broader = filtered[1]
    narrow_set = narrow.astype(jnp.bfloat16).reshape(chan_dev, row_count)
    broad_set = (
        (broader * root_weight[None, :, None, None])
        .astype(jnp.bfloat16)
        .reshape(chan_dev, row_count)
    )
    weighted = (stresses.astype(jnp.float32) * root_weight[None, :, None, None]).astype(
        jnp.bfloat16
    )
    weighted = weighted.reshape(STRESS, row_count)
    chunk = row_count // col_devices
    lanes = 128
    chunk_rows = chunk // lanes
    channels = chan_dev * col_devices
    sets = jnp.stack([narrow_set, broad_set]).reshape(2, chan_dev, col_devices, chunk_rows, lanes)
    sets = jnp.transpose(sets, (2, 0, 1, 3, 4)).reshape(col_devices, 2 * chan_dev * chunk_rows, lanes)
    sets = lax.all_to_all(sets, "cols", 0, 0, tiled=True)
    sets = sets.reshape(col_devices, 2, chan_dev, chunk_rows, lanes)
    sets = jnp.transpose(sets, (1, 0, 2, 3, 4)).reshape(2, channels, chunk_rows, lanes)
    narrow_all, broad_all = sets[0], sets[1]
    weighted = weighted.reshape(STRESS, col_devices, chunk_rows, lanes)
    weighted = lax.dynamic_index_in_dim(weighted, column_index, 1, keepdims=False)
    block_rows = chunk_rows
    block_count = chunk_rows // block_rows

    def gram_step(block_index, carry):
        gram_acc, rhs_acc = carry
        start = block_index * block_rows
        narrow_piece = lax.dynamic_slice_in_dim(narrow_all, start, block_rows, 1)
        broad_piece = lax.dynamic_slice_in_dim(broad_all, start, block_rows, 1)
        all_terms = library(narrow_piece, broad_piece)
        weighted_piece = lax.dynamic_slice_in_dim(weighted, start, block_rows, 1)
        gram_acc = gram_acc + jnp.einsum(
            "iqr,jqr->ij", all_terms, all_terms, preferred_element_type=jnp.float32
        )
        rhs_acc = rhs_acc + jnp.einsum(
            "iqr,kqr->ik", all_terms, weighted_piece, preferred_element_type=jnp.float32
        )
        return (gram_acc, rhs_acc)

    gram_part, rhs_part = lax.fori_loop(
        0,
        block_count,
        gram_step,
        (jnp.zeros((TERMS, TERMS), jnp.float32), jnp.zeros((TERMS, STRESS), jnp.float32)),
    )
    full_rows = split_sum(jnp.concatenate([gram_part, rhs_part], axis=1), "rep", ("slab", "cols"))
    gram_matrix = full_rows[:, :TERMS]
    rhs_sums = full_rows[:, TERMS:]
    on_diagonal = lax.broadcasted_iota(jnp.int32, (TERMS, TERMS), 0) == lax.broadcasted_iota(
        jnp.int32, (TERMS, TERMS), 1
    )
    diagonal = jnp.sum(jnp.where(on_diagonal, gram_matrix, 0.0), axis=1)
    column_scale = 1.0 / jnp.sqrt(diagonal / samples + epsilon)
    normal_gram = column_scale[:, None] * gram_matrix * column_scale[None, :] / samples
    target_norm = column_scale[None, :] * rhs_sums.T / samples

    padded_rows = -(-STRESS // 8) * 8
    target_padded = jnp.zeros((padded_rows, TERMS), jnp.float32).at[:STRESS].set(target_norm)
    masks_padded = (
        jnp.zeros((PASSES, padded_rows, TERMS), jnp.float32)
        .at[:, :STRESS]
        .set(active_masks.astype(jnp.float32))
    )
    passes = pl.pallas_call(
        conjugate_passes,
        out_shape=jax.ShapeDtypeStruct((PASSES, padded_rows, TERMS), jnp.float32),
    )(normal_gram, target_padded, masks_padded)
    coefficients = lax.dynamic_slice_in_dim(passes[:, :STRESS], offset, term_dev, 2)
    solution_all = passes[PASSES - 1, :STRESS]
    final_weights = (column_scale[None, :] * solution_all).astype(jnp.bfloat16)

    def misfit_step(block_index, misfit_acc):
        start = block_index * block_rows
        narrow_piece = lax.dynamic_slice_in_dim(narrow_all, start, block_rows, 1)
        broad_piece = lax.dynamic_slice_in_dim(broad_all, start, block_rows, 1)
        all_terms = library(narrow_piece, broad_piece)
        predicted = jnp.einsum(
            "ki,iqr->kqr", final_weights, all_terms, preferred_element_type=jnp.float32
        )
        weighted_piece = lax.dynamic_slice_in_dim(weighted, start, block_rows, 1)
        piece_misfit = (weighted_piece.astype(jnp.float32) - predicted).astype(jnp.bfloat16)
        return lax.dynamic_update_slice_in_dim(misfit_acc, piece_misfit, start, 1)

    misfit = lax.fori_loop(
        0, block_count, misfit_step, jnp.zeros((STRESS, chunk_rows, lanes), jnp.bfloat16)
    )
    misfit = lax.all_gather(misfit, "cols", axis=1, tiled=True)
    misfit = misfit.reshape(STRESS, plane_count, coarse_x, coarse_z)
    return (coefficients, misfit)


def solution(mesh):
    placed = (
        P("cols", "groups", "rep", "slab"),
        P(None, "groups", "rep", "slab"),
        P("groups"),
        P(),
    )
    return jax.shard_map(
        local,
        mesh=mesh,
        in_specs=placed,
        out_specs=(P(None, "groups", "cols"), P(None, "groups", "rep", "slab")),
        check_vma=False,
    )
```

```python
import math

import jax
import jax.numpy as jnp
import numpy as np
from jax import lax
from jax.experimental import pallas as pl
from jax.sharding import PartitionSpec as P

STRESS = 6
TERMS = 256
NY = 2048
PASSES = 3
ITERS = 3


ridge_weight = 0.05
epsilon = 1e-06


def extended(array, sides, width):
    for axis, dim in sides:
        count, length = (lax.axis_size(axis), array.shape[dim])
        up = [(i, (i + 1) % count) for i in range(count)]
        down = [(j, i) for i, j in up]
        last = lax.slice_in_dim(array, length - width, length, axis=dim)
        leading = lax.slice_in_dim(array, 0, width, axis=dim)
        before = lax.ppermute(last, axis, up)
        after = lax.ppermute(leading, axis, down)
        array = jnp.concatenate([before, array, after], axis=dim)
    return array


def tree_sum(value, axes):
    for axis in axes:
        count = lax.axis_size(axis)
        if count & (count - 1):
            value = lax.psum(value, axis)
            continue
        step = 1
        while step < count:
            partner = [(i, i ^ step) for i in range(count)]
            value = value + lax.ppermute(value, axis, partner)
            step *= 2
    return value


def split_sum(value, lead, axes):
    count = lax.axis_size(lead)
    if count != 2 or value.shape[0] % 2:
        return tree_sum(value, (lead,) + axes)
    swap = [(0, 1), (1, 0)]
    value = value + lax.ppermute(value, lead, swap)
    half = value.shape[0] // 2
    first = lax.axis_index(lead) == 0
    mine = jnp.where(first, value[:half], value[half:])
    mine = tree_sum(mine, axes)
    other = lax.ppermute(mine, lead, swap)
    return jnp.where(first, jnp.concatenate([mine, other]), jnp.concatenate([other, mine]))


def neighbour_edges(array, axis, dim, width):
    count, length = (lax.axis_size(axis), array.shape[dim])
    up = [(i, (i + 1) % count) for i in range(count)]
    down = [(j, i) for i, j in up]
    last = lax.slice_in_dim(array, length - width, length, axis=dim)
    leading = lax.slice_in_dim(array, 0, width, axis=dim)
    return (lax.ppermute(last, axis, up), lax.ppermute(leading, axis, down))


def conjugate_passes(gram_ref, target_ref, mask_ref, out_ref):
    gram = gram_ref[...]
    target = target_ref[...]
    gram_high = gram.astype(jnp.bfloat16)
    gram_low = (gram - gram_high.astype(jnp.float32)).astype(jnp.bfloat16)

    def product_with(left, right):
        return lax.dot_general(
            left, right, (((1,), (1,)), ((), ())), preferred_element_type=jnp.float32
        )

    def apply_normal(vector, active):
        masked = active * vector
        masked_high = masked.astype(jnp.bfloat16)
        masked_low = (masked - masked_high.astype(jnp.float32)).astype(jnp.bfloat16)
        product = (
            product_with(masked_high, gram_high)
            + product_with(masked_low, gram_high)
            + product_with(masked_high, gram_low)
        )
        return active * product + ridge_weight * vector

    solution_all = jnp.zeros(target.shape, jnp.float32)
    for pass_index in range(PASSES):
        active = mask_ref[pass_index]
        solution_all = active * solution_all
        remain = active * target - apply_normal(solution_all, active)
        direction = remain
        norm_now = jnp.sum(remain * remain, axis=1, keepdims=True)
        for turn_index in range(ITERS):
            applied = apply_normal(direction, active)
            curve_sum = jnp.sum(direction * applied, axis=1, keepdims=True)
            step_size = norm_now / (curve_sum + epsilon)
            solution_all = solution_all + step_size * direction
            remain = remain - step_size * applied
            norm_next = jnp.sum(remain * remain, axis=1, keepdims=True)
            direction = remain + (norm_next / (norm_now + epsilon)) * direction
            norm_now = norm_next
        out_ref[pass_index] = solution_all


def kernel(spread):
    offsets = np.arange(13) - 6.0
    values = np.exp(-offsets * offsets / (2.0 * spread * spread))
    return values / values.sum()


def filter_table(cells, first_taps, second_taps, guard, order):
    out_count = cells // 4
    shape = tuple((cells + 10, 2, out_count)[d] for d in order)
    where = {d: order.index(d) for d in range(3)}
    position = lax.broadcasted_iota(jnp.int32, shape, where[0])
    which = lax.broadcasted_iota(jnp.int32, shape, where[1])
    out_index = lax.broadcasted_iota(jnp.int32, shape, where[2])
    tap_at = position - 1 - 4 * out_index + guard
    table = jnp.zeros(shape, jnp.float32)
    for tap_index in range(13):
        value = jnp.where(
            which == 0, np.float32(first_taps[tap_index]), np.float32(second_taps[tap_index])
        )
        table = jnp.where(tap_at == tap_index, value, table)
    return table


def library(narrow_part, broad_part):
    product = (
        narrow_part.astype(jnp.float32)[:, None] * broad_part.astype(jnp.float32)[None, :]
    )
    return product.astype(jnp.bfloat16).reshape(
        (narrow_part.shape[0] * broad_part.shape[0],) + narrow_part.shape[1:]
    )


def local(fields, stresses, planes, active_masks):
    chan_dev, plane_count, cells_x, cells_z = fields.shape
    coarse_x = cells_x // 4
    coarse_z = cells_z // 4
    row_count = plane_count * coarse_x * coarse_z
    col_devices = lax.axis_size("cols")
    column_index = lax.axis_index("cols")
    term_dev = TERMS // col_devices
    offset = column_index * term_dev
    samples = float(row_count * lax.axis_size("slab") * lax.axis_size("rep"))
    height = 2.0 * (planes.astype(jnp.float32) + 0.5) / NY - 1.0
    root_weight = jnp.sqrt(1.2 - height * height)
    width = 5
    top, bottom = neighbour_edges(fields, "rep", 2, width)
    narrow_taps = kernel(1.5)
    broad_taps = kernel(3.0)
    guard = jnp.minimum(lax.axis_index("rep"), 0)
    span_table = filter_table(cells_z, narrow_taps, broad_taps, guard, (0, 1, 2))
    stream_table = filter_table(cells_x, narrow_taps, broad_taps, guard, (1, 0, 2))
    highest = lax.Precision.HIGHEST
    along_stream = (
        jnp.einsum(
            "cpxz,sxm->scpmz",
            fields.astype(jnp.float32),
            stream_table[:, width : width + cells_x],
            precision=lax.Precision.HIGH,
        )
        + jnp.einsum(
            "cpxz,sxm->scpmz", top.astype(jnp.float32), stream_table[:, :width], precision=lax.Precision.HIGH
        )
        + jnp.einsum(
            "cpxz,sxm->scpmz",
            bottom.astype(jnp.float32),
            stream_table[:, width + cells_x :],
            precision=lax.Precision.HIGH,
        )
    )
    left, right = neighbour_edges(jnp.swapaxes(along_stream, 3, 4), "slab", 3, width)
    filtered = (
        jnp.einsum(
            "scpmz,zsn->scpmn",
            along_stream,
            span_table[width : width + cells_z],
            precision=lax.Precision.HIGH,
        )
        + jnp.einsum("scpzm,zsn->scpmn", left, span_table[:width], precision=lax.Precision.HIGH)
        + jnp.einsum("scpzm,zsn->scpmn", right, span_table[width + cells_z :], precision=lax.Precision.HIGH)
    )
    narrow = filtered[0]
    broader = filtered[1]
    narrow_set = narrow.astype(jnp.bfloat16).reshape(chan_dev, row_count)
    broad_set = (
        (broader * root_weight[None, :, None, None])
        .astype(jnp.bfloat16)
        .reshape(chan_dev, row_count)
    )
    weighted = (stresses.astype(jnp.float32) * root_weight[None, :, None, None]).astype(
        jnp.bfloat16
    )
    weighted = weighted.reshape(STRESS, row_count)
    chunk = row_count // col_devices
    lanes = 128
    chunk_rows = chunk // lanes
    channels = chan_dev * col_devices
    sets = jnp.stack([narrow_set, broad_set]).reshape(2, chan_dev, col_devices, chunk_rows, lanes)
    sets = jnp.transpose(sets, (2, 0, 1, 3, 4)).reshape(col_devices, 2 * chan_dev * chunk_rows, lanes)
    sets = lax.all_to_all(sets, "cols", 0, 0, tiled=True)
    sets = sets.reshape(col_devices, 2, chan_dev, chunk_rows, lanes)
    sets = jnp.transpose(sets, (1, 0, 2, 3, 4)).reshape(2, channels, chunk_rows, lanes)
    narrow_all, broad_all = sets[0], sets[1]
    weighted = weighted.reshape(STRESS, col_devices, chunk_rows, lanes)
    weighted = lax.dynamic_index_in_dim(weighted, column_index, 1, keepdims=False)
    block_rows = chunk_rows
    block_count = chunk_rows // block_rows

    def gram_step(block_index, carry):
        gram_acc, rhs_acc = carry
        start = block_index * block_rows
        narrow_piece = lax.dynamic_slice_in_dim(narrow_all, start, block_rows, 1)
        broad_piece = lax.dynamic_slice_in_dim(broad_all, start, block_rows, 1)
        all_terms = library(narrow_piece, broad_piece)
        weighted_piece = lax.dynamic_slice_in_dim(weighted, start, block_rows, 1)
        gram_acc = gram_acc + jnp.einsum(
            "iqr,jqr->ij", all_terms, all_terms, preferred_element_type=jnp.float32
        )
        rhs_acc = rhs_acc + jnp.einsum(
            "iqr,kqr->ik", all_terms, weighted_piece, preferred_element_type=jnp.float32
        )
        return (gram_acc, rhs_acc)

    gram_part, rhs_part = lax.fori_loop(
        0,
        block_count,
        gram_step,
        (jnp.zeros((TERMS, TERMS), jnp.float32), jnp.zeros((TERMS, STRESS), jnp.float32)),
    )
    full_rows = split_sum(jnp.concatenate([gram_part, rhs_part], axis=1), "rep", ("slab", "cols"))
    gram_matrix = full_rows[:, :TERMS]
    rhs_sums = full_rows[:, TERMS:]
    on_diagonal = lax.broadcasted_iota(jnp.int32, (TERMS, TERMS), 0) == lax.broadcasted_iota(
        jnp.int32, (TERMS, TERMS), 1
    )
    diagonal = jnp.sum(jnp.where(on_diagonal, gram_matrix, 0.0), axis=1)
    column_scale = 1.0 / jnp.sqrt(diagonal / samples + epsilon)
    normal_gram = column_scale[:, None] * gram_matrix * column_scale[None, :] / samples
    target_norm = column_scale[None, :] * rhs_sums.T / samples

    passes = pl.pallas_call(
        conjugate_passes,
        out_shape=jax.ShapeDtypeStruct((PASSES, STRESS, TERMS), jnp.float32),
    )(normal_gram, target_norm, active_masks.astype(jnp.float32))
    coefficients = lax.dynamic_slice_in_dim(passes[:, :STRESS], offset, term_dev, 2)
    solution_all = passes[PASSES - 1, :STRESS]
    final_weights = (column_scale[None, :] * solution_all).astype(jnp.bfloat16)

    def misfit_step(block_index, misfit_acc):
        start = block_index * block_rows
        narrow_piece = lax.dynamic_slice_in_dim(narrow_all, start, block_rows, 1)
        broad_piece = lax.dynamic_slice_in_dim(broad_all, start, block_rows, 1)
        all_terms = library(narrow_piece, broad_piece)
        predicted = jnp.einsum(
            "ki,iqr->kqr", final_weights, all_terms, preferred_element_type=jnp.float32
        )
        weighted_piece = lax.dynamic_slice_in_dim(weighted, start, block_rows, 1)
        piece_misfit = (weighted_piece.astype(jnp.float32) - predicted).astype(jnp.bfloat16)
        return lax.dynamic_update_slice_in_dim(misfit_acc, piece_misfit, start, 1)

    misfit = lax.fori_loop(
        0, block_count, misfit_step, jnp.zeros((STRESS, chunk_rows, lanes), jnp.bfloat16)
    )
    misfit = lax.all_gather(misfit, "cols", axis=1, tiled=True)
    misfit = misfit.reshape(STRESS, plane_count, coarse_x, coarse_z)
    return (coefficients, misfit)


def solution(mesh):
    placed = (
        P("cols", "groups", "rep", "slab"),
        P(None, "groups", "rep", "slab"),
        P("groups"),
        P(),
    )
    return jax.shard_map(
        local,
        mesh=mesh,
        in_specs=placed,
        out_specs=(P(None, "groups", "cols"), P(None, "groups", "rep", "slab")),
        check_vma=False,
    )
```

```python
import math

import jax
import jax.numpy as jnp
import numpy as np
from jax import lax
from jax.experimental import pallas as pl
from jax.sharding import PartitionSpec as P

STRESS = 6
TERMS = 256
NY = 2048
PASSES = 3
ITERS = 3


ridge_weight = 0.05
epsilon = 1e-06


def extended(array, sides, width):
    for axis, dim in sides:
        count, length = (lax.axis_size(axis), array.shape[dim])
        up = [(i, (i + 1) % count) for i in range(count)]
        down = [(j, i) for i, j in up]
        last = lax.slice_in_dim(array, length - width, length, axis=dim)
        leading = lax.slice_in_dim(array, 0, width, axis=dim)
        before = lax.ppermute(last, axis, up)
        after = lax.ppermute(leading, axis, down)
        array = jnp.concatenate([before, array, after], axis=dim)
    return array


def tree_sum(value, axes):
    for axis in axes:
        count = lax.axis_size(axis)
        if count & (count - 1):
            value = lax.psum(value, axis)
            continue
        step = 1
        while step < count:
            partner = [(i, i ^ step) for i in range(count)]
            value = value + lax.ppermute(value, axis, partner)
            step *= 2
    return value


def split_sum(value, lead, axes):
    count = lax.axis_size(lead)
    if count != 2 or value.shape[0] % 2:
        return tree_sum(value, (lead,) + axes)
    swap = [(0, 1), (1, 0)]
    value = value + lax.ppermute(value, lead, swap)
    half = value.shape[0] // 2
    first = lax.axis_index(lead) == 0
    mine = jnp.where(first, value[:half], value[half:])
    mine = tree_sum(mine, axes)
    other = lax.ppermute(mine, lead, swap)
    return jnp.where(first, jnp.concatenate([mine, other]), jnp.concatenate([other, mine]))


def neighbour_edges(array, axis, dim, width):
    count, length = (lax.axis_size(axis), array.shape[dim])
    up = [(i, (i + 1) % count) for i in range(count)]
    down = [(j, i) for i, j in up]
    last = lax.slice_in_dim(array, length - width, length, axis=dim)
    leading = lax.slice_in_dim(array, 0, width, axis=dim)
    return (lax.ppermute(last, axis, up), lax.ppermute(leading, axis, down))


def conjugate_passes(gram_ref, target_ref, mask_ref, out_ref):
    gram = gram_ref[...]
    target = target_ref[...]
    gram_high = gram.astype(jnp.bfloat16)
    gram_low = (gram - gram_high.astype(jnp.float32)).astype(jnp.bfloat16)

    def product_with(left, right):
        return lax.dot_general(
            left, right, (((1,), (1,)), ((), ())), preferred_element_type=jnp.float32
        )

    def apply_normal(vector, active):
        masked = active * vector
        masked_high = masked.astype(jnp.bfloat16)
        masked_low = (masked - masked_high.astype(jnp.float32)).astype(jnp.bfloat16)
        product = (
            product_with(masked_high, gram_high)
            + product_with(masked_low, gram_high)
            + product_with(masked_high, gram_low)
        )
        return active * product + ridge_weight * vector

    solution_all = jnp.zeros(target.shape, jnp.float32)
    for pass_index in range(PASSES):
        active = mask_ref[pass_index]
        solution_all = active * solution_all
        remain = active * target - apply_normal(solution_all, active)
        direction = remain
        norm_now = jnp.sum(remain * remain, axis=1, keepdims=True)
        for turn_index in range(ITERS):
            applied = apply_normal(direction, active)
            curve_sum = jnp.sum(direction * applied, axis=1, keepdims=True)
            step_size = norm_now / (curve_sum + epsilon)
            solution_all = solution_all + step_size * direction
            remain = remain - step_size * applied
            norm_next = jnp.sum(remain * remain, axis=1, keepdims=True)
            direction = remain + (norm_next / (norm_now + epsilon)) * direction
            norm_now = norm_next
        out_ref[pass_index] = solution_all


def kernel(spread):
    offsets = np.arange(13) - 6.0
    values = np.exp(-offsets * offsets / (2.0 * spread * spread))
    return values / values.sum()


def filter_table(cells, first_taps, second_taps, guard, order):
    out_count = cells // 4
    shape = tuple((cells + 10, 2, out_count)[d] for d in order)
    where = {d: order.index(d) for d in range(3)}
    position = lax.broadcasted_iota(jnp.int32, shape, where[0])
    which = lax.broadcasted_iota(jnp.int32, shape, where[1])
    out_index = lax.broadcasted_iota(jnp.int32, shape, where[2])
    tap_at = position - 1 - 4 * out_index + guard
    spread = jnp.where(which == 0, np.float32(1.5), np.float32(3.0))
    total = jnp.where(
        which == 0, np.float32(gauss_total(1.5)), np.float32(gauss_total(3.0))
    )
    offset = (tap_at - 6).astype(jnp.float32)
    value = jnp.exp(-offset * offset / (2.0 * spread * spread)) / total
    return jnp.where((tap_at >= 0) & (tap_at <= 12), value, 0.0)


def gauss_total(spread):
    offsets = np.arange(13) - 6.0
    return np.exp(-offsets * offsets / (2.0 * spread * spread)).sum()


def library(narrow_part, broad_part):
    product = (
        narrow_part.astype(jnp.float32)[:, None] * broad_part.astype(jnp.float32)[None, :]
    )
    return product.astype(jnp.bfloat16).reshape(
        (narrow_part.shape[0] * broad_part.shape[0],) + narrow_part.shape[1:]
    )


def local(fields, stresses, planes, active_masks):
    chan_dev, plane_count, cells_x, cells_z = fields.shape
    coarse_x = cells_x // 4
    coarse_z = cells_z // 4
    row_count = plane_count * coarse_x * coarse_z
    col_devices = lax.axis_size("cols")
    column_index = lax.axis_index("cols")
    term_dev = TERMS // col_devices
    offset = column_index * term_dev
    samples = float(row_count * lax.axis_size("slab") * lax.axis_size("rep"))
    height = 2.0 * (planes.astype(jnp.float32) + 0.5) / NY - 1.0
    root_weight = jnp.sqrt(1.2 - height * height)
    width = 5
    top, bottom = neighbour_edges(fields, "rep", 2, width)
    narrow_taps = kernel(1.5)
    broad_taps = kernel(3.0)
    guard = jnp.minimum(lax.axis_index("rep"), 0)
    span_table = filter_table(cells_z, narrow_taps, broad_taps, guard, (0, 1, 2))
    stream_table = filter_table(cells_x, narrow_taps, broad_taps, guard, (1, 0, 2))
    highest = lax.Precision.HIGHEST
    along_stream = (
        jnp.einsum(
            "cpxz,sxm->scpmz",
            fields.astype(jnp.float32),
            stream_table[:, width : width + cells_x],
            precision=lax.Precision.HIGH,
        )
        + jnp.einsum(
            "cpxz,sxm->scpmz", top.astype(jnp.float32), stream_table[:, :width], precision=lax.Precision.HIGH
        )
        + jnp.einsum(
            "cpxz,sxm->scpmz",
            bottom.astype(jnp.float32),
            stream_table[:, width + cells_x :],
            precision=lax.Precision.HIGH,
        )
    )
    left, right = neighbour_edges(jnp.swapaxes(along_stream, 3, 4), "slab", 3, width)
    filtered = (
        jnp.einsum(
            "scpmz,zsn->scpmn",
            along_stream,
            span_table[width : width + cells_z],
            precision=lax.Precision.HIGH,
        )
        + jnp.einsum("scpzm,zsn->scpmn", left, span_table[:width], precision=lax.Precision.HIGH)
        + jnp.einsum("scpzm,zsn->scpmn", right, span_table[width + cells_z :], precision=lax.Precision.HIGH)
    )
    narrow = filtered[0]
    broader = filtered[1]
    narrow_set = narrow.astype(jnp.bfloat16).reshape(chan_dev, row_count)
    broad_set = (
        (broader * root_weight[None, :, None, None])
        .astype(jnp.bfloat16)
        .reshape(chan_dev, row_count)
    )
    weighted = (stresses.astype(jnp.float32) * root_weight[None, :, None, None]).astype(
        jnp.bfloat16
    )
    weighted = weighted.reshape(STRESS, row_count)
    chunk = row_count // col_devices
    lanes = 128
    chunk_rows = chunk // lanes
    channels = chan_dev * col_devices
    sets = jnp.stack([narrow_set, broad_set]).reshape(2, chan_dev, col_devices, chunk_rows, lanes)
    sets = jnp.transpose(sets, (2, 0, 1, 3, 4)).reshape(col_devices, 2 * chan_dev * chunk_rows, lanes)
    sets = lax.all_to_all(sets, "cols", 0, 0, tiled=True)
    sets = sets.reshape(col_devices, 2, chan_dev, chunk_rows, lanes)
    sets = jnp.transpose(sets, (1, 0, 2, 3, 4)).reshape(2, channels, chunk_rows, lanes)
    narrow_all, broad_all = sets[0], sets[1]
    weighted = weighted.reshape(STRESS, col_devices, chunk_rows, lanes)
    weighted = lax.dynamic_index_in_dim(weighted, column_index, 1, keepdims=False)
    block_rows = chunk_rows
    block_count = chunk_rows // block_rows

    def gram_step(block_index, carry):
        gram_acc, rhs_acc = carry
        start = block_index * block_rows
        narrow_piece = lax.dynamic_slice_in_dim(narrow_all, start, block_rows, 1)
        broad_piece = lax.dynamic_slice_in_dim(broad_all, start, block_rows, 1)
        all_terms = library(narrow_piece, broad_piece)
        weighted_piece = lax.dynamic_slice_in_dim(weighted, start, block_rows, 1)
        gram_acc = gram_acc + jnp.einsum(
            "iqr,jqr->ij", all_terms, all_terms, preferred_element_type=jnp.float32
        )
        rhs_acc = rhs_acc + jnp.einsum(
            "iqr,kqr->ik", all_terms, weighted_piece, preferred_element_type=jnp.float32
        )
        return (gram_acc, rhs_acc)

    gram_part, rhs_part = lax.fori_loop(
        0,
        block_count,
        gram_step,
        (jnp.zeros((TERMS, TERMS), jnp.float32), jnp.zeros((TERMS, STRESS), jnp.float32)),
    )
    full_rows = split_sum(jnp.concatenate([gram_part, rhs_part], axis=1), "rep", ("slab", "cols"))
    gram_matrix = full_rows[:, :TERMS]
    rhs_sums = full_rows[:, TERMS:]
    on_diagonal = lax.broadcasted_iota(jnp.int32, (TERMS, TERMS), 0) == lax.broadcasted_iota(
        jnp.int32, (TERMS, TERMS), 1
    )
    diagonal = jnp.sum(jnp.where(on_diagonal, gram_matrix, 0.0), axis=1)
    column_scale = 1.0 / jnp.sqrt(diagonal / samples + epsilon)
    normal_gram = column_scale[:, None] * gram_matrix * column_scale[None, :] / samples
    target_norm = column_scale[None, :] * rhs_sums.T / samples

    passes = pl.pallas_call(
        conjugate_passes,
        out_shape=jax.ShapeDtypeStruct((PASSES, STRESS, TERMS), jnp.float32),
    )(normal_gram, target_norm, active_masks.astype(jnp.float32))
    coefficients = lax.dynamic_slice_in_dim(passes[:, :STRESS], offset, term_dev, 2)
    solution_all = passes[PASSES - 1, :STRESS]
    final_weights = (column_scale[None, :] * solution_all).astype(jnp.bfloat16)

    def misfit_step(block_index, misfit_acc):
        start = block_index * block_rows
        narrow_piece = lax.dynamic_slice_in_dim(narrow_all, start, block_rows, 1)
        broad_piece = lax.dynamic_slice_in_dim(broad_all, start, block_rows, 1)
        all_terms = library(narrow_piece, broad_piece)
        predicted = jnp.einsum(
            "ki,iqr->kqr", final_weights, all_terms, preferred_element_type=jnp.float32
        )
        weighted_piece = lax.dynamic_slice_in_dim(weighted, start, block_rows, 1)
        piece_misfit = (weighted_piece.astype(jnp.float32) - predicted).astype(jnp.bfloat16)
        return lax.dynamic_update_slice_in_dim(misfit_acc, piece_misfit, start, 1)

    misfit = lax.fori_loop(
        0, block_count, misfit_step, jnp.zeros((STRESS, chunk_rows, lanes), jnp.bfloat16)
    )
    misfit = lax.all_gather(misfit, "cols", axis=1, tiled=True)
    misfit = misfit.reshape(STRESS, plane_count, coarse_x, coarse_z)
    return (coefficients, misfit)


def solution(mesh):
    placed = (
        P("cols", "groups", "rep", "slab"),
        P(None, "groups", "rep", "slab"),
        P("groups"),
        P(),
    )
    return jax.shard_map(
        local,
        mesh=mesh,
        in_specs=placed,
        out_specs=(P(None, "groups", "cols"), P(None, "groups", "rep", "slab")),
        check_vma=False,
    )
```
